256 devices in a mesh: theta: 16 (over y, x_hi, core), phi: 16 (over x_lo, z).
Axes of the slice: x: 4 (x_hi: 2, x_lo: 2; x = x_hi * 2 + x_lo), y: 4, z: 8, core: 2. Of those that a mesh axis runs over, the one named last changes fastest.
Arguments:
- density: float32 [2, 128, 1536, 128], P(None, 'theta', 'phi'), may hold values from 0.5 to 2
- velocity: float32 [3, 128, 1536, 128], P(None, 'theta', 'phi'), may hold values from -3 to 3
- bfield: float32 [3, 128, 1536, 128], P(None, 'theta', 'phi'), may hold values from -6 to 6
- levels: int32 [2, 4], replicated, may hold values from 0 to 3
Outputs:
- density_new: float32 [2, 128, 1536, 128], P(None, 'theta', 'phi')
- bfield_new: float32 [3, 128, 1536, 128], P(None, 'theta', 'phi')
The draws below stay inside these ranges and needn't reach their ends.
Inputs may be any that keep to these rules, and one draw needn't show every extreme that they name: `levels`: a row at level l keeps the azimuthal modes below 128 // 2**l.
All inputs are finite; a program needn't handle non-finite values.
Results may differ from the reference program's by a relative error of at most 0.00007.
Values sent between devices are 32-bit elements; how exact they have to be, the bound alone decides.
No kernel may reach another device: no remote copies, remote signals or barrier semaphores. Data moves between devices by JAX's collectives and lax.ppermute only.
A program may use at most 64 MiB of HBM per device.

```python
import jax
import jax.numpy as jnp
from jax import lax

NR = 128
CT = 8
CAP = 4
KMAX = 128
LEVELS = 4
NTH = 128
NPH = 1536
N_THETA = 16


def touch_ends(values, own_key, least, high):
    spot = [jax.random.randint(jax.random.fold_in(own_key, axis), (), 0, length) for axis, length in enumerate(values.shape)]
    main_axis = values.shape.index(max(values.shape))
    next_to = spot[:main_axis] + [(spot[main_axis] + 1) % values.shape[main_axis]] + spot[main_axis + 1:]
    return values.at[tuple(spot)].set(least).at[tuple(next_to)].set(high)


def block_scale(stream_key, shape, shards, least, high):
    factor_of = 1.0
    for axis_at, blocks in shards:
        draws = jax.random.uniform(jax.random.fold_in(jax.random.fold_in(stream_key, 6), axis_at), (blocks,), jnp.float32, least / len(shards), high / len(shards))
        factor_of = factor_of * jnp.repeat(jnp.exp(draws), shape[axis_at] // blocks).reshape((-1,) + (1,) * (len(shape) - 1 - axis_at))
    return factor_of


def scatter_about(key, shape, scale, most, pieces=(), kind=jnp.bfloat16):
    values = scale * jax.random.normal(key, shape, jnp.float32)
    if pieces:
        values = values * block_scale(key, shape, pieces, -0.22, 0.18)
    return jnp.clip(values, -most, most).astype(kind)


def setup_inputs(seed: int = 0) -> dict:
    seeds = jax.random.split(jax.random.key(seed), 5)
    density = jnp.clip(0.5 + 1.5 * jax.random.uniform(seeds[0], (2, NTH, NPH, NR), jnp.float32) ** block_scale(seeds[0], (2, NTH, NPH, NR), ((1, 16), (2, 16)), -0.2, 0.2), 0.5, 2.0)
    velocity = scatter_about(seeds[1], (3, NTH, NPH, NR), 0.5, 3.0, ((1, 16), (2, 16)), jnp.float32)
    bfield = scatter_about(seeds[2], (3, NTH, NPH, NR), 1.0, 6.0, ((1, 16), (2, 16)), jnp.float32)
    levels = touch_ends(jax.random.randint(seeds[3], (2, CAP), 0, LEVELS), jax.random.fold_in(seeds[3], 1), 0, LEVELS - 1).astype(jnp.int32)
    return {"density": density, "velocity": velocity, "bfield": bfield, "levels": levels}


TIME_STEP = 0.2
PARITY = (1.0, 1.0, 1.0, -1.0, -1.0, 1.0, -1.0, -1.0)


def window_of(array, spans):
    return array[spans[0][0]:spans[0][1], spans[1][0]:spans[1][1], spans[2][0]:spans[2][1]]


def moved(spans, direction, start, length):
    return tuple((start, start + length) if other == direction else spans[other] for other in range(3))


def corner_mean(field, extents, first_axis, second_axis):
    base = [(1, extents[0] + 1), (1, extents[1] + 1), (1, extents[2] + 1)]
    total = jnp.zeros((), jnp.float32)
    for first_start in (0, 1):
        for second_start in (0, 1):
            spans_now = list(base)
            spans_now[first_axis] = (first_start, first_start + extents[first_axis] + 1)
            spans_now[second_axis] = (second_start, second_start + extents[second_axis] + 1)
            total = total + window_of(field, spans_now)
    return 0.25 * total


def advance(extended):
    extents = (extended.shape[1] - 4, extended.shape[2] - 4, extended.shape[3] - 4)
    inner_span = tuple((2, extent + 2) for extent in extents)
    speed_for = (3, 4, 2)
    densities = []
    for channel in range(2):
        amount = extended[channel]
        tendency = jnp.zeros(extents, jnp.float32)
        for direction in range(3):
            extent_now = extents[direction]
            lower_span = moved(inner_span, direction, 1, extent_now + 1)
            upper_span = moved(inner_span, direction, 2, extent_now + 1)
            speed_field = extended[speed_for[direction]]
            left_amount = window_of(amount, lower_span)
            right_amount = window_of(amount, upper_span)
            left_speed = window_of(speed_field, lower_span)
            right_speed = window_of(speed_field, upper_span)
            fluxes = 0.5 * (left_amount * left_speed + right_amount * right_speed) - 0.5 * jnp.maximum(jnp.abs(left_speed), jnp.abs(right_speed)) * (right_amount - left_amount)
            tendency = tendency + lax.slice_in_dim(fluxes, 1, extent_now + 1, axis=direction) - lax.slice_in_dim(fluxes, 0, extent_now, axis=direction)
        densities.append(window_of(amount, inner_span) - TIME_STEP * tendency)
    wide_span = tuple((1, extent + 3) for extent in extents)
    axis_of = (2, 0, 1)
    centred = []
    for component in range(3):
        direction = axis_of[component]
        shifted = moved(wide_span, direction, 2, extents[direction] + 2)
        face_field = extended[5 + component]
        centred.append(0.5 * (window_of(face_field, wide_span) + window_of(face_field, shifted)))
    speeds = [window_of(extended[2 + component], wide_span) for component in range(3)]
    emf_radial = -(speeds[1] * centred[2] - speeds[2] * centred[1])
    emf_theta = -(speeds[2] * centred[0] - speeds[0] * centred[2])
    emf_phi = -(speeds[0] * centred[1] - speeds[1] * centred[0])
    edge_phi = corner_mean(emf_phi, extents, 0, 2)
    edge_theta = corner_mean(emf_theta, extents, 1, 2)
    edge_radial = corner_mean(emf_radial, extents, 0, 1)
    radial_len = extents[2]
    inner_faces = [window_of(extended[5 + component], inner_span) for component in range(3)]
    new_radial = inner_faces[0] - TIME_STEP * ((edge_phi[1:, :, :radial_len] - edge_phi[:-1, :, :radial_len]) - (edge_theta[:, 1:, :radial_len] - edge_theta[:, :-1, :radial_len]))
    new_theta = inner_faces[1] - TIME_STEP * ((edge_radial[:-1, 1:, :] - edge_radial[:-1, :-1, :]) - (edge_phi[:-1, :, 1:] - edge_phi[:-1, :, :-1]))
    new_phi = inner_faces[2] - TIME_STEP * ((edge_theta[:, :-1, 1:] - edge_theta[:, :-1, :-1]) - (edge_radial[1:, :-1, :] - edge_radial[:-1, :-1, :]))
    return jnp.stack(densities), jnp.stack([new_radial, new_theta, new_phi])


def pole_filter(rows, level_row):
    spectrum = jnp.fft.rfft(rows, axis=2)
    limits = jnp.right_shift(jnp.int32(KMAX), level_row.astype(jnp.int32))
    orders = jnp.arange(spectrum.shape[2], dtype=jnp.int32)
    kept = orders[None, :] < limits[:, None]
    spectrum = jnp.where(kept[None, :, :, None], spectrum, jnp.zeros_like(spectrum))
    return jnp.fft.irfft(spectrum, n=rows.shape[2], axis=2).astype(jnp.float32)


def reference(density, velocity, bfield, levels):
    combined = jnp.concatenate([density, velocity, bfield], axis=0)
    theta_len = combined.shape[1]
    half_turn = combined.shape[2] // 2
    north_rows = pole_filter(combined[:, :CAP], levels[0])
    south_rows = pole_filter(combined[:, theta_len - CAP:], levels[1])
    combined = jnp.concatenate([north_rows, combined[:, CAP:theta_len - CAP], south_rows], axis=1)
    parity = jnp.array(PARITY, jnp.float32)[:, None, None]

    def across_pole(row_index):
        return parity * jnp.roll(combined[:, row_index], half_turn, axis=1)

    north_ghosts = jnp.stack([across_pole(1), across_pole(0)], axis=1)
    south_ghosts = jnp.stack([across_pole(theta_len - 1), across_pole(theta_len - 2)], axis=1)
    full_rows = jnp.concatenate([north_ghosts, combined, south_ghosts], axis=1)
    density_parts = []
    field_parts = []
    for block_index in range(N_THETA):
        block_rows = full_rows[:, block_index * CT:block_index * CT + CT + 4]
        block_rows = jnp.concatenate([block_rows[:, :, -2:], block_rows, block_rows[:, :, :2]], axis=2)
        block_rows = jnp.pad(block_rows, ((0, 0), (0, 0), (0, 0), (2, 2)), mode="edge")
        density_block, field_block = advance(block_rows)
        density_parts.append(density_block)
        field_parts.append(field_block)
    return jnp.concatenate(density_parts, axis=1), jnp.concatenate(field_parts, axis=1)
```

```python
import math

import jax
import jax.numpy as jnp
from jax import lax
from jax.sharding import PartitionSpec as P

CAP = 4
KMAX = 128


TIME_STEP = 0.2
PARITY = (1.0, 1.0, 1.0, -1.0, -1.0, 1.0, -1.0, -1.0)


def up_r(a):
    return jnp.concatenate([a[..., 1:], a[..., -1:]], axis=-1)


def down_r(a):
    return jnp.concatenate([a[..., :1], a[..., :-1]], axis=-1)


def face_flux(left_amount, right_amount, left_speed, right_speed):
    return 0.5 * (left_amount * left_speed + right_amount * right_speed) - 0.5 * jnp.maximum(
        jnp.abs(left_speed), jnp.abs(right_speed)
    ) * (right_amount - left_amount)


def corner4(e00, e01, e10, e11):
    return 0.25 * (((e00 + e01) + e10) + e11)


def advance(x):
    ct = x.shape[1] - 3
    npc = x.shape[2] - 3
    densities = []
    for channel in range(2):
        q = x[channel]
        v_t = x[3]
        v_p = x[4]
        v_r = x[2]
        fl_t = face_flux(
            q[0 : ct + 1, 1 : npc + 1], q[1 : ct + 2, 1 : npc + 1],
            v_t[0 : ct + 1, 1 : npc + 1], v_t[1 : ct + 2, 1 : npc + 1],
        )
        fl_p = face_flux(
            q[1 : ct + 1, 0 : npc + 1], q[1 : ct + 1, 1 : npc + 2],
            v_p[1 : ct + 1, 0 : npc + 1], v_p[1 : ct + 1, 1 : npc + 2],
        )
        qi = q[1 : ct + 1, 1 : npc + 1]
        vi = v_r[1 : ct + 1, 1 : npc + 1]
        fl_lo = face_flux(down_r(qi), qi, down_r(vi), vi)
        fl_hi = face_flux(qi, up_r(qi), vi, up_r(vi))
        tendency = (fl_t[1:] - fl_t[:-1]) + (fl_p[:, 1:] - fl_p[:, :-1]) + (fl_hi - fl_lo)
        densities.append(qi - TIME_STEP * tendency)

    wr = slice(0, ct + 2)
    wc = slice(0, npc + 2)
    b_r = x[5][wr, wc]
    b_t = x[6]
    b_p = x[7]
    c_r = 0.5 * (b_r + up_r(b_r))
    c_t = 0.5 * (b_t[0 : ct + 2, wc] + b_t[1 : ct + 3, wc])
    c_p = 0.5 * (b_p[wr, 0 : npc + 2] + b_p[wr, 1 : npc + 3])
    s_r = x[2][wr, wc]
    s_t = x[3][wr, wc]
    s_p = x[4][wr, wc]
    emf_r = -(s_t * c_p - s_p * c_t)
    emf_t = -(s_p * c_r - s_r * c_p)
    emf_p = -(s_r * c_t - s_t * c_r)
    lane = lax.broadcasted_iota(jnp.int32, emf_t.shape, 2)
    last = emf_t.shape[2] - 1
    edge_t = -(s_p * b_r - s_r * c_p)
    edge_p = -(s_r * c_t - s_t * b_r)
    t_lo = jnp.where(lane == 0, edge_t, down_r(emf_t))
    t_hi = jnp.where(lane == last, edge_t, up_r(emf_t))
    p_lo = jnp.where(lane == 0, edge_p, down_r(emf_p))
    p_hi = jnp.where(lane == last, edge_p, up_r(emf_p))

    rows_a = slice(0, ct + 1)
    rows_b = slice(1, ct + 2)
    cols_in = slice(1, npc + 1)
    ep_lo = corner4(p_lo[rows_a, cols_in], emf_p[rows_a, cols_in], p_lo[rows_b, cols_in], emf_p[rows_b, cols_in])
    ep_hi = corner4(emf_p[rows_a, cols_in], p_hi[rows_a, cols_in], emf_p[rows_b, cols_in], p_hi[rows_b, cols_in])
    rows_in = slice(1, ct + 1)
    cols_a = slice(0, npc + 1)
    cols_b = slice(1, npc + 2)
    et_lo = corner4(t_lo[rows_in, cols_a], emf_t[rows_in, cols_a], t_lo[rows_in, cols_b], emf_t[rows_in, cols_b])
    et_hi = corner4(emf_t[rows_in, cols_a], t_hi[rows_in, cols_a], emf_t[rows_in, cols_b], t_hi[rows_in, cols_b])
    er = corner4(emf_r[rows_a, cols_a], emf_r[rows_a, cols_b], emf_r[rows_b, cols_a], emf_r[rows_b, cols_b])

    inner = (slice(1, ct + 1), slice(1, npc + 1))
    new_radial = x[5][inner] - TIME_STEP * (
        (ep_lo[1:] - ep_lo[:-1]) - (et_lo[:, 1:] - et_lo[:, :-1])
    )
    new_theta = x[6][inner] - TIME_STEP * (
        (er[:-1, 1:] - er[:-1, :-1]) - (ep_hi[:-1] - ep_lo[:-1])
    )
    new_phi = x[7][inner] - TIME_STEP * (
        (et_hi[:, :-1] - et_lo[:, :-1]) - (er[1:, :-1] - er[:-1, :-1])
    )
    return jnp.stack(densities), jnp.stack([new_radial, new_theta, new_phi])


def fourier_rows(cols, cycle_len):
    orders = jnp.arange(KMAX, dtype=jnp.int32)
    phase = (cols[..., None] * orders) % cycle_len
    angle = phase.astype(jnp.float32) * (2.0 * math.pi / cycle_len)
    return jnp.concatenate([jnp.cos(angle), jnp.sin(angle)], axis=-1)


def local(density, velocity, bfield, levels):
    combined = jnp.concatenate([density, velocity, bfield], axis=0)
    channels, ct, npc, nr = combined.shape
    theta_count = lax.axis_size("theta")
    phi_count = lax.axis_size("phi")
    t = lax.axis_index("theta")
    p = lax.axis_index("phi")
    at_north = t == 0
    at_south = t == theta_count - 1
    is_pole = at_north | at_south
    cycle_len = npc * phi_count
    parity = jnp.array(PARITY, jnp.float32)
    poles = (0, theta_count - 1)
    both = ("theta", "phi")

    def pole_pairs(shift):
        return [
            (a * phi_count + b, a * phi_count + (b + shift) % phi_count)
            for a in poles
            for b in range(phi_count)
        ]

    low_halo = lax.ppermute(
        combined[:, ct - 1], "theta", [(i, i + 1) for i in range(theta_count - 1)]
    )
    up_send = jnp.concatenate([combined[:, 0], combined[6:7, 1]], axis=0)
    up_halo = lax.ppermute(up_send, "theta", [(i + 1, i) for i in range(theta_count - 1)])
    rows_ext = jnp.concatenate(
        [
            low_halo[:, None],
            combined,
            up_halo[:channels, None],
            jnp.broadcast_to(up_halo[channels:], (channels, npc, nr))[:, None],
        ],
        axis=1,
    )
    left_cols = lax.ppermute(
        rows_ext[:, :, npc - 1 :], "phi", [(i, (i + 1) % phi_count) for i in range(phi_count)]
    )
    right_cols = lax.ppermute(
        rows_ext[:, :, :2], "phi", [((i + 1) % phi_count, i) for i in range(phi_count)]
    )
    early = jnp.concatenate([left_cols, rows_ext, right_cols], axis=2)

    edge_rows = jnp.where(at_north, combined[:, :CAP], combined[:, ct - CAP :])
    slot_rows = edge_rows.reshape(channels * CAP, npc, nr)
    per_device = channels * CAP // phi_count
    pieces = []
    for shift in range(phi_count):
        target = (p + shift) % phi_count
        piece = lax.dynamic_slice_in_dim(slot_rows, target * per_device, per_device, axis=0)
        if shift:
            piece = lax.ppermute(piece, both, pole_pairs(shift))
        pieces.append(piece)
    cycle = jnp.concatenate(pieces, axis=1)
    shifts = jnp.arange(phi_count, dtype=jnp.int32)
    src_cols = (
        ((p - shifts) % phi_count)[:, None] * npc + jnp.arange(npc, dtype=jnp.int32)[None, :]
    ).reshape(-1)
    analysis = fourier_rows(src_cols, cycle_len)
    dst_cols = (
        ((p - shifts) % phi_count)[:, None] * npc
        - 1
        + jnp.arange(npc + 3, dtype=jnp.int32)[None, :]
    ) % cycle_len
    synthesis = fourier_rows(dst_cols, cycle_len)

    pole_pick = jnp.where(at_north, 0, 1).astype(jnp.int32)
    level_row = lax.dynamic_index_in_dim(levels, pole_pick, 0, keepdims=False)
    slot_ids = p * per_device + jnp.arange(per_device, dtype=jnp.int32)
    row_ids = slot_ids % CAP
    slot_levels = jnp.sum(
        jnp.where(
            row_ids[:, None] == jnp.arange(CAP, dtype=jnp.int32)[None, :], level_row[None, :], 0
        ),
        axis=1,
    )
    limits = jnp.right_shift(jnp.int32(KMAX), slot_levels)
    column_order = jnp.arange(2 * KMAX, dtype=jnp.int32) % KMAX
    column_weight = jnp.where(column_order == 0, 1.0 / cycle_len, 2.0 / cycle_len).astype(
        jnp.float32
    )
    kept_weight = jnp.where(column_order[None, :] < limits[:, None], column_weight[None, :], 0.0)
    coeffs = jnp.einsum("smr,mn->snr", cycle, analysis, precision=lax.Precision.HIGHEST)
    coeffs = coeffs * kept_weight[:, :, None]
    out = jnp.einsum("snr,kjn->skjr", coeffs, synthesis, precision=lax.Precision.HIGHEST)

    back = []
    for shift in range(phi_count):
        piece = out[:, shift]
        if shift:
            piece = lax.ppermute(piece, both, pole_pairs(-shift))
        back.append(piece)
    stacked = jnp.stack(back, axis=0)
    ordered = jnp.roll(stacked, p, axis=0)
    cap_rows = ordered.reshape(channels, CAP, npc + 3, nr)

    ghost_send = jnp.where(
        at_north,
        jnp.concatenate([cap_rows[:, 0], cap_rows[6:7, 1]], axis=0),
        jnp.concatenate([cap_rows[:, CAP - 1], cap_rows[6:7, CAP - 2]], axis=0),
    )
    ghost = lax.ppermute(ghost_send, both, pole_pairs(phi_count // 2))
    ghost_main = ghost[:channels] * parity[:, None, None]
    ghost_b = ghost[channels:] * parity[6]
    north_block = jnp.concatenate(
        [ghost_main[:, None], cap_rows, early[:, CAP + 1 : CAP + 2]], axis=1
    )
    south_block = jnp.concatenate(
        [
            cap_rows,
            ghost_main[:, None],
            jnp.broadcast_to(ghost_b, (channels, npc + 3, nr))[:, None],
        ],
        axis=1,
    )
    offset = jnp.where(at_north, 0, ct - CAP + 1)
    kept_block = lax.dynamic_slice_in_dim(early, offset, CAP + 2, axis=1)
    block = jnp.where(
        at_north, north_block, jnp.where(at_south, south_block, kept_block)
    )
    extended = lax.dynamic_update_slice_in_dim(early, block, offset, axis=1)
    del is_pole
    return advance(extended)


def solution(mesh):
    return jax.shard_map(
        local,
        mesh=mesh,
        in_specs=(
            P(None, "theta", "phi", None),
            P(None, "theta", "phi", None),
            P(None, "theta", "phi", None),
            P(),
        ),
        out_specs=(P(None, "theta", "phi", None), P(None, "theta", "phi", None)),
        check_vma=False,
    )
```

```python
import math

import jax
import jax.numpy as jnp
from jax import lax
from jax.sharding import PartitionSpec as P

CAP = 4
KMAX = 128


TIME_STEP = 0.2
PARITY = (1.0, 1.0, 1.0, -1.0, -1.0, 1.0, -1.0, -1.0)


def up_r(a):
    return jnp.concatenate([a[..., 1:], a[..., -1:]], axis=-1)


def down_r(a):
    return jnp.concatenate([a[..., :1], a[..., :-1]], axis=-1)


def face_flux(left_amount, right_amount, left_speed, right_speed):
    return 0.5 * (left_amount * left_speed + right_amount * right_speed) - 0.5 * jnp.maximum(
        jnp.abs(left_speed), jnp.abs(right_speed)
    ) * (right_amount - left_amount)


def corner4(e00, e01, e10, e11):
    return 0.25 * (((e00 + e01) + e10) + e11)


def advance(x):
    ct = x.shape[1] - 3
    npc = x.shape[2] - 3
    densities = []
    for channel in range(2):
        q = x[channel]
        v_t = x[3]
        v_p = x[4]
        v_r = x[2]
        fl_t = face_flux(
            q[0 : ct + 1, 1 : npc + 1], q[1 : ct + 2, 1 : npc + 1],
            v_t[0 : ct + 1, 1 : npc + 1], v_t[1 : ct + 2, 1 : npc + 1],
        )
        fl_p = face_flux(
            q[1 : ct + 1, 0 : npc + 1], q[1 : ct + 1, 1 : npc + 2],
            v_p[1 : ct + 1, 0 : npc + 1], v_p[1 : ct + 1, 1 : npc + 2],
        )
        qi = q[1 : ct + 1, 1 : npc + 1]
        vi = v_r[1 : ct + 1, 1 : npc + 1]
        fl_lo = face_flux(down_r(qi), qi, down_r(vi), vi)
        fl_hi = face_flux(qi, up_r(qi), vi, up_r(vi))
        tendency = (fl_t[1:] - fl_t[:-1]) + (fl_p[:, 1:] - fl_p[:, :-1]) + (fl_hi - fl_lo)
        densities.append(qi - TIME_STEP * tendency)

    wr = slice(0, ct + 2)
    wc = slice(0, npc + 2)
    b_r = x[5][wr, wc]
    b_t = x[6]
    b_p = x[7]
    c_r = 0.5 * (b_r + up_r(b_r))
    c_t = 0.5 * (b_t[0 : ct + 2, wc] + b_t[1 : ct + 3, wc])
    c_p = 0.5 * (b_p[wr, 0 : npc + 2] + b_p[wr, 1 : npc + 3])
    s_r = x[2][wr, wc]
    s_t = x[3][wr, wc]
    s_p = x[4][wr, wc]
    emf_r = -(s_t * c_p - s_p * c_t)
    emf_t = -(s_p * c_r - s_r * c_p)
    emf_p = -(s_r * c_t - s_t * c_r)
    lane = lax.broadcasted_iota(jnp.int32, emf_t.shape, 2)
    last = emf_t.shape[2] - 1
    edge_t = -(s_p * b_r - s_r * c_p)
    edge_p = -(s_r * c_t - s_t * b_r)
    t_lo = jnp.where(lane == 0, edge_t, down_r(emf_t))
    t_hi = jnp.where(lane == last, edge_t, up_r(emf_t))
    p_lo = jnp.where(lane == 0, edge_p, down_r(emf_p))
    p_hi = jnp.where(lane == last, edge_p, up_r(emf_p))

    rows_a = slice(0, ct + 1)
    rows_b = slice(1, ct + 2)
    cols_in = slice(1, npc + 1)
    ep_lo = corner4(p_lo[rows_a, cols_in], emf_p[rows_a, cols_in], p_lo[rows_b, cols_in], emf_p[rows_b, cols_in])
    ep_hi = corner4(emf_p[rows_a, cols_in], p_hi[rows_a, cols_in], emf_p[rows_b, cols_in], p_hi[rows_b, cols_in])
    rows_in = slice(1, ct + 1)
    cols_a = slice(0, npc + 1)
    cols_b = slice(1, npc + 2)
    et_lo = corner4(t_lo[rows_in, cols_a], emf_t[rows_in, cols_a], t_lo[rows_in, cols_b], emf_t[rows_in, cols_b])
    et_hi = corner4(emf_t[rows_in, cols_a], t_hi[rows_in, cols_a], emf_t[rows_in, cols_b], t_hi[rows_in, cols_b])
    er = corner4(emf_r[rows_a, cols_a], emf_r[rows_a, cols_b], emf_r[rows_b, cols_a], emf_r[rows_b, cols_b])

    inner = (slice(1, ct + 1), slice(1, npc + 1))
    new_radial = x[5][inner] - TIME_STEP * (
        (ep_lo[1:] - ep_lo[:-1]) - (et_lo[:, 1:] - et_lo[:, :-1])
    )
    new_theta = x[6][inner] - TIME_STEP * (
        (er[:-1, 1:] - er[:-1, :-1]) - (ep_hi[:-1] - ep_lo[:-1])
    )
    new_phi = x[7][inner] - TIME_STEP * (
        (et_hi[:, :-1] - et_lo[:, :-1]) - (er[1:, :-1] - er[:-1, :-1])
    )
    return jnp.stack(densities), jnp.stack([new_radial, new_theta, new_phi])


def fourier_rows(cols, cycle_len):
    orders = jnp.arange(KMAX, dtype=jnp.int32)
    phase = (cols[..., None] * orders) % cycle_len
    angle = phase.astype(jnp.float32) * (2.0 * math.pi / cycle_len)
    return jnp.concatenate([jnp.cos(angle), jnp.sin(angle)], axis=-1)


def local(density, velocity, bfield, levels):
    combined = jnp.concatenate([density, velocity, bfield], axis=0)
    channels, ct, npc, nr = combined.shape
    theta_count = lax.axis_size("theta")
    phi_count = lax.axis_size("phi")
    t = lax.axis_index("theta")
    p = lax.axis_index("phi")
    at_north = t == 0
    at_south = t == theta_count - 1
    cycle_len = npc * phi_count
    parity = jnp.array(PARITY, jnp.float32)
    poles = (0, theta_count - 1)
    both = ("theta", "phi")

    def pole_pairs(shift):
        return [
            (a * phi_count + b, a * phi_count + (b + shift) % phi_count)
            for a in poles
            for b in range(phi_count)
        ]

    low_halo = lax.ppermute(
        combined[:, ct - 1], "theta", [(i, i + 1) for i in range(theta_count - 1)]
    )
    up_send = jnp.concatenate([combined[:, 0], combined[6:7, 1]], axis=0)
    up_halo = lax.ppermute(up_send, "theta", [(i + 1, i) for i in range(theta_count - 1)])
    rows_ext = jnp.concatenate(
        [
            low_halo[:, None],
            combined,
            up_halo[:channels, None],
            jnp.broadcast_to(up_halo[channels:], (channels, npc, nr))[:, None],
        ],
        axis=1,
    )
    left_cols = lax.ppermute(
        rows_ext[:, :, npc - 1 :], "phi", [(i, (i + 1) % phi_count) for i in range(phi_count)]
    )
    right_cols = lax.ppermute(
        rows_ext[:, :, :2], "phi", [((i + 1) % phi_count, i) for i in range(phi_count)]
    )
    early = jnp.concatenate([left_cols, rows_ext, right_cols], axis=2)

    north_side = t <= 1
    helper = (t == 1) | (t == theta_count - 2)
    edge_rows = jnp.where(at_north, combined[:, :CAP], combined[:, ct - CAP :])
    slot_rows = edge_rows.reshape(channels * CAP, npc, nr)
    half = channels * CAP // 2
    pairs_out = [(0, 1), (theta_count - 1, theta_count - 2)]
    pairs_in = [(1, 0), (theta_count - 2, theta_count - 1)]
    handed = lax.ppermute(slot_rows[half:], "theta", pairs_out)
    work = jnp.where(helper, handed, slot_rows[:half])
    per_device = half // phi_count
    cycle = lax.all_to_all(
        work.reshape(phi_count, per_device, npc, nr), "phi", split_axis=0, concat_axis=2, tiled=True
    )
    cycle = cycle.reshape(per_device, cycle_len, nr)
    analysis = fourier_rows(jnp.arange(cycle_len, dtype=jnp.int32), cycle_len)
    dst_cols = (
        jnp.arange(phi_count, dtype=jnp.int32)[:, None] * npc
        - 1
        + jnp.arange(npc + 3, dtype=jnp.int32)[None, :]
    ) % cycle_len
    synthesis = fourier_rows(dst_cols, cycle_len)

    pole_pick = jnp.where(north_side, 0, 1).astype(jnp.int32)
    level_row = lax.dynamic_index_in_dim(levels, pole_pick, 0, keepdims=False)
    slot_ids = jnp.where(helper, half, 0) + p * per_device + jnp.arange(per_device, dtype=jnp.int32)
    row_ids = slot_ids % CAP
    slot_levels = jnp.sum(
        jnp.where(
            row_ids[:, None] == jnp.arange(CAP, dtype=jnp.int32)[None, :], level_row[None, :], 0
        ),
        axis=1,
    )
    limits = jnp.right_shift(jnp.int32(KMAX), slot_levels)
    column_order = jnp.arange(2 * KMAX, dtype=jnp.int32) % KMAX
    column_weight = jnp.where(column_order == 0, 1.0 / cycle_len, 2.0 / cycle_len).astype(
        jnp.float32
    )
    kept_weight = jnp.where(column_order[None, :] < limits[:, None], column_weight[None, :], 0.0)
    coeffs = jnp.einsum("smr,mn->snr", cycle, analysis, precision=lax.Precision.HIGHEST)
    coeffs = coeffs * kept_weight[:, :, None]
    out = jnp.einsum("snr,kjn->ksjr", coeffs, synthesis, precision=lax.Precision.HIGHEST)
    mine = lax.all_to_all(out, "phi", split_axis=0, concat_axis=0, tiled=True)
    mine = mine.reshape(half, npc + 3, nr)

    from_helper = lax.ppermute(mine, "theta", pairs_in)
    cap_rows = jnp.concatenate([mine, from_helper], axis=0).reshape(channels, CAP, npc + 3, nr)
    per_half = channels // 2
    first_rows = mine[0::CAP]
    last_rows = mine[CAP - 1 :: CAP]
    spare = mine[(6 - per_half) * CAP + CAP - 2 : (6 - per_half) * CAP + CAP - 1]
    ghost_send = jnp.concatenate([jnp.where(north_side, first_rows, last_rows), spare], axis=0)
    turn = phi_count // 2
    pole_ghost = lax.ppermute(
        ghost_send,
        both,
        [(a * phi_count + b, a * phi_count + (b + turn) % phi_count) for a in poles for b in range(phi_count)],
    )
    helper_ghost = lax.ppermute(
        ghost_send,
        both,
        [
            (h * phi_count + b, a * phi_count + (b + turn) % phi_count)
            for h, a in ((1, 0), (theta_count - 2, theta_count - 1))
            for b in range(phi_count)
        ],
    )
    ghost_main = jnp.concatenate([pole_ghost[:per_half], helper_ghost[:per_half]], axis=0)
    ghost_main = ghost_main * parity[:, None, None]
    ghost_b = helper_ghost[per_half:] * parity[6]
    north_block = jnp.concatenate(
        [ghost_main[:, None], cap_rows, early[:, CAP + 1 : CAP + 2]], axis=1
    )
    south_block = jnp.concatenate(
        [
            cap_rows,
            ghost_main[:, None],
            jnp.broadcast_to(ghost_b, (channels, npc + 3, nr))[:, None],
        ],
        axis=1,
    )
    offset = jnp.where(at_north, 0, ct - CAP + 1)
    kept_block = lax.dynamic_slice_in_dim(early, offset, CAP + 2, axis=1)
    block = jnp.where(
        at_north, north_block, jnp.where(at_south, south_block, kept_block)
    )
    extended = lax.dynamic_update_slice_in_dim(early, block, offset, axis=1)
    return advance(extended)


def solution(mesh):
    return jax.shard_map(
        local,
        mesh=mesh,
        in_specs=(
            P(None, "theta", "phi", None),
            P(None, "theta", "phi", None),
            P(None, "theta", "phi", None),
            P(),
        ),
        out_specs=(P(None, "theta", "phi", None), P(None, "theta", "phi", None)),
        check_vma=False,
    )
```

```python
import math

import jax
import jax.numpy as jnp
from jax import lax
from jax.sharding import PartitionSpec as P

CAP = 4
KMAX = 128


TIME_STEP = 0.2
PARITY = (1.0, 1.0, 1.0, -1.0, -1.0, 1.0, -1.0, -1.0)


def up_r(a):
    return jnp.concatenate([a[..., 1:], a[..., -1:]], axis=-1)


def down_r(a):
    return jnp.concatenate([a[..., :1], a[..., :-1]], axis=-1)


def face_flux(left_amount, right_amount, left_speed, right_speed):
    return 0.5 * (left_amount * left_speed + right_amount * right_speed) - 0.5 * jnp.maximum(
        jnp.abs(left_speed), jnp.abs(right_speed)
    ) * (right_amount - left_amount)


def corner4(e00, e01, e10, e11):
    return 0.25 * (((e00 + e01) + e10) + e11)


def advance(x):
    ct = x.shape[1] - 3
    npc = x.shape[2] - 3
    densities = []
    for channel in range(2):
        q = x[channel]
        v_t = x[3]
        v_p = x[4]
        v_r = x[2]
        fl_t = face_flux(
            q[0 : ct + 1, 1 : npc + 1], q[1 : ct + 2, 1 : npc + 1],
            v_t[0 : ct + 1, 1 : npc + 1], v_t[1 : ct + 2, 1 : npc + 1],
        )
        fl_p = face_flux(
            q[1 : ct + 1, 0 : npc + 1], q[1 : ct + 1, 1 : npc + 2],
            v_p[1 : ct + 1, 0 : npc + 1], v_p[1 : ct + 1, 1 : npc + 2],
        )
        qi = q[1 : ct + 1, 1 : npc + 1]
        vi = v_r[1 : ct + 1, 1 : npc + 1]
        fl_lo = face_flux(down_r(qi), qi, down_r(vi), vi)
        fl_hi = face_flux(qi, up_r(qi), vi, up_r(vi))
        tendency = (fl_t[1:] - fl_t[:-1]) + (fl_p[:, 1:] - fl_p[:, :-1]) + (fl_hi - fl_lo)
        densities.append(qi - TIME_STEP * tendency)

    wr = slice(0, ct + 2)
    wc = slice(0, npc + 2)
    b_r = x[5][wr, wc]
    b_t = x[6]
    b_p = x[7]
    c_r = 0.5 * (b_r + up_r(b_r))
    c_t = 0.5 * (b_t[0 : ct + 2, wc] + b_t[1 : ct + 3, wc])
    c_p = 0.5 * (b_p[wr, 0 : npc + 2] + b_p[wr, 1 : npc + 3])
    s_r = x[2][wr, wc]
    s_t = x[3][wr, wc]
    s_p = x[4][wr, wc]
    emf_r = -(s_t * c_p - s_p * c_t)
    emf_t = -(s_p * c_r - s_r * c_p)
    emf_p = -(s_r * c_t - s_t * c_r)
    lane = lax.broadcasted_iota(jnp.int32, emf_t.shape, 2)
    last = emf_t.shape[2] - 1
    edge_t = -(s_p * b_r - s_r * c_p)
    edge_p = -(s_r * c_t - s_t * b_r)
    t_lo = jnp.where(lane == 0, edge_t, down_r(emf_t))
    t_hi = jnp.where(lane == last, edge_t, up_r(emf_t))
    p_lo = jnp.where(lane == 0, edge_p, down_r(emf_p))
    p_hi = jnp.where(lane == last, edge_p, up_r(emf_p))

    rows_a = slice(0, ct + 1)
    rows_b = slice(1, ct + 2)
    cols_in = slice(1, npc + 1)
    ep_lo = corner4(p_lo[rows_a, cols_in], emf_p[rows_a, cols_in], p_lo[rows_b, cols_in], emf_p[rows_b, cols_in])
    ep_hi = corner4(emf_p[rows_a, cols_in], p_hi[rows_a, cols_in], emf_p[rows_b, cols_in], p_hi[rows_b, cols_in])
    rows_in = slice(1, ct + 1)
    cols_a = slice(0, npc + 1)
    cols_b = slice(1, npc + 2)
    et_lo = corner4(t_lo[rows_in, cols_a], emf_t[rows_in, cols_a], t_lo[rows_in, cols_b], emf_t[rows_in, cols_b])
    et_hi = corner4(emf_t[rows_in, cols_a], t_hi[rows_in, cols_a], emf_t[rows_in, cols_b], t_hi[rows_in, cols_b])
    er = corner4(emf_r[rows_a, cols_a], emf_r[rows_a, cols_b], emf_r[rows_b, cols_a], emf_r[rows_b, cols_b])

    inner = (slice(1, ct + 1), slice(1, npc + 1))
    new_radial = x[5][inner] - TIME_STEP * (
        (ep_lo[1:] - ep_lo[:-1]) - (et_lo[:, 1:] - et_lo[:, :-1])
    )
    new_theta = x[6][inner] - TIME_STEP * (
        (er[:-1, 1:] - er[:-1, :-1]) - (ep_hi[:-1] - ep_lo[:-1])
    )
    new_phi = x[7][inner] - TIME_STEP * (
        (et_hi[:, :-1] - et_lo[:, :-1]) - (er[1:, :-1] - er[:-1, :-1])
    )
    return jnp.stack(densities), jnp.stack([new_radial, new_theta, new_phi])


def fourier_rows(cols, cycle_len):
    orders = jnp.arange(KMAX, dtype=jnp.int32)
    phase = (cols[..., None] * orders) % cycle_len
    angle = phase.astype(jnp.float32) * (2.0 * math.pi / cycle_len)
    return jnp.concatenate([jnp.cos(angle), jnp.sin(angle)], axis=-1)


def local(density, velocity, bfield, levels):
    combined = jnp.concatenate([density, velocity, bfield], axis=0)
    channels, ct, npc, nr = combined.shape
    theta_count = lax.axis_size("theta")
    phi_count = lax.axis_size("phi")
    t = lax.axis_index("theta")
    p = lax.axis_index("phi")
    at_north = t == 0
    at_south = t == theta_count - 1
    cycle_len = npc * phi_count
    parity = jnp.array(PARITY, jnp.float32)
    poles = (0, theta_count - 1)
    both = ("theta", "phi")

    def pole_pairs(shift):
        return [
            (a * phi_count + b, a * phi_count + (b + shift) % phi_count)
            for a in poles
            for b in range(phi_count)
        ]

    low_halo = lax.ppermute(
        combined[:, ct - 1], "theta", [(i, i + 1) for i in range(theta_count - 1)]
    )
    up_send = jnp.concatenate([combined[:, 0], combined[6:7, 1]], axis=0)
    up_halo = lax.ppermute(up_send, "theta", [(i + 1, i) for i in range(theta_count - 1)])
    rows_ext = jnp.concatenate(
        [
            low_halo[:, None],
            combined,
            up_halo[:channels, None],
            jnp.broadcast_to(up_halo[channels:], (channels, npc, nr))[:, None],
        ],
        axis=1,
    )
    left_cols = lax.ppermute(
        rows_ext[:, :, npc - 1 :], "phi", [(i, (i + 1) % phi_count) for i in range(phi_count)]
    )
    right_cols = lax.ppermute(
        rows_ext[:, :, :2], "phi", [((i + 1) % phi_count, i) for i in range(phi_count)]
    )
    early = jnp.concatenate([left_cols, rows_ext, right_cols], axis=2)

    north_side = t <= 1
    helper = (t == 1) | (t == theta_count - 2)
    half = channels * CAP // 2
    first_half = jnp.concatenate([density, velocity[:2]], axis=0)
    second_half = jnp.concatenate([velocity[2:], bfield], axis=0)

    def cap_of(fields):
        rows = jnp.where(at_north, fields[:, :CAP], fields[:, ct - CAP :])
        return rows.reshape(half, npc, nr)

    pairs_out = [(0, 1), (theta_count - 1, theta_count - 2)]
    pairs_in = [(1, 0), (theta_count - 2, theta_count - 1)]
    handed = lax.ppermute(cap_of(second_half), "theta", pairs_out)
    work = jnp.where(helper, handed, cap_of(first_half))
    per_device = half // phi_count
    cycle = lax.all_to_all(work, "phi", split_axis=0, concat_axis=1, tiled=True)
    analysis = fourier_rows(jnp.arange(cycle_len, dtype=jnp.int32), cycle_len)
    dst_cols = (
        jnp.arange(phi_count, dtype=jnp.int32)[:, None] * npc
        - 1
        + jnp.arange(npc + 3, dtype=jnp.int32)[None, :]
    ) % cycle_len
    synthesis = fourier_rows(dst_cols, cycle_len)

    pole_pick = jnp.where(north_side, 0, 1).astype(jnp.int32)
    level_row = lax.dynamic_index_in_dim(levels, pole_pick, 0, keepdims=False)
    slot_ids = jnp.where(helper, half, 0) + p * per_device + jnp.arange(per_device, dtype=jnp.int32)
    row_ids = slot_ids % CAP
    slot_levels = jnp.sum(
        jnp.where(
            row_ids[:, None] == jnp.arange(CAP, dtype=jnp.int32)[None, :], level_row[None, :], 0
        ),
        axis=1,
    )
    limits = jnp.right_shift(jnp.int32(KMAX), slot_levels)
    column_order = jnp.arange(2 * KMAX, dtype=jnp.int32) % KMAX
    column_weight = jnp.where(column_order == 0, 1.0 / cycle_len, 2.0 / cycle_len).astype(
        jnp.float32
    )
    kept_weight = jnp.where(column_order[None, :] < limits[:, None], column_weight[None, :], 0.0)
    coeffs = jnp.einsum("smr,mn->snr", cycle, analysis, precision=lax.Precision.HIGHEST)
    coeffs = coeffs * kept_weight[:, :, None]
    out = jnp.einsum("snr,kjn->ksjr", coeffs, synthesis, precision=lax.Precision.HIGHEST)
    out = out.reshape(phi_count * per_device, npc + 3, nr)
    mine = lax.all_to_all(out, "phi", split_axis=0, concat_axis=0, tiled=True)

    from_helper = lax.ppermute(mine, "theta", pairs_in)
    cap_rows = jnp.concatenate([mine, from_helper], axis=0).reshape(channels, CAP, npc + 3, nr)
    per_half = channels // 2
    first_rows = mine[0::CAP]
    last_rows = mine[CAP - 1 :: CAP]
    spare = mine[(6 - per_half) * CAP + CAP - 2 : (6 - per_half) * CAP + CAP - 1]
    ghost_send = jnp.concatenate([jnp.where(north_side, first_rows, last_rows), spare], axis=0)
    turn = phi_count // 2
    pole_ghost = lax.ppermute(
        ghost_send,
        both,
        [(a * phi_count + b, a * phi_count + (b + turn) % phi_count) for a in poles for b in range(phi_count)],
    )
    helper_ghost = lax.ppermute(
        ghost_send,
        both,
        [
            (h * phi_count + b, a * phi_count + (b + turn) % phi_count)
            for h, a in ((1, 0), (theta_count - 2, theta_count - 1))
            for b in range(phi_count)
        ],
    )
    ghost_main = jnp.concatenate([pole_ghost[:per_half], helper_ghost[:per_half]], axis=0)
    ghost_main = ghost_main * parity[:, None, None]
    ghost_b = helper_ghost[per_half:] * parity[6]
    north_block = jnp.concatenate(
        [ghost_main[:, None], cap_rows, early[:, CAP + 1 : CAP + 2]], axis=1
    )
    south_block = jnp.concatenate(
        [
            cap_rows,
            ghost_main[:, None],
            jnp.broadcast_to(ghost_b, (channels, npc + 3, nr))[:, None],
        ],
        axis=1,
    )
    offset = jnp.where(at_north, 0, ct - CAP + 1)
    kept_block = lax.dynamic_slice_in_dim(early, offset, CAP + 2, axis=1)
    block = jnp.where(
        at_north, north_block, jnp.where(at_south, south_block, kept_block)
    )
    extended = lax.dynamic_update_slice_in_dim(early, block, offset, axis=1)
    return advance(extended)


def solution(mesh):
    return jax.shard_map(
        local,
        mesh=mesh,
        in_specs=(
            P(None, "theta", "phi", None),
            P(None, "theta", "phi", None),
            P(None, "theta", "phi", None),
            P(),
        ),
        out_specs=(P(None, "theta", "phi", None), P(None, "theta", "phi", None)),
        check_vma=False,
    )
```

```python
import math

import jax
import jax.numpy as jnp
from jax import lax
from jax.sharding import PartitionSpec as P

CAP = 4
KMAX = 128


TIME_STEP = 0.2
PARITY = (1.0, 1.0, 1.0, -1.0, -1.0, 1.0, -1.0, -1.0)


def up_r(a):
    return jnp.concatenate([a[..., 1:], a[..., -1:]], axis=-1)


def down_r(a):
    return jnp.concatenate([a[..., :1], a[..., :-1]], axis=-1)


def face_flux(left_amount, right_amount, left_speed, right_speed):
    return 0.5 * (left_amount * left_speed + right_amount * right_speed) - 0.5 * jnp.maximum(
        jnp.abs(left_speed), jnp.abs(right_speed)
    ) * (right_amount - left_amount)


def corner4(e00, e01, e10, e11):
    return 0.25 * (((e00 + e01) + e10) + e11)


def advance(x):
    ct = x.shape[1] - 3
    npc = x.shape[2] - 3
    densities = []
    for channel in range(2):
        q = x[channel]
        v_t = x[3]
        v_p = x[4]
        v_r = x[2]
        fl_t = face_flux(
            q[0 : ct + 1, 1 : npc + 1], q[1 : ct + 2, 1 : npc + 1],
            v_t[0 : ct + 1, 1 : npc + 1], v_t[1 : ct + 2, 1 : npc + 1],
        )
        fl_p = face_flux(
            q[1 : ct + 1, 0 : npc + 1], q[1 : ct + 1, 1 : npc + 2],
            v_p[1 : ct + 1, 0 : npc + 1], v_p[1 : ct + 1, 1 : npc + 2],
        )
        qi = q[1 : ct + 1, 1 : npc + 1]
        vi = v_r[1 : ct + 1, 1 : npc + 1]
        fl_lo = face_flux(down_r(qi), qi, down_r(vi), vi)
        fl_hi = face_flux(qi, up_r(qi), vi, up_r(vi))
        tendency = (fl_t[1:] - fl_t[:-1]) + (fl_p[:, 1:] - fl_p[:, :-1]) + (fl_hi - fl_lo)
        densities.append(qi - TIME_STEP * tendency)

    wr = slice(0, ct + 2)
    wc = slice(0, npc + 2)
    b_r = x[5][wr, wc]
    b_t = x[6]
    b_p = x[7]
    c_r = 0.5 * (b_r + up_r(b_r))
    c_t = 0.5 * (b_t[0 : ct + 2, wc] + b_t[1 : ct + 3, wc])
    c_p = 0.5 * (b_p[wr, 0 : npc + 2] + b_p[wr, 1 : npc + 3])
    s_r = x[2][wr, wc]
    s_t = x[3][wr, wc]
    s_p = x[4][wr, wc]
    emf_r = -(s_t * c_p - s_p * c_t)
    emf_t = -(s_p * c_r - s_r * c_p)
    emf_p = -(s_r * c_t - s_t * c_r)
    lane = lax.broadcasted_iota(jnp.int32, emf_t.shape, 2)
    last = emf_t.shape[2] - 1
    edge_t = -(s_p * b_r - s_r * c_p)
    edge_p = -(s_r * c_t - s_t * b_r)
    t_lo = jnp.where(lane == 0, edge_t, down_r(emf_t))
    t_hi = jnp.where(lane == last, edge_t, up_r(emf_t))
    p_lo = jnp.where(lane == 0, edge_p, down_r(emf_p))
    p_hi = jnp.where(lane == last, edge_p, up_r(emf_p))

    rows_a = slice(0, ct + 1)
    rows_b = slice(1, ct + 2)
    cols_in = slice(1, npc + 1)
    ep_lo = corner4(p_lo[rows_a, cols_in], emf_p[rows_a, cols_in], p_lo[rows_b, cols_in], emf_p[rows_b, cols_in])
    ep_hi = corner4(emf_p[rows_a, cols_in], p_hi[rows_a, cols_in], emf_p[rows_b, cols_in], p_hi[rows_b, cols_in])
    rows_in = slice(1, ct + 1)
    cols_a = slice(0, npc + 1)
    cols_b = slice(1, npc + 2)
    et_lo = corner4(t_lo[rows_in, cols_a], emf_t[rows_in, cols_a], t_lo[rows_in, cols_b], emf_t[rows_in, cols_b])
    et_hi = corner4(emf_t[rows_in, cols_a], t_hi[rows_in, cols_a], emf_t[rows_in, cols_b], t_hi[rows_in, cols_b])
    er = corner4(emf_r[rows_a, cols_a], emf_r[rows_a, cols_b], emf_r[rows_b, cols_a], emf_r[rows_b, cols_b])

    inner = (slice(1, ct + 1), slice(1, npc + 1))
    new_radial = x[5][inner] - TIME_STEP * (
        (ep_lo[1:] - ep_lo[:-1]) - (et_lo[:, 1:] - et_lo[:, :-1])
    )
    new_theta = x[6][inner] - TIME_STEP * (
        (er[:-1, 1:] - er[:-1, :-1]) - (ep_hi[:-1] - ep_lo[:-1])
    )
    new_phi = x[7][inner] - TIME_STEP * (
        (et_hi[:, :-1] - et_lo[:, :-1]) - (er[1:, :-1] - er[:-1, :-1])
    )
    return jnp.stack(densities), jnp.stack([new_radial, new_theta, new_phi])


def fourier_rows(cols, cycle_len):
    orders = jnp.arange(KMAX, dtype=jnp.int32)
    phase = (cols[..., None] * orders) % cycle_len
    angle = phase.astype(jnp.float32) * (2.0 * math.pi / cycle_len)
    return jnp.concatenate([jnp.cos(angle), jnp.sin(angle)], axis=-1)


def local(density, velocity, bfield, levels):
    combined = jnp.concatenate([density, velocity, bfield], axis=0)
    channels, ct, npc, nr = combined.shape
    theta_count = lax.axis_size("theta")
    phi_count = lax.axis_size("phi")
    t = lax.axis_index("theta")
    p = lax.axis_index("phi")
    at_north = t == 0
    at_south = t == theta_count - 1
    cycle_len = npc * phi_count
    parity = jnp.array(PARITY, jnp.float32)
    poles = (0, theta_count - 1)
    both = ("theta", "phi")

    def pole_pairs(shift):
        return [
            (a * phi_count + b, a * phi_count + (b + shift) % phi_count)
            for a in poles
            for b in range(phi_count)
        ]

    low_halo = lax.ppermute(
        combined[:, ct - 1], "theta", [(i, i + 1) for i in range(theta_count - 1)]
    )
    up_send = jnp.concatenate([combined[:, 0], combined[6:7, 1]], axis=0)
    up_halo = lax.ppermute(up_send, "theta", [(i + 1, i) for i in range(theta_count - 1)])
    rows_ext = jnp.concatenate(
        [
            low_halo[:, None],
            combined,
            up_halo[:channels, None],
            jnp.broadcast_to(up_halo[channels:], (channels, npc, nr))[:, None],
        ],
        axis=1,
    )
    left_cols = lax.ppermute(
        rows_ext[:, :, npc - 1 :], "phi", [(i, (i + 1) % phi_count) for i in range(phi_count)]
    )
    right_cols = lax.ppermute(
        rows_ext[:, :, :2], "phi", [((i + 1) % phi_count, i) for i in range(phi_count)]
    )
    early = jnp.concatenate([left_cols, rows_ext, right_cols], axis=2)

    north_side = t <= 1
    helper = (t == 1) | (t == theta_count - 2)
    half = channels * CAP // 2
    first_half = jnp.concatenate([density, velocity[:2]], axis=0)
    second_half = jnp.concatenate([velocity[2:], bfield], axis=0)

    def cap_of(fields):
        rows = jnp.where(at_north, fields[:, :CAP], fields[:, ct - CAP :])
        return jnp.swapaxes(rows, 0, 1).reshape(half, npc, nr)

    pairs_out = [(0, 1), (theta_count - 1, theta_count - 2)]
    pairs_in = [(1, 0), (theta_count - 2, theta_count - 1)]
    handed = lax.ppermute(cap_of(second_half), "theta", pairs_out)
    work = jnp.where(helper, handed, cap_of(first_half))
    per_device = half // phi_count
    cycle = lax.all_to_all(work, "phi", split_axis=0, concat_axis=1, tiled=True)
    analysis = fourier_rows(jnp.arange(cycle_len, dtype=jnp.int32), cycle_len)
    dst_cols = (
        jnp.arange(phi_count, dtype=jnp.int32)[:, None] * npc
        - 1
        + jnp.arange(npc + 3, dtype=jnp.int32)[None, :]
    ) % cycle_len
    synthesis = fourier_rows(dst_cols, cycle_len)

    pole_pick = jnp.where(north_side, 0, 1).astype(jnp.int32)
    level_row = lax.dynamic_index_in_dim(levels, pole_pick, 0, keepdims=False)
    slot_ids = p * per_device + jnp.arange(per_device, dtype=jnp.int32)
    row_ids = slot_ids // (channels // 2)
    slot_levels = jnp.sum(
        jnp.where(
            row_ids[:, None] == jnp.arange(CAP, dtype=jnp.int32)[None, :], level_row[None, :], 0
        ),
        axis=1,
    )
    limits = jnp.right_shift(jnp.int32(KMAX), slot_levels)
    column_order = jnp.arange(2 * KMAX, dtype=jnp.int32) % KMAX
    column_weight = jnp.where(column_order == 0, 1.0 / cycle_len, 2.0 / cycle_len).astype(
        jnp.float32
    )
    kept_weight = jnp.where(column_order[None, :] < limits[:, None], column_weight[None, :], 0.0)
    coeffs = jnp.einsum("smr,mn->snr", cycle, analysis, precision=lax.Precision.HIGHEST)
    coeffs = coeffs * kept_weight[:, :, None]
    out = jnp.einsum("snr,kjn->ksjr", coeffs, synthesis, precision=lax.Precision.HIGHEST)
    out = out.reshape(phi_count * per_device, npc + 3, nr)
    mine = lax.all_to_all(out, "phi", split_axis=0, concat_axis=0, tiled=True)

    from_helper = lax.ppermute(mine, "theta", pairs_in)
    per_half = channels // 2
    cap_rows = jnp.concatenate([mine, from_helper], axis=0).reshape(2, CAP, per_half, npc + 3, nr)
    cap_rows = jnp.transpose(cap_rows, (0, 2, 1, 3, 4)).reshape(channels, CAP, npc + 3, nr)
    first_rows = mine[:per_half]
    last_rows = mine[(CAP - 1) * per_half :]
    spare_at = (CAP - 2) * per_half + 6 - per_half
    spare = mine[spare_at : spare_at + 1]
    ghost_send = jnp.concatenate([jnp.where(north_side, first_rows, last_rows), spare], axis=0)
    turn = phi_count // 2
    pole_ghost = lax.ppermute(
        ghost_send,
        both,
        [(a * phi_count + b, a * phi_count + (b + turn) % phi_count) for a in poles for b in range(phi_count)],
    )
    helper_ghost = lax.ppermute(
        ghost_send,
        both,
        [
            (h * phi_count + b, a * phi_count + (b + turn) % phi_count)
            for h, a in ((1, 0), (theta_count - 2, theta_count - 1))
            for b in range(phi_count)
        ],
    )
    ghost_main = jnp.concatenate([pole_ghost[:per_half], helper_ghost[:per_half]], axis=0)
    ghost_main = ghost_main * parity[:, None, None]
    ghost_b = helper_ghost[per_half:] * parity[6]
    north_block = jnp.concatenate(
        [ghost_main[:, None], cap_rows, early[:, CAP + 1 : CAP + 2]], axis=1
    )
    south_block = jnp.concatenate(
        [
            cap_rows,
            ghost_main[:, None],
            jnp.broadcast_to(ghost_b, (channels, npc + 3, nr))[:, None],
        ],
        axis=1,
    )
    offset = jnp.where(at_north, 0, ct - CAP + 1)
    kept_block = lax.dynamic_slice_in_dim(early, offset, CAP + 2, axis=1)
    block = jnp.where(
        at_north, north_block, jnp.where(at_south, south_block, kept_block)
    )
    extended = lax.dynamic_update_slice_in_dim(early, block, offset, axis=1)
    return advance(extended)


def solution(mesh):
    return jax.shard_map(
        local,
        mesh=mesh,
        in_specs=(
            P(None, "theta", "phi", None),
            P(None, "theta", "phi", None),
            P(None, "theta", "phi", None),
            P(),
        ),
        out_specs=(P(None, "theta", "phi", None), P(None, "theta", "phi", None)),
        check_vma=False,
    )
```

```python
import math

import jax
import jax.numpy as jnp
from jax import lax
from jax.sharding import PartitionSpec as P

CAP = 4
KMAX = 128


TIME_STEP = 0.2
PARITY = (1.0, 1.0, 1.0, -1.0, -1.0, 1.0, -1.0, -1.0)


def up_r(a):
    return jnp.concatenate([a[..., 1:], a[..., -1:]], axis=-1)


def down_r(a):
    return jnp.concatenate([a[..., :1], a[..., :-1]], axis=-1)


def face_flux(left_amount, right_amount, left_speed, right_speed):
    return 0.5 * (left_amount * left_speed + right_amount * right_speed) - 0.5 * jnp.maximum(
        jnp.abs(left_speed), jnp.abs(right_speed)
    ) * (right_amount - left_amount)


def corner4(e00, e01, e10, e11):
    return 0.25 * (((e00 + e01) + e10) + e11)


def advance(x):
    ct = x.shape[1] - 3
    npc = x.shape[2] - 3
    densities = []
    for channel in range(2):
        q = x[channel]
        v_t = x[3]
        v_p = x[4]
        v_r = x[2]
        fl_t = face_flux(
            q[0 : ct + 1, 1 : npc + 1], q[1 : ct + 2, 1 : npc + 1],
            v_t[0 : ct + 1, 1 : npc + 1], v_t[1 : ct + 2, 1 : npc + 1],
        )
        fl_p = face_flux(
            q[1 : ct + 1, 0 : npc + 1], q[1 : ct + 1, 1 : npc + 2],
            v_p[1 : ct + 1, 0 : npc + 1], v_p[1 : ct + 1, 1 : npc + 2],
        )
        qi = q[1 : ct + 1, 1 : npc + 1]
        vi = v_r[1 : ct + 1, 1 : npc + 1]
        fl_lo = face_flux(down_r(qi), qi, down_r(vi), vi)
        fl_hi = face_flux(qi, up_r(qi), vi, up_r(vi))
        tendency = (fl_t[1:] - fl_t[:-1]) + (fl_p[:, 1:] - fl_p[:, :-1]) + (fl_hi - fl_lo)
        densities.append(qi - TIME_STEP * tendency)

    wr = slice(0, ct + 2)
    wc = slice(0, npc + 2)
    b_r = x[5][wr, wc]
    b_t = x[6]
    b_p = x[7]
    c_r = 0.5 * (b_r + up_r(b_r))
    c_t = 0.5 * (b_t[0 : ct + 2, wc] + b_t[1 : ct + 3, wc])
    c_p = 0.5 * (b_p[wr, 0 : npc + 2] + b_p[wr, 1 : npc + 3])
    s_r = x[2][wr, wc]
    s_t = x[3][wr, wc]
    s_p = x[4][wr, wc]
    emf_r = -(s_t * c_p - s_p * c_t)
    emf_t = -(s_p * c_r - s_r * c_p)
    emf_p = -(s_r * c_t - s_t * c_r)
    lane = lax.broadcasted_iota(jnp.int32, emf_t.shape, 2)
    last = emf_t.shape[2] - 1
    edge_t = -(s_p * b_r - s_r * c_p)
    edge_p = -(s_r * c_t - s_t * b_r)
    t_lo = jnp.where(lane == 0, edge_t, down_r(emf_t))
    t_hi = jnp.where(lane == last, edge_t, up_r(emf_t))
    p_lo = jnp.where(lane == 0, edge_p, down_r(emf_p))
    p_hi = jnp.where(lane == last, edge_p, up_r(emf_p))

    rows_a = slice(0, ct + 1)
    rows_b = slice(1, ct + 2)
    cols_in = slice(1, npc + 1)
    ep_lo = corner4(p_lo[rows_a, cols_in], emf_p[rows_a, cols_in], p_lo[rows_b, cols_in], emf_p[rows_b, cols_in])
    ep_hi = corner4(emf_p[rows_a, cols_in], p_hi[rows_a, cols_in], emf_p[rows_b, cols_in], p_hi[rows_b, cols_in])
    rows_in = slice(1, ct + 1)
    cols_a = slice(0, npc + 1)
    cols_b = slice(1, npc + 2)
    et_lo = corner4(t_lo[rows_in, cols_a], emf_t[rows_in, cols_a], t_lo[rows_in, cols_b], emf_t[rows_in, cols_b])
    et_hi = corner4(emf_t[rows_in, cols_a], t_hi[rows_in, cols_a], emf_t[rows_in, cols_b], t_hi[rows_in, cols_b])
    er = corner4(emf_r[rows_a, cols_a], emf_r[rows_a, cols_b], emf_r[rows_b, cols_a], emf_r[rows_b, cols_b])

    inner = (slice(1, ct + 1), slice(1, npc + 1))
    new_radial = x[5][inner] - TIME_STEP * (
        (ep_lo[1:] - ep_lo[:-1]) - (et_lo[:, 1:] - et_lo[:, :-1])
    )
    new_theta = x[6][inner] - TIME_STEP * (
        (er[:-1, 1:] - er[:-1, :-1]) - (ep_hi[:-1] - ep_lo[:-1])
    )
    new_phi = x[7][inner] - TIME_STEP * (
        (et_hi[:, :-1] - et_lo[:, :-1]) - (er[1:, :-1] - er[:-1, :-1])
    )
    return jnp.stack(densities), jnp.stack([new_radial, new_theta, new_phi])


def fourier_rows(cols, cycle_len):
    orders = jnp.arange(KMAX, dtype=jnp.int32)
    phase = (cols[..., None] * orders) % cycle_len
    angle = phase.astype(jnp.float32) * (2.0 * math.pi / cycle_len)
    return jnp.concatenate([jnp.cos(angle), jnp.sin(angle)], axis=-1)


def local(density, velocity, bfield, levels):
    combined = jnp.concatenate([density, velocity, bfield], axis=0)
    channels, ct, npc, nr = combined.shape
    theta_count = lax.axis_size("theta")
    phi_count = lax.axis_size("phi")
    t = lax.axis_index("theta")
    p = lax.axis_index("phi")
    at_north = t == 0
    at_south = t == theta_count - 1
    cycle_len = npc * phi_count
    parity = jnp.array(PARITY, jnp.float32)
    poles = (0, theta_count - 1)
    both = ("theta", "phi")

    def pole_pairs(shift):
        return [
            (a * phi_count + b, a * phi_count + (b + shift) % phi_count)
            for a in poles
            for b in range(phi_count)
        ]

    low_halo = lax.ppermute(
        combined[:, ct - 1], "theta", [(i, i + 1) for i in range(theta_count - 1)]
    )
    up_send = jnp.concatenate([combined[:, 0], combined[6:7, 1]], axis=0)
    up_halo = lax.ppermute(up_send, "theta", [(i + 1, i) for i in range(theta_count - 1)])
    rows_ext = jnp.concatenate(
        [
            low_halo[:, None],
            combined,
            up_halo[:channels, None],
            jnp.broadcast_to(up_halo[channels:], (channels, npc, nr))[:, None],
        ],
        axis=1,
    )
    left_cols = lax.ppermute(
        rows_ext[:, :, npc - 1 :], "phi", [(i, (i + 1) % phi_count) for i in range(phi_count)]
    )
    right_cols = lax.ppermute(
        rows_ext[:, :, :2], "phi", [((i + 1) % phi_count, i) for i in range(phi_count)]
    )
    early = jnp.concatenate([left_cols, rows_ext, right_cols], axis=2)

    north_side = t <= 1
    helper = (t == 1) | (t == theta_count - 2)
    half = channels * CAP // 2
    first_half = jnp.concatenate([density, velocity[:2]], axis=0)
    second_half = jnp.concatenate([velocity[2:], bfield], axis=0)

    def cap_of(fields):
        rows = jnp.where(at_north, fields[:, :CAP], fields[:, ct - CAP :])
        return jnp.swapaxes(rows, 0, 1).reshape(half, npc, nr)

    pairs_out = [(0, 1), (theta_count - 1, theta_count - 2)]
    pairs_in = [(1, 0), (theta_count - 2, theta_count - 1)]
    handed = lax.ppermute(cap_of(second_half), "theta", pairs_out)
    work = jnp.where(helper, handed, cap_of(first_half))
    per_device = half // phi_count
    cycle = lax.all_to_all(work, "phi", split_axis=0, concat_axis=1, tiled=True)
    analysis = fourier_rows(jnp.arange(cycle_len, dtype=jnp.int32), cycle_len)
    dst_cols = (
        jnp.arange(phi_count, dtype=jnp.int32)[:, None] * npc
        - 1
        + jnp.arange(npc + 3, dtype=jnp.int32)[None, :]
    ) % cycle_len
    synthesis = fourier_rows(dst_cols, cycle_len)

    pole_pick = jnp.where(north_side, 0, 1).astype(jnp.int32)
    level_row = lax.dynamic_index_in_dim(levels, pole_pick, 0, keepdims=False)
    slot_ids = p * per_device + jnp.arange(per_device, dtype=jnp.int32)
    row_ids = slot_ids // (channels // 2)
    slot_levels = jnp.sum(
        jnp.where(
            row_ids[:, None] == jnp.arange(CAP, dtype=jnp.int32)[None, :], level_row[None, :], 0
        ),
        axis=1,
    )
    limits = jnp.right_shift(jnp.int32(KMAX), slot_levels)
    column_order = jnp.arange(2 * KMAX, dtype=jnp.int32) % KMAX
    column_weight = jnp.where(column_order == 0, 1.0 / cycle_len, 2.0 / cycle_len).astype(
        jnp.float32
    )
    kept_weight = jnp.where(column_order[None, :] < limits[:, None], column_weight[None, :], 0.0)
    coeffs = jnp.einsum("smr,mn->snr", cycle, analysis, precision=lax.Precision.HIGHEST)
    coeffs = coeffs * kept_weight[:, :, None]
    out = jnp.einsum("snr,kjn->ksjr", coeffs, synthesis, precision=lax.Precision.HIGHEST)
    out = out.reshape(phi_count * per_device, npc + 3, nr)
    mine = lax.all_to_all(out, "phi", split_axis=0, concat_axis=0, tiled=True)

    from_helper = lax.ppermute(mine, "theta", pairs_in)
    per_half = channels // 2
    cap_rows = jnp.concatenate([mine, from_helper], axis=0).reshape(2, CAP, per_half, npc + 3, nr)
    cap_rows = jnp.transpose(cap_rows, (0, 2, 1, 3, 4)).reshape(channels, CAP, npc + 3, nr)
    first_rows = mine[:per_half]
    last_rows = mine[(CAP - 1) * per_half :]
    spare_at = (CAP - 2) * per_half + 6 - per_half
    spare = mine[spare_at : spare_at + 1]
    ghost_send = jnp.concatenate([jnp.where(north_side, first_rows, last_rows), spare], axis=0)
    turn = phi_count // 2
    pole_ghost = lax.ppermute(
        ghost_send,
        both,
        [(a * phi_count + b, a * phi_count + (b + turn) % phi_count) for a in poles for b in range(phi_count)],
    )
    helper_ghost = lax.ppermute(
        ghost_send,
        both,
        [
            (h * phi_count + b, a * phi_count + (b + turn) % phi_count)
            for h, a in ((1, 0), (theta_count - 2, theta_count - 1))
            for b in range(phi_count)
        ],
    )
    ghost_main = jnp.concatenate([pole_ghost[:per_half], helper_ghost[:per_half]], axis=0)
    ghost_main = ghost_main * parity[:, None, None]
    ghost_b = helper_ghost[per_half:] * parity[6]
    north_block = jnp.concatenate(
        [ghost_main[:, None], cap_rows, early[:, CAP + 1 : CAP + 2]], axis=1
    )
    south_block = jnp.concatenate(
        [
            cap_rows,
            ghost_main[:, None],
            jnp.broadcast_to(ghost_b, (channels, npc + 3, nr))[:, None],
        ],
        axis=1,
    )
    offset = jnp.where(at_north, 0, ct - CAP + 1)
    kept_block = lax.dynamic_slice_in_dim(early, offset, CAP + 2, axis=1)
    block = jnp.where(at_north, north_block, jnp.where(at_south, south_block, kept_block))
    extended = lax.dynamic_update_slice_in_dim(early, block, offset, axis=1)

    cap_start = jnp.where(at_north, 1, ct - CAP + 1)
    kept_cap = lax.dynamic_slice_in_dim(early, cap_start, CAP, axis=1)
    cap_block = jnp.where(at_north | at_south, cap_rows, kept_cap)
    with_caps = lax.dynamic_update_slice_in_dim(early, cap_block, cap_start, axis=1)

    near_rows = 2
    far_rows = ct - CAP - near_rows
    mid_rows = CAP

    def rows_from(x, first, count):
        return advance(lax.dynamic_slice_in_dim(x, first, count + 3, axis=1))

    far = rows_from(early, jnp.where(at_north, ct - far_rows, 0), far_rows)
    mid = rows_from(with_caps, jnp.where(at_north, near_rows, far_rows), mid_rows)
    near = rows_from(extended, jnp.where(at_north, 0, ct - near_rows), near_rows)
    outs = []
    for a, b, c in zip(far, mid, near):
        north_order = jnp.concatenate([c, b, a], axis=1)
        other_order = jnp.concatenate([a, b, c], axis=1)
        outs.append(jnp.where(at_north, north_order, other_order))
    return tuple(outs)


def solution(mesh):
    return jax.shard_map(
        local,
        mesh=mesh,
        in_specs=(
            P(None, "theta", "phi", None),
            P(None, "theta", "phi", None),
            P(None, "theta", "phi", None),
            P(),
        ),
        out_specs=(P(None, "theta", "phi", None), P(None, "theta", "phi", None)),
        check_vma=False,
    )
```

```python
import math

import jax
import jax.numpy as jnp
from jax import lax
from jax.sharding import PartitionSpec as P

CAP = 4
KMAX = 128


TIME_STEP = 0.2
PARITY = (1.0, 1.0, 1.0, -1.0, -1.0, 1.0, -1.0, -1.0)


def up_r(a):
    return jnp.concatenate([a[..., 1:], a[..., -1:]], axis=-1)


def down_r(a):
    return jnp.concatenate([a[..., :1], a[..., :-1]], axis=-1)


def face_flux(left_amount, right_amount, left_speed, right_speed):
    return 0.5 * (left_amount * left_speed + right_amount * right_speed) - 0.5 * jnp.maximum(
        jnp.abs(left_speed), jnp.abs(right_speed)
    ) * (right_amount - left_amount)


def corner4(e00, e01, e10, e11):
    return 0.25 * (((e00 + e01) + e10) + e11)


def advance(x):
    ct = x.shape[1] - 3
    npc = x.shape[2] - 3
    densities = []
    for channel in range(2):
        q = x[channel]
        v_t = x[3]
        v_p = x[4]
        v_r = x[2]
        fl_t = face_flux(
            q[0 : ct + 1, 1 : npc + 1], q[1 : ct + 2, 1 : npc + 1],
            v_t[0 : ct + 1, 1 : npc + 1], v_t[1 : ct + 2, 1 : npc + 1],
        )
        fl_p = face_flux(
            q[1 : ct + 1, 0 : npc + 1], q[1 : ct + 1, 1 : npc + 2],
            v_p[1 : ct + 1, 0 : npc + 1], v_p[1 : ct + 1, 1 : npc + 2],
        )
        qi = q[1 : ct + 1, 1 : npc + 1]
        vi = v_r[1 : ct + 1, 1 : npc + 1]
        fl_lo = face_flux(down_r(qi), qi, down_r(vi), vi)
        fl_hi = face_flux(qi, up_r(qi), vi, up_r(vi))
        tendency = (fl_t[1:] - fl_t[:-1]) + (fl_p[:, 1:] - fl_p[:, :-1]) + (fl_hi - fl_lo)
        densities.append(qi - TIME_STEP * tendency)

    wr = slice(0, ct + 2)
    wc = slice(0, npc + 2)
    b_r = x[5][wr, wc]
    b_t = x[6]
    b_p = x[7]
    c_r = 0.5 * (b_r + up_r(b_r))
    c_t = 0.5 * (b_t[0 : ct + 2, wc] + b_t[1 : ct + 3, wc])
    c_p = 0.5 * (b_p[wr, 0 : npc + 2] + b_p[wr, 1 : npc + 3])
    s_r = x[2][wr, wc]
    s_t = x[3][wr, wc]
    s_p = x[4][wr, wc]
    emf_r = -(s_t * c_p - s_p * c_t)
    emf_t = -(s_p * c_r - s_r * c_p)
    emf_p = -(s_r * c_t - s_t * c_r)
    lane = lax.broadcasted_iota(jnp.int32, emf_t.shape, 2)
    last = emf_t.shape[2] - 1
    edge_t = -(s_p * b_r - s_r * c_p)
    edge_p = -(s_r * c_t - s_t * b_r)
    t_lo = jnp.where(lane == 0, edge_t, down_r(emf_t))
    t_hi = jnp.where(lane == last, edge_t, up_r(emf_t))
    p_lo = jnp.where(lane == 0, edge_p, down_r(emf_p))
    p_hi = jnp.where(lane == last, edge_p, up_r(emf_p))

    rows_a = slice(0, ct + 1)
    rows_b = slice(1, ct + 2)
    cols_in = slice(1, npc + 1)
    ep_lo = corner4(p_lo[rows_a, cols_in], emf_p[rows_a, cols_in], p_lo[rows_b, cols_in], emf_p[rows_b, cols_in])
    ep_hi = corner4(emf_p[rows_a, cols_in], p_hi[rows_a, cols_in], emf_p[rows_b, cols_in], p_hi[rows_b, cols_in])
    rows_in = slice(1, ct + 1)
    cols_a = slice(0, npc + 1)
    cols_b = slice(1, npc + 2)
    et_lo = corner4(t_lo[rows_in, cols_a], emf_t[rows_in, cols_a], t_lo[rows_in, cols_b], emf_t[rows_in, cols_b])
    et_hi = corner4(emf_t[rows_in, cols_a], t_hi[rows_in, cols_a], emf_t[rows_in, cols_b], t_hi[rows_in, cols_b])
    er = corner4(emf_r[rows_a, cols_a], emf_r[rows_a, cols_b], emf_r[rows_b, cols_a], emf_r[rows_b, cols_b])

    inner = (slice(1, ct + 1), slice(1, npc + 1))
    new_radial = x[5][inner] - TIME_STEP * (
        (ep_lo[1:] - ep_lo[:-1]) - (et_lo[:, 1:] - et_lo[:, :-1])
    )
    new_theta = x[6][inner] - TIME_STEP * (
        (er[:-1, 1:] - er[:-1, :-1]) - (ep_hi[:-1] - ep_lo[:-1])
    )
    new_phi = x[7][inner] - TIME_STEP * (
        (et_hi[:, :-1] - et_lo[:, :-1]) - (er[1:, :-1] - er[:-1, :-1])
    )
    return jnp.stack(densities), jnp.stack([new_radial, new_theta, new_phi])


def fourier_rows(cols, cycle_len):
    orders = jnp.arange(KMAX, dtype=jnp.int32)
    phase = (cols[..., None] * orders) % cycle_len
    angle = phase.astype(jnp.float32) * (2.0 * math.pi / cycle_len)
    return jnp.concatenate([jnp.cos(angle), jnp.sin(angle)], axis=-1)


def local(density, velocity, bfield, levels):
    combined = jnp.concatenate([density, velocity, bfield], axis=0)
    channels, ct, npc, nr = combined.shape
    theta_count = lax.axis_size("theta")
    phi_count = lax.axis_size("phi")
    t = lax.axis_index("theta")
    p = lax.axis_index("phi")
    at_north = t == 0
    at_south = t == theta_count - 1
    cycle_len = npc * phi_count
    parity = jnp.array(PARITY, jnp.float32)
    poles = (0, theta_count - 1)
    both = ("theta", "phi")

    def pole_pairs(shift):
        return [
            (a * phi_count + b, a * phi_count + (b + shift) % phi_count)
            for a in poles
            for b in range(phi_count)
        ]

    north_side = t <= 1
    helper = (t == 1) | (t == theta_count - 2)
    half = channels * CAP // 2
    first_half = jnp.concatenate([density, velocity[:2]], axis=0)
    second_half = jnp.concatenate([velocity[2:], bfield], axis=0)

    def cap_of(fields):
        rows = jnp.where(at_north, fields[:, :CAP], fields[:, ct - CAP :])
        return jnp.swapaxes(rows, 0, 1).reshape(half, npc, nr)

    pairs_out = [(0, 1), (theta_count - 1, theta_count - 2)]
    pairs_in = [(1, 0), (theta_count - 2, theta_count - 1)]
    handed = lax.ppermute(cap_of(second_half), "theta", pairs_out)
    work = jnp.where(helper, handed, cap_of(first_half))
    per_device = half // phi_count
    cycle = lax.all_to_all(work, "phi", split_axis=0, concat_axis=1, tiled=True)
    analysis = fourier_rows(jnp.arange(cycle_len, dtype=jnp.int32), cycle_len)
    dst_cols = (
        jnp.arange(phi_count, dtype=jnp.int32)[:, None] * npc
        - 1
        + jnp.arange(npc + 3, dtype=jnp.int32)[None, :]
    ) % cycle_len
    synthesis = fourier_rows(dst_cols, cycle_len)

    pole_pick = jnp.where(north_side, 0, 1).astype(jnp.int32)
    level_row = lax.dynamic_index_in_dim(levels, pole_pick, 0, keepdims=False)
    slot_ids = p * per_device + jnp.arange(per_device, dtype=jnp.int32)
    row_ids = slot_ids // (channels // 2)
    slot_levels = jnp.sum(
        jnp.where(
            row_ids[:, None] == jnp.arange(CAP, dtype=jnp.int32)[None, :], level_row[None, :], 0
        ),
        axis=1,
    )
    limits = jnp.right_shift(jnp.int32(KMAX), slot_levels)
    column_order = jnp.arange(2 * KMAX, dtype=jnp.int32) % KMAX
    column_weight = jnp.where(column_order == 0, 1.0 / cycle_len, 2.0 / cycle_len).astype(
        jnp.float32
    )
    kept_weight = jnp.where(column_order[None, :] < limits[:, None], column_weight[None, :], 0.0)
    coeffs = jnp.einsum("smr,mn->snr", cycle, analysis, precision=lax.Precision.HIGHEST)
    coeffs = coeffs * kept_weight[:, :, None]
    out = jnp.einsum("snr,kjn->ksjr", coeffs, synthesis, precision=lax.Precision.HIGHEST)
    out = out.reshape(phi_count * per_device, npc + 3, nr)
    low_halo = lax.ppermute(
        combined[:, ct - 1], "theta", [(i, i + 1) for i in range(theta_count - 1)]
    )
    up_send = jnp.concatenate([combined[:, 0], combined[6:7, 1]], axis=0)
    up_halo = lax.ppermute(up_send, "theta", [(i + 1, i) for i in range(theta_count - 1)])
    rows_ext = jnp.concatenate(
        [
            low_halo[:, None],
            combined,
            up_halo[:channels, None],
            jnp.broadcast_to(up_halo[channels:], (channels, npc, nr))[:, None],
        ],
        axis=1,
    )
    left_cols = lax.ppermute(
        rows_ext[:, :, npc - 1 :], "phi", [(i, (i + 1) % phi_count) for i in range(phi_count)]
    )
    right_cols = lax.ppermute(
        rows_ext[:, :, :2], "phi", [((i + 1) % phi_count, i) for i in range(phi_count)]
    )
    early = jnp.concatenate([left_cols, rows_ext, right_cols], axis=2)

    mine = lax.all_to_all(out, "phi", split_axis=0, concat_axis=0, tiled=True)

    from_helper = lax.ppermute(mine, "theta", pairs_in)
    per_half = channels // 2
    cap_rows = jnp.concatenate([mine, from_helper], axis=0).reshape(2, CAP, per_half, npc + 3, nr)
    cap_rows = jnp.transpose(cap_rows, (0, 2, 1, 3, 4)).reshape(channels, CAP, npc + 3, nr)
    first_rows = mine[:per_half]
    last_rows = mine[(CAP - 1) * per_half :]
    spare_at = (CAP - 2) * per_half + 6 - per_half
    spare = mine[spare_at : spare_at + 1]
    ghost_send = jnp.concatenate([jnp.where(north_side, first_rows, last_rows), spare], axis=0)
    turn = phi_count // 2
    pole_ghost = lax.ppermute(
        ghost_send,
        both,
        [(a * phi_count + b, a * phi_count + (b + turn) % phi_count) for a in poles for b in range(phi_count)],
    )
    helper_ghost = lax.ppermute(
        ghost_send,
        both,
        [
            (h * phi_count + b, a * phi_count + (b + turn) % phi_count)
            for h, a in ((1, 0), (theta_count - 2, theta_count - 1))
            for b in range(phi_count)
        ],
    )
    cap_start = jnp.where(at_north, 1, ct - CAP + 1)
    kept_cap = lax.dynamic_slice_in_dim(early, cap_start, CAP, axis=1)
    cap_block = jnp.where(at_north | at_south, cap_rows, kept_cap)
    with_caps = lax.dynamic_update_slice_in_dim(early, cap_block, cap_start, axis=1)

    near_rows = 2
    rest_rows = ct - near_rows

    def rows_from(x, first, count):
        return advance(lax.dynamic_slice_in_dim(x, first, count + 3, axis=1))

    rest = rows_from(with_caps, jnp.where(at_north, near_rows, 0), rest_rows)
    (pole_ghost, helper_ghost), rest = lax.optimization_barrier(((pole_ghost, helper_ghost), rest))
    ghost_main = jnp.concatenate([pole_ghost[:per_half], helper_ghost[:per_half]], axis=0)
    ghost_main = ghost_main * parity[:, None, None]
    ghost_b = helper_ghost[per_half:] * parity[6]
    north_block = jnp.concatenate(
        [ghost_main[:, None], cap_rows, early[:, CAP + 1 : CAP + 2]], axis=1
    )
    south_block = jnp.concatenate(
        [
            cap_rows,
            ghost_main[:, None],
            jnp.broadcast_to(ghost_b, (channels, npc + 3, nr))[:, None],
        ],
        axis=1,
    )
    offset = jnp.where(at_north, 0, ct - CAP + 1)
    kept_block = lax.dynamic_slice_in_dim(early, offset, CAP + 2, axis=1)
    block = jnp.where(at_north, north_block, jnp.where(at_south, south_block, kept_block))
    extended = lax.dynamic_update_slice_in_dim(early, block, offset, axis=1)

    near = rows_from(extended, jnp.where(at_north, 0, rest_rows), near_rows)
    outs = []
    for a, c in zip(rest, near):
        north_order = jnp.concatenate([c, a], axis=1)
        other_order = jnp.concatenate([a, c], axis=1)
        outs.append(jnp.where(at_north, north_order, other_order))
    return tuple(outs)


def solution(mesh):
    return jax.shard_map(
        local,
        mesh=mesh,
        in_specs=(
            P(None, "theta", "phi", None),
            P(None, "theta", "phi", None),
            P(None, "theta", "phi", None),
            P(),
        ),
        out_specs=(P(None, "theta", "phi", None), P(None, "theta", "phi", None)),
        check_vma=False,
    )
```

```python
import math

import jax
import jax.numpy as jnp
from jax import lax
from jax.sharding import PartitionSpec as P

CAP = 4
KMAX = 128


TIME_STEP = 0.2
PARITY = (1.0, 1.0, 1.0, -1.0, -1.0, 1.0, -1.0, -1.0)


def up_r(a):
    return jnp.concatenate([a[..., 1:], a[..., -1:]], axis=-1)


def down_r(a):
    return jnp.concatenate([a[..., :1], a[..., :-1]], axis=-1)


def face_flux(left_amount, right_amount, left_speed, right_speed):
    return 0.5 * (left_amount * left_speed + right_amount * right_speed) - 0.5 * jnp.maximum(
        jnp.abs(left_speed), jnp.abs(right_speed)
    ) * (right_amount - left_amount)


def corner4(e00, e01, e10, e11):
    return 0.25 * (((e00 + e01) + e10) + e11)


def advance(x):
    ct = x.shape[1] - 3
    npc = x.shape[2] - 3
    densities = []
    for channel in range(2):
        q = x[channel]
        v_t = x[3]
        v_p = x[4]
        v_r = x[2]
        fl_t = face_flux(
            q[0 : ct + 1, 1 : npc + 1], q[1 : ct + 2, 1 : npc + 1],
            v_t[0 : ct + 1, 1 : npc + 1], v_t[1 : ct + 2, 1 : npc + 1],
        )
        fl_p = face_flux(
            q[1 : ct + 1, 0 : npc + 1], q[1 : ct + 1, 1 : npc + 2],
            v_p[1 : ct + 1, 0 : npc + 1], v_p[1 : ct + 1, 1 : npc + 2],
        )
        qi = q[1 : ct + 1, 1 : npc + 1]
        vi = v_r[1 : ct + 1, 1 : npc + 1]
        fl_lo = face_flux(down_r(qi), qi, down_r(vi), vi)
        fl_hi = face_flux(qi, up_r(qi), vi, up_r(vi))
        tendency = (fl_t[1:] - fl_t[:-1]) + (fl_p[:, 1:] - fl_p[:, :-1]) + (fl_hi - fl_lo)
        densities.append(qi - TIME_STEP * tendency)

    wr = slice(0, ct + 2)
    wc = slice(0, npc + 2)
    b_r = x[5][wr, wc]
    b_t = x[6]
    b_p = x[7]
    c_r = 0.5 * (b_r + up_r(b_r))
    c_t = 0.5 * (b_t[0 : ct + 2, wc] + b_t[1 : ct + 3, wc])
    c_p = 0.5 * (b_p[wr, 0 : npc + 2] + b_p[wr, 1 : npc + 3])
    s_r = x[2][wr, wc]
    s_t = x[3][wr, wc]
    s_p = x[4][wr, wc]
    emf_r = -(s_t * c_p - s_p * c_t)
    emf_t = -(s_p * c_r - s_r * c_p)
    emf_p = -(s_r * c_t - s_t * c_r)
    lane = lax.broadcasted_iota(jnp.int32, emf_t.shape, 2)
    last = emf_t.shape[2] - 1
    edge_t = -(s_p * b_r - s_r * c_p)
    edge_p = -(s_r * c_t - s_t * b_r)
    t_lo = jnp.where(lane == 0, edge_t, down_r(emf_t))
    t_hi = jnp.where(lane == last, edge_t, up_r(emf_t))
    p_lo = jnp.where(lane == 0, edge_p, down_r(emf_p))
    p_hi = jnp.where(lane == last, edge_p, up_r(emf_p))

    rows_a = slice(0, ct + 1)
    rows_b = slice(1, ct + 2)
    cols_in = slice(1, npc + 1)
    ep_lo = corner4(p_lo[rows_a, cols_in], emf_p[rows_a, cols_in], p_lo[rows_b, cols_in], emf_p[rows_b, cols_in])
    ep_hi = corner4(emf_p[rows_a, cols_in], p_hi[rows_a, cols_in], emf_p[rows_b, cols_in], p_hi[rows_b, cols_in])
    rows_in = slice(1, ct + 1)
    cols_a = slice(0, npc + 1)
    cols_b = slice(1, npc + 2)
    et_lo = corner4(t_lo[rows_in, cols_a], emf_t[rows_in, cols_a], t_lo[rows_in, cols_b], emf_t[rows_in, cols_b])
    et_hi = corner4(emf_t[rows_in, cols_a], t_hi[rows_in, cols_a], emf_t[rows_in, cols_b], t_hi[rows_in, cols_b])
    er = corner4(emf_r[rows_a, cols_a], emf_r[rows_a, cols_b], emf_r[rows_b, cols_a], emf_r[rows_b, cols_b])

    inner = (slice(1, ct + 1), slice(1, npc + 1))
    new_radial = x[5][inner] - TIME_STEP * (
        (ep_lo[1:] - ep_lo[:-1]) - (et_lo[:, 1:] - et_lo[:, :-1])
    )
    new_theta = x[6][inner] - TIME_STEP * (
        (er[:-1, 1:] - er[:-1, :-1]) - (ep_hi[:-1] - ep_lo[:-1])
    )
    new_phi = x[7][inner] - TIME_STEP * (
        (et_hi[:, :-1] - et_lo[:, :-1]) - (er[1:, :-1] - er[:-1, :-1])
    )
    return jnp.stack(densities), jnp.stack([new_radial, new_theta, new_phi])


def fourier_rows(cols, cycle_len):
    orders = jnp.arange(KMAX, dtype=jnp.int32)
    phase = (cols[..., None] * orders) % cycle_len
    angle = phase.astype(jnp.float32) * (2.0 * math.pi / cycle_len)
    return jnp.concatenate([jnp.cos(angle), jnp.sin(angle)], axis=-1)


def local(density, velocity, bfield, levels):
    combined = jnp.concatenate([density, velocity, bfield], axis=0)
    channels, ct, npc, nr = combined.shape
    theta_count = lax.axis_size("theta")
    phi_count = lax.axis_size("phi")
    t = lax.axis_index("theta")
    p = lax.axis_index("phi")
    at_north = t == 0
    at_south = t == theta_count - 1
    cycle_len = npc * phi_count
    parity = jnp.array(PARITY, jnp.float32)
    poles = (0, theta_count - 1)
    both = ("theta", "phi")

    def pole_pairs(shift):
        return [
            (a * phi_count + b, a * phi_count + (b + shift) % phi_count)
            for a in poles
            for b in range(phi_count)
        ]

    north_side = t <= 1
    helper = (t == 1) | (t == theta_count - 2)
    half = channels * CAP // 2
    first_half = jnp.concatenate([density, velocity[:2]], axis=0)
    second_half = jnp.concatenate([velocity[2:], bfield], axis=0)

    def cap_of(fields):
        rows = jnp.where(at_north, fields[:, :CAP], fields[:, ct - CAP :])
        return jnp.swapaxes(rows, 0, 1).reshape(half, npc, nr)

    pairs_out = [(0, 1), (theta_count - 1, theta_count - 2)]
    pairs_in = [(1, 0), (theta_count - 2, theta_count - 1)]
    handed = lax.ppermute(cap_of(second_half), "theta", pairs_out)
    work = jnp.where(helper, handed, cap_of(first_half))
    per_device = half // phi_count
    cycle = lax.all_to_all(work, "phi", split_axis=0, concat_axis=1, tiled=True)
    analysis = fourier_rows(jnp.arange(cycle_len, dtype=jnp.int32), cycle_len)
    dst_cols = (
        jnp.arange(phi_count, dtype=jnp.int32)[:, None] * npc
        - 1
        + jnp.arange(npc + 3, dtype=jnp.int32)[None, :]
    ) % cycle_len
    synthesis = fourier_rows(dst_cols, cycle_len)

    pole_pick = jnp.where(north_side, 0, 1).astype(jnp.int32)
    level_row = lax.dynamic_index_in_dim(levels, pole_pick, 0, keepdims=False)
    slot_ids = p * per_device + jnp.arange(per_device, dtype=jnp.int32)
    row_ids = slot_ids // (channels // 2)
    slot_levels = jnp.sum(
        jnp.where(
            row_ids[:, None] == jnp.arange(CAP, dtype=jnp.int32)[None, :], level_row[None, :], 0
        ),
        axis=1,
    )
    limits = jnp.right_shift(jnp.int32(KMAX), slot_levels)
    column_order = jnp.arange(2 * KMAX, dtype=jnp.int32) % KMAX
    column_weight = jnp.where(column_order == 0, 1.0 / cycle_len, 2.0 / cycle_len).astype(
        jnp.float32
    )
    kept_weight = jnp.where(column_order[None, :] < limits[:, None], column_weight[None, :], 0.0)
    coeffs = jnp.einsum("smr,mn->snr", cycle, analysis, precision=lax.Precision.HIGHEST)
    coeffs = coeffs * kept_weight[:, :, None]
    out = jnp.einsum("snr,kjn->ksjr", coeffs, synthesis, precision=lax.Precision.HIGHEST)
    out = out.reshape(phi_count * per_device, npc + 3, nr)
    low_halo = lax.ppermute(
        combined[:, ct - 1], "theta", [(i, i + 1) for i in range(theta_count - 1)]
    )
    up_send = jnp.concatenate([combined[:, 0], combined[6:7, 1]], axis=0)
    up_halo = lax.ppermute(up_send, "theta", [(i + 1, i) for i in range(theta_count - 1)])
    rows_ext = jnp.concatenate(
        [
            low_halo[:, None],
            combined,
            up_halo[:channels, None],
            jnp.broadcast_to(up_halo[channels:], (channels, npc, nr))[:, None],
        ],
        axis=1,
    )
    left_cols = lax.ppermute(
        rows_ext[:, :, npc - 1 :], "phi", [(i, (i + 1) % phi_count) for i in range(phi_count)]
    )
    right_cols = lax.ppermute(
        rows_ext[:, :, :2], "phi", [((i + 1) % phi_count, i) for i in range(phi_count)]
    )
    early = jnp.concatenate([left_cols, rows_ext, right_cols], axis=2)

    mine = lax.all_to_all(out, "phi", split_axis=0, concat_axis=0, tiled=True)
    mine, early = lax.optimization_barrier((mine, early))

    from_helper = lax.ppermute(mine, "theta", pairs_in)
    per_half = channels // 2
    cap_rows = jnp.concatenate([mine, from_helper], axis=0).reshape(2, CAP, per_half, npc + 3, nr)
    cap_rows = jnp.transpose(cap_rows, (0, 2, 1, 3, 4)).reshape(channels, CAP, npc + 3, nr)
    first_rows = mine[:per_half]
    last_rows = mine[(CAP - 1) * per_half :]
    spare_at = (CAP - 2) * per_half + 6 - per_half
    spare = mine[spare_at : spare_at + 1]
    ghost_send = jnp.concatenate([jnp.where(north_side, first_rows, last_rows), spare], axis=0)
    turn = phi_count // 2
    pole_ghost = lax.ppermute(
        ghost_send,
        both,
        [(a * phi_count + b, a * phi_count + (b + turn) % phi_count) for a in poles for b in range(phi_count)],
    )
    helper_ghost = lax.ppermute(
        ghost_send,
        both,
        [
            (h * phi_count + b, a * phi_count + (b + turn) % phi_count)
            for h, a in ((1, 0), (theta_count - 2, theta_count - 1))
            for b in range(phi_count)
        ],
    )
    cap_start = jnp.where(at_north, 1, ct - CAP + 1)
    kept_cap = lax.dynamic_slice_in_dim(early, cap_start, CAP, axis=1)
    cap_block = jnp.where(at_north | at_south, cap_rows, kept_cap)
    with_caps = lax.dynamic_update_slice_in_dim(early, cap_block, cap_start, axis=1)

    near_rows = 2
    rest_rows = ct - near_rows

    def rows_from(x, first, count):
        return advance(lax.dynamic_slice_in_dim(x, first, count + 3, axis=1))

    rest = rows_from(with_caps, jnp.where(at_north, near_rows, 0), rest_rows)
    (pole_ghost, helper_ghost), rest = lax.optimization_barrier(((pole_ghost, helper_ghost), rest))
    ghost_main = jnp.concatenate([pole_ghost[:per_half], helper_ghost[:per_half]], axis=0)
    ghost_main = ghost_main * parity[:, None, None]
    ghost_b = helper_ghost[per_half:] * parity[6]
    north_block = jnp.concatenate(
        [ghost_main[:, None], cap_rows, early[:, CAP + 1 : CAP + 2]], axis=1
    )
    south_block = jnp.concatenate(
        [
            cap_rows,
            ghost_main[:, None],
            jnp.broadcast_to(ghost_b, (channels, npc + 3, nr))[:, None],
        ],
        axis=1,
    )
    offset = jnp.where(at_north, 0, ct - CAP + 1)
    kept_block = lax.dynamic_slice_in_dim(early, offset, CAP + 2, axis=1)
    block = jnp.where(at_north, north_block, jnp.where(at_south, south_block, kept_block))
    extended = lax.dynamic_update_slice_in_dim(early, block, offset, axis=1)

    near = rows_from(extended, jnp.where(at_north, 0, rest_rows), near_rows)
    outs = []
    for a, c in zip(rest, near):
        north_order = jnp.concatenate([c, a], axis=1)
        other_order = jnp.concatenate([a, c], axis=1)
        outs.append(jnp.where(at_north, north_order, other_order))
    return tuple(outs)


def solution(mesh):
    return jax.shard_map(
        local,
        mesh=mesh,
        in_specs=(
            P(None, "theta", "phi", None),
            P(None, "theta", "phi", None),
            P(None, "theta", "phi", None),
            P(),
        ),
        out_specs=(P(None, "theta", "phi", None), P(None, "theta", "phi", None)),
        check_vma=False,
    )
```

```python
import math

import jax
import jax.numpy as jnp
from jax import lax
from jax.sharding import PartitionSpec as P

CAP = 4
KMAX = 128


TIME_STEP = 0.2
PARITY = (1.0, 1.0, 1.0, -1.0, -1.0, 1.0, -1.0, -1.0)


def up_r(a):
    return jnp.concatenate([a[..., 1:], a[..., -1:]], axis=-1)


def down_r(a):
    return jnp.concatenate([a[..., :1], a[..., :-1]], axis=-1)


def face_flux(left_amount, right_amount, left_speed, right_speed):
    return 0.5 * (left_amount * left_speed + right_amount * right_speed) - 0.5 * jnp.maximum(
        jnp.abs(left_speed), jnp.abs(right_speed)
    ) * (right_amount - left_amount)


def corner4(e00, e01, e10, e11):
    return 0.25 * (((e00 + e01) + e10) + e11)


def advance(x):
    ct = x.shape[1] - 3
    npc = x.shape[2] - 3
    densities = []
    for channel in range(2):
        q = x[channel]
        v_t = x[3]
        v_p = x[4]
        v_r = x[2]
        fl_t = face_flux(
            q[0 : ct + 1, 1 : npc + 1], q[1 : ct + 2, 1 : npc + 1],
            v_t[0 : ct + 1, 1 : npc + 1], v_t[1 : ct + 2, 1 : npc + 1],
        )
        fl_p = face_flux(
            q[1 : ct + 1, 0 : npc + 1], q[1 : ct + 1, 1 : npc + 2],
            v_p[1 : ct + 1, 0 : npc + 1], v_p[1 : ct + 1, 1 : npc + 2],
        )
        qi = q[1 : ct + 1, 1 : npc + 1]
        vi = v_r[1 : ct + 1, 1 : npc + 1]
        fl_lo = face_flux(down_r(qi), qi, down_r(vi), vi)
        fl_hi = face_flux(qi, up_r(qi), vi, up_r(vi))
        tendency = (fl_t[1:] - fl_t[:-1]) + (fl_p[:, 1:] - fl_p[:, :-1]) + (fl_hi - fl_lo)
        densities.append(qi - TIME_STEP * tendency)

    wr = slice(0, ct + 2)
    wc = slice(0, npc + 2)
    b_r = x[5][wr, wc]
    b_t = x[6]
    b_p = x[7]
    c_r = 0.5 * (b_r + up_r(b_r))
    c_t = 0.5 * (b_t[0 : ct + 2, wc] + b_t[1 : ct + 3, wc])
    c_p = 0.5 * (b_p[wr, 0 : npc + 2] + b_p[wr, 1 : npc + 3])
    s_r = x[2][wr, wc]
    s_t = x[3][wr, wc]
    s_p = x[4][wr, wc]
    emf_r = -(s_t * c_p - s_p * c_t)
    emf_t = -(s_p * c_r - s_r * c_p)
    emf_p = -(s_r * c_t - s_t * c_r)
    lane = lax.broadcasted_iota(jnp.int32, emf_t.shape, 2)
    last = emf_t.shape[2] - 1
    edge_t = -(s_p * b_r - s_r * c_p)
    edge_p = -(s_r * c_t - s_t * b_r)
    t_lo = jnp.where(lane == 0, edge_t, down_r(emf_t))
    t_hi = jnp.where(lane == last, edge_t, up_r(emf_t))
    p_lo = jnp.where(lane == 0, edge_p, down_r(emf_p))
    p_hi = jnp.where(lane == last, edge_p, up_r(emf_p))

    rows_a = slice(0, ct + 1)
    rows_b = slice(1, ct + 2)
    cols_in = slice(1, npc + 1)
    ep_lo = corner4(p_lo[rows_a, cols_in], emf_p[rows_a, cols_in], p_lo[rows_b, cols_in], emf_p[rows_b, cols_in])
    ep_hi = corner4(emf_p[rows_a, cols_in], p_hi[rows_a, cols_in], emf_p[rows_b, cols_in], p_hi[rows_b, cols_in])
    rows_in = slice(1, ct + 1)
    cols_a = slice(0, npc + 1)
    cols_b = slice(1, npc + 2)
    et_lo = corner4(t_lo[rows_in, cols_a], emf_t[rows_in, cols_a], t_lo[rows_in, cols_b], emf_t[rows_in, cols_b])
    et_hi = corner4(emf_t[rows_in, cols_a], t_hi[rows_in, cols_a], emf_t[rows_in, cols_b], t_hi[rows_in, cols_b])
    er = corner4(emf_r[rows_a, cols_a], emf_r[rows_a, cols_b], emf_r[rows_b, cols_a], emf_r[rows_b, cols_b])

    inner = (slice(1, ct + 1), slice(1, npc + 1))
    new_radial = x[5][inner] - TIME_STEP * (
        (ep_lo[1:] - ep_lo[:-1]) - (et_lo[:, 1:] - et_lo[:, :-1])
    )
    new_theta = x[6][inner] - TIME_STEP * (
        (er[:-1, 1:] - er[:-1, :-1]) - (ep_hi[:-1] - ep_lo[:-1])
    )
    new_phi = x[7][inner] - TIME_STEP * (
        (et_hi[:, :-1] - et_lo[:, :-1]) - (er[1:, :-1] - er[:-1, :-1])
    )
    return jnp.stack(densities), jnp.stack([new_radial, new_theta, new_phi])


def fourier_rows(cols, cycle_len):
    orders = jnp.arange(KMAX, dtype=jnp.int32)
    phase = (cols[..., None] * orders) % cycle_len
    angle = phase.astype(jnp.float32) * (2.0 * math.pi / cycle_len)
    return jnp.concatenate([jnp.cos(angle), jnp.sin(angle)], axis=-1)


def local(density, velocity, bfield, levels):
    combined = jnp.concatenate([density, velocity, bfield], axis=0)
    channels, ct, npc, nr = combined.shape
    theta_count = lax.axis_size("theta")
    phi_count = lax.axis_size("phi")
    t = lax.axis_index("theta")
    p = lax.axis_index("phi")
    at_north = t == 0
    at_south = t == theta_count - 1
    cycle_len = npc * phi_count
    parity = jnp.array(PARITY, jnp.float32)
    poles = (0, theta_count - 1)
    both = ("theta", "phi")

    def pole_pairs(shift):
        return [
            (a * phi_count + b, a * phi_count + (b + shift) % phi_count)
            for a in poles
            for b in range(phi_count)
        ]

    north_side = t <= 1
    helper = (t == 1) | (t == theta_count - 2)
    half = channels * CAP // 2
    first_half = jnp.concatenate([density, velocity[:2]], axis=0)
    second_half = jnp.concatenate([velocity[2:], bfield], axis=0)

    def cap_of(fields):
        rows = jnp.where(at_north, fields[:, :CAP], fields[:, ct - CAP :])
        return jnp.swapaxes(rows, 0, 1).reshape(half, npc, nr)

    pairs_out = [(0, 1), (theta_count - 1, theta_count - 2)]
    pairs_in = [(1, 0), (theta_count - 2, theta_count - 1)]
    handed = lax.ppermute(cap_of(second_half), "theta", pairs_out)
    work = jnp.where(helper, handed, cap_of(first_half))
    per_device = half // phi_count
    cycle = lax.all_to_all(work, "phi", split_axis=0, concat_axis=1, tiled=True)
    low_halo = lax.ppermute(
        combined[:, ct - 1], "theta", [(i, i + 1) for i in range(theta_count - 1)]
    )
    up_send = jnp.concatenate([combined[:, 0], combined[6:7, 1]], axis=0)
    up_halo = lax.ppermute(up_send, "theta", [(i + 1, i) for i in range(theta_count - 1)])
    rows_ext = jnp.concatenate(
        [
            low_halo[:, None],
            combined,
            up_halo[:channels, None],
            jnp.broadcast_to(up_halo[channels:], (channels, npc, nr))[:, None],
        ],
        axis=1,
    )
    left_cols = lax.ppermute(
        rows_ext[:, :, npc - 1 :], "phi", [(i, (i + 1) % phi_count) for i in range(phi_count)]
    )
    right_cols = lax.ppermute(
        rows_ext[:, :, :2], "phi", [((i + 1) % phi_count, i) for i in range(phi_count)]
    )
    early = jnp.concatenate([left_cols, rows_ext, right_cols], axis=2)

    cycle, early = lax.optimization_barrier((cycle, early))
    analysis = fourier_rows(jnp.arange(cycle_len, dtype=jnp.int32), cycle_len)
    dst_cols = (
        jnp.arange(phi_count, dtype=jnp.int32)[:, None] * npc
        - 1
        + jnp.arange(npc + 3, dtype=jnp.int32)[None, :]
    ) % cycle_len
    synthesis = fourier_rows(dst_cols, cycle_len)

    pole_pick = jnp.where(north_side, 0, 1).astype(jnp.int32)
    level_row = lax.dynamic_index_in_dim(levels, pole_pick, 0, keepdims=False)
    slot_ids = p * per_device + jnp.arange(per_device, dtype=jnp.int32)
    row_ids = slot_ids // (channels // 2)
    slot_levels = jnp.sum(
        jnp.where(
            row_ids[:, None] == jnp.arange(CAP, dtype=jnp.int32)[None, :], level_row[None, :], 0
        ),
        axis=1,
    )
    limits = jnp.right_shift(jnp.int32(KMAX), slot_levels)
    column_order = jnp.arange(2 * KMAX, dtype=jnp.int32) % KMAX
    column_weight = jnp.where(column_order == 0, 1.0 / cycle_len, 2.0 / cycle_len).astype(
        jnp.float32
    )
    kept_weight = jnp.where(column_order[None, :] < limits[:, None], column_weight[None, :], 0.0)
    coeffs = jnp.einsum("smr,mn->snr", cycle, analysis, precision=lax.Precision.HIGHEST)
    coeffs = coeffs * kept_weight[:, :, None]
    out = jnp.einsum("snr,kjn->ksjr", coeffs, synthesis, precision=lax.Precision.HIGHEST)
    out = out.reshape(phi_count * per_device, npc + 3, nr)
    mine = lax.all_to_all(out, "phi", split_axis=0, concat_axis=0, tiled=True)

    from_helper = lax.ppermute(mine, "theta", pairs_in)
    per_half = channels // 2
    cap_rows = jnp.concatenate([mine, from_helper], axis=0).reshape(2, CAP, per_half, npc + 3, nr)
    cap_rows = jnp.transpose(cap_rows, (0, 2, 1, 3, 4)).reshape(channels, CAP, npc + 3, nr)
    first_rows = mine[:per_half]
    last_rows = mine[(CAP - 1) * per_half :]
    spare_at = (CAP - 2) * per_half + 6 - per_half
    spare = mine[spare_at : spare_at + 1]
    ghost_send = jnp.concatenate([jnp.where(north_side, first_rows, last_rows), spare], axis=0)
    turn = phi_count // 2
    pole_ghost = lax.ppermute(
        ghost_send,
        both,
        [(a * phi_count + b, a * phi_count + (b + turn) % phi_count) for a in poles for b in range(phi_count)],
    )
    helper_ghost = lax.ppermute(
        ghost_send,
        both,
        [
            (h * phi_count + b, a * phi_count + (b + turn) % phi_count)
            for h, a in ((1, 0), (theta_count - 2, theta_count - 1))
            for b in range(phi_count)
        ],
    )
    cap_start = jnp.where(at_north, 1, ct - CAP + 1)
    kept_cap = lax.dynamic_slice_in_dim(early, cap_start, CAP, axis=1)
    cap_block = jnp.where(at_north | at_south, cap_rows, kept_cap)
    with_caps = lax.dynamic_update_slice_in_dim(early, cap_block, cap_start, axis=1)

    near_rows = 2
    rest_rows = ct - near_rows

    def rows_from(x, first, count):
        return advance(lax.dynamic_slice_in_dim(x, first, count + 3, axis=1))

    rest = rows_from(with_caps, jnp.where(at_north, near_rows, 0), rest_rows)
    (pole_ghost, helper_ghost), rest = lax.optimization_barrier(((pole_ghost, helper_ghost), rest))
    ghost_main = jnp.concatenate([pole_ghost[:per_half], helper_ghost[:per_half]], axis=0)
    ghost_main = ghost_main * parity[:, None, None]
    ghost_b = helper_ghost[per_half:] * parity[6]
    north_block = jnp.concatenate(
        [ghost_main[:, None], cap_rows, early[:, CAP + 1 : CAP + 2]], axis=1
    )
    south_block = jnp.concatenate(
        [
            cap_rows,
            ghost_main[:, None],
            jnp.broadcast_to(ghost_b, (channels, npc + 3, nr))[:, None],
        ],
        axis=1,
    )
    offset = jnp.where(at_north, 0, ct - CAP + 1)
    kept_block = lax.dynamic_slice_in_dim(early, offset, CAP + 2, axis=1)
    block = jnp.where(at_north, north_block, jnp.where(at_south, south_block, kept_block))
    extended = lax.dynamic_update_slice_in_dim(early, block, offset, axis=1)

    near = rows_from(extended, jnp.where(at_north, 0, rest_rows), near_rows)
    outs = []
    for a, c in zip(rest, near):
        north_order = jnp.concatenate([c, a], axis=1)
        other_order = jnp.concatenate([a, c], axis=1)
        outs.append(jnp.where(at_north, north_order, other_order))
    return tuple(outs)


def solution(mesh):
    return jax.shard_map(
        local,
        mesh=mesh,
        in_specs=(
            P(None, "theta", "phi", None),
            P(None, "theta", "phi", None),
            P(None, "theta", "phi", None),
            P(),
        ),
        out_specs=(P(None, "theta", "phi", None), P(None, "theta", "phi", None)),
        check_vma=False,
    )
```

```python
import math

import jax
import jax.numpy as jnp
from jax import lax
from jax.sharding import PartitionSpec as P

CAP = 4
KMAX = 128


TIME_STEP = 0.2
PARITY = (1.0, 1.0, 1.0, -1.0, -1.0, 1.0, -1.0, -1.0)


def up_r(a):
    return jnp.concatenate([a[..., 1:], a[..., -1:]], axis=-1)


def down_r(a):
    return jnp.concatenate([a[..., :1], a[..., :-1]], axis=-1)


def face_flux(left_amount, right_amount, left_speed, right_speed):
    return 0.5 * (left_amount * left_speed + right_amount * right_speed) - 0.5 * jnp.maximum(
        jnp.abs(left_speed), jnp.abs(right_speed)
    ) * (right_amount - left_amount)


def corner4(e00, e01, e10, e11):
    return 0.25 * (((e00 + e01) + e10) + e11)


def advance(x):
    ct = x.shape[1] - 3
    npc = x.shape[2] - 3
    densities = []
    for channel in range(2):
        q = x[channel]
        v_t = x[3]
        v_p = x[4]
        v_r = x[2]
        fl_t = face_flux(
            q[0 : ct + 1, 1 : npc + 1], q[1 : ct + 2, 1 : npc + 1],
            v_t[0 : ct + 1, 1 : npc + 1], v_t[1 : ct + 2, 1 : npc + 1],
        )
        fl_p = face_flux(
            q[1 : ct + 1, 0 : npc + 1], q[1 : ct + 1, 1 : npc + 2],
            v_p[1 : ct + 1, 0 : npc + 1], v_p[1 : ct + 1, 1 : npc + 2],
        )
        qi = q[1 : ct + 1, 1 : npc + 1]
        vi = v_r[1 : ct + 1, 1 : npc + 1]
        fl_lo = face_flux(down_r(qi), qi, down_r(vi), vi)
        fl_hi = face_flux(qi, up_r(qi), vi, up_r(vi))
        tendency = (fl_t[1:] - fl_t[:-1]) + (fl_p[:, 1:] - fl_p[:, :-1]) + (fl_hi - fl_lo)
        densities.append(qi - TIME_STEP * tendency)

    wr = slice(0, ct + 2)
    wc = slice(0, npc + 2)
    b_r = x[5][wr, wc]
    b_t = x[6]
    b_p = x[7]
    c_r = 0.5 * (b_r + up_r(b_r))
    c_t = 0.5 * (b_t[0 : ct + 2, wc] + b_t[1 : ct + 3, wc])
    c_p = 0.5 * (b_p[wr, 0 : npc + 2] + b_p[wr, 1 : npc + 3])
    s_r = x[2][wr, wc]
    s_t = x[3][wr, wc]
    s_p = x[4][wr, wc]
    emf_r = -(s_t * c_p - s_p * c_t)
    emf_t = -(s_p * c_r - s_r * c_p)
    emf_p = -(s_r * c_t - s_t * c_r)
    lane = lax.broadcasted_iota(jnp.int32, emf_t.shape, 2)
    last = emf_t.shape[2] - 1
    edge_t = -(s_p * b_r - s_r * c_p)
    edge_p = -(s_r * c_t - s_t * b_r)
    t_lo = jnp.where(lane == 0, edge_t, down_r(emf_t))
    t_hi = jnp.where(lane == last, edge_t, up_r(emf_t))
    p_lo = jnp.where(lane == 0, edge_p, down_r(emf_p))
    p_hi = jnp.where(lane == last, edge_p, up_r(emf_p))

    rows_a = slice(0, ct + 1)
    rows_b = slice(1, ct + 2)
    cols_in = slice(1, npc + 1)
    ep_lo = corner4(p_lo[rows_a, cols_in], emf_p[rows_a, cols_in], p_lo[rows_b, cols_in], emf_p[rows_b, cols_in])
    ep_hi = corner4(emf_p[rows_a, cols_in], p_hi[rows_a, cols_in], emf_p[rows_b, cols_in], p_hi[rows_b, cols_in])
    rows_in = slice(1, ct + 1)
    cols_a = slice(0, npc + 1)
    cols_b = slice(1, npc + 2)
    et_lo = corner4(t_lo[rows_in, cols_a], emf_t[rows_in, cols_a], t_lo[rows_in, cols_b], emf_t[rows_in, cols_b])
    et_hi = corner4(emf_t[rows_in, cols_a], t_hi[rows_in, cols_a], emf_t[rows_in, cols_b], t_hi[rows_in, cols_b])
    er = corner4(emf_r[rows_a, cols_a], emf_r[rows_a, cols_b], emf_r[rows_b, cols_a], emf_r[rows_b, cols_b])

    inner = (slice(1, ct + 1), slice(1, npc + 1))
    new_radial = x[5][inner] - TIME_STEP * (
        (ep_lo[1:] - ep_lo[:-1]) - (et_lo[:, 1:] - et_lo[:, :-1])
    )
    new_theta = x[6][inner] - TIME_STEP * (
        (er[:-1, 1:] - er[:-1, :-1]) - (ep_hi[:-1] - ep_lo[:-1])
    )
    new_phi = x[7][inner] - TIME_STEP * (
        (et_hi[:, :-1] - et_lo[:, :-1]) - (er[1:, :-1] - er[:-1, :-1])
    )
    return jnp.stack(densities), jnp.stack([new_radial, new_theta, new_phi])


def fourier_rows(cols, cycle_len):
    orders = jnp.arange(KMAX, dtype=jnp.int32)
    phase = (cols[..., None] * orders) % cycle_len
    angle = phase.astype(jnp.float32) * (2.0 * math.pi / cycle_len)
    return jnp.concatenate([jnp.cos(angle), jnp.sin(angle)], axis=-1)


def local(density, velocity, bfield, levels):
    combined = jnp.concatenate([density, velocity, bfield], axis=0)
    channels, ct, npc, nr = combined.shape
    theta_count = lax.axis_size("theta")
    phi_count = lax.axis_size("phi")
    t = lax.axis_index("theta")
    p = lax.axis_index("phi")
    at_north = t == 0
    at_south = t == theta_count - 1
    cycle_len = npc * phi_count
    parity = jnp.array(PARITY, jnp.float32)
    poles = (0, theta_count - 1)
    both = ("theta", "phi")

    def pole_pairs(shift):
        return [
            (a * phi_count + b, a * phi_count + (b + shift) % phi_count)
            for a in poles
            for b in range(phi_count)
        ]

    low_halo = lax.ppermute(
        combined[:, ct - 1], "theta", [(i, i + 1) for i in range(theta_count - 1)]
    )
    up_send = jnp.concatenate([combined[:, 0], combined[6:7, 1]], axis=0)
    up_halo = lax.ppermute(up_send, "theta", [(i + 1, i) for i in range(theta_count - 1)])
    rows_ext = jnp.concatenate(
        [
            low_halo[:, None],
            combined,
            up_halo[:channels, None],
            jnp.broadcast_to(up_halo[channels:], (channels, npc, nr))[:, None],
        ],
        axis=1,
    )
    left_cols = lax.ppermute(
        rows_ext[:, :, npc - 1 :], "phi", [(i, (i + 1) % phi_count) for i in range(phi_count)]
    )
    right_cols = lax.ppermute(
        rows_ext[:, :, :2], "phi", [((i + 1) % phi_count, i) for i in range(phi_count)]
    )
    early = jnp.concatenate([left_cols, rows_ext, right_cols], axis=2)

    north_side = t <= 1
    helper = (t == 1) | (t == theta_count - 2)
    half = channels * CAP // 2
    first_half = jnp.concatenate([density, velocity[:2]], axis=0)
    second_half = jnp.concatenate([velocity[2:], bfield], axis=0)

    def cap_of(fields):
        rows = jnp.where(at_north, fields[:, :CAP], fields[:, ct - CAP :])
        return jnp.swapaxes(rows, 0, 1).reshape(half, npc, nr)

    pairs_out = [(0, 1), (theta_count - 1, theta_count - 2)]
    pairs_in = [(1, 0), (theta_count - 2, theta_count - 1)]
    handed = lax.ppermute(cap_of(second_half), "theta", pairs_out)
    work = jnp.where(helper, handed, cap_of(first_half))
    per_device = half // phi_count
    cycle = lax.all_to_all(work, "phi", split_axis=0, concat_axis=1, tiled=True)
    analysis = fourier_rows(jnp.arange(cycle_len, dtype=jnp.int32), cycle_len)
    dst_cols = (
        jnp.arange(phi_count, dtype=jnp.int32)[:, None] * npc
        - 1
        + jnp.arange(npc + 3, dtype=jnp.int32)[None, :]
    ) % cycle_len
    synthesis = fourier_rows(dst_cols, cycle_len)

    pole_pick = jnp.where(north_side, 0, 1).astype(jnp.int32)
    level_row = lax.dynamic_index_in_dim(levels, pole_pick, 0, keepdims=False)
    slot_ids = p * per_device + jnp.arange(per_device, dtype=jnp.int32)
    row_ids = slot_ids // (channels // 2)
    slot_levels = jnp.sum(
        jnp.where(
            row_ids[:, None] == jnp.arange(CAP, dtype=jnp.int32)[None, :], level_row[None, :], 0
        ),
        axis=1,
    )
    limits = jnp.right_shift(jnp.int32(KMAX), slot_levels)
    column_order = jnp.arange(2 * KMAX, dtype=jnp.int32) % KMAX
    column_weight = jnp.where(column_order == 0, 1.0 / cycle_len, 2.0 / cycle_len).astype(
        jnp.float32
    )
    kept_weight = jnp.where(column_order[None, :] < limits[:, None], column_weight[None, :], 0.0)
    coeffs = jnp.einsum("smr,mn->snr", cycle, analysis, precision=lax.Precision.HIGH)
    coeffs = coeffs * kept_weight[:, :, None]
    out = jnp.einsum("snr,kjn->ksjr", coeffs, synthesis, precision=lax.Precision.HIGH)
    out = out.reshape(phi_count * per_device, npc + 3, nr)
    mine = lax.all_to_all(out, "phi", split_axis=0, concat_axis=0, tiled=True)

    from_helper = lax.ppermute(mine, "theta", pairs_in)
    per_half = channels // 2
    cap_rows = jnp.concatenate([mine, from_helper], axis=0).reshape(2, CAP, per_half, npc + 3, nr)
    cap_rows = jnp.transpose(cap_rows, (0, 2, 1, 3, 4)).reshape(channels, CAP, npc + 3, nr)
    first_rows = mine[:per_half]
    last_rows = mine[(CAP - 1) * per_half :]
    spare_at = (CAP - 2) * per_half + 6 - per_half
    spare = mine[spare_at : spare_at + 1]
    ghost_send = jnp.concatenate([jnp.where(north_side, first_rows, last_rows), spare], axis=0)
    turn = phi_count // 2
    pole_ghost = lax.ppermute(
        ghost_send,
        both,
        [(a * phi_count + b, a * phi_count + (b + turn) % phi_count) for a in poles for b in range(phi_count)],
    )
    helper_ghost = lax.ppermute(
        ghost_send,
        both,
        [
            (h * phi_count + b, a * phi_count + (b + turn) % phi_count)
            for h, a in ((1, 0), (theta_count - 2, theta_count - 1))
            for b in range(phi_count)
        ],
    )
    ghost_main = jnp.concatenate([pole_ghost[:per_half], helper_ghost[:per_half]], axis=0)
    ghost_main = ghost_main * parity[:, None, None]
    ghost_b = helper_ghost[per_half:] * parity[6]
    north_block = jnp.concatenate(
        [ghost_main[:, None], cap_rows, early[:, CAP + 1 : CAP + 2]], axis=1
    )
    south_block = jnp.concatenate(
        [
            cap_rows,
            ghost_main[:, None],
            jnp.broadcast_to(ghost_b, (channels, npc + 3, nr))[:, None],
        ],
        axis=1,
    )
    offset = jnp.where(at_north, 0, ct - CAP + 1)
    kept_block = lax.dynamic_slice_in_dim(early, offset, CAP + 2, axis=1)
    block = jnp.where(
        at_north, north_block, jnp.where(at_south, south_block, kept_block)
    )
    extended = lax.dynamic_update_slice_in_dim(early, block, offset, axis=1)
    return advance(extended)


def solution(mesh):
    return jax.shard_map(
        local,
        mesh=mesh,
        in_specs=(
            P(None, "theta", "phi", None),
            P(None, "theta", "phi", None),
            P(None, "theta", "phi", None),
            P(),
        ),
        out_specs=(P(None, "theta", "phi", None), P(None, "theta", "phi", None)),
        check_vma=False,
    )
```

```python
import math

import jax
import jax.numpy as jnp
from jax import lax
from jax.sharding import PartitionSpec as P

CAP = 4
KMAX = 128


TIME_STEP = 0.2
PARITY = (1.0, 1.0, 1.0, -1.0, -1.0, 1.0, -1.0, -1.0)


def up_r(a):
    return jnp.concatenate([a[..., 1:], a[..., -1:]], axis=-1)


def down_r(a):
    return jnp.concatenate([a[..., :1], a[..., :-1]], axis=-1)


def face_flux(left_amount, right_amount, left_speed, right_speed):
    return 0.5 * (left_amount * left_speed + right_amount * right_speed) - 0.5 * jnp.maximum(
        jnp.abs(left_speed), jnp.abs(right_speed)
    ) * (right_amount - left_amount)


def corner4(e00, e01, e10, e11):
    return 0.25 * (((e00 + e01) + e10) + e11)


def advance(x):
    ct = x.shape[1] - 3
    npc = x.shape[2] - 3
    densities = []
    for channel in range(2):
        q = x[channel]
        v_t = x[3]
        v_p = x[4]
        v_r = x[2]
        fl_t = face_flux(
            q[0 : ct + 1, 1 : npc + 1], q[1 : ct + 2, 1 : npc + 1],
            v_t[0 : ct + 1, 1 : npc + 1], v_t[1 : ct + 2, 1 : npc + 1],
        )
        fl_p = face_flux(
            q[1 : ct + 1, 0 : npc + 1], q[1 : ct + 1, 1 : npc + 2],
            v_p[1 : ct + 1, 0 : npc + 1], v_p[1 : ct + 1, 1 : npc + 2],
        )
        qi = q[1 : ct + 1, 1 : npc + 1]
        vi = v_r[1 : ct + 1, 1 : npc + 1]
        fl_lo = face_flux(down_r(qi), qi, down_r(vi), vi)
        fl_hi = face_flux(qi, up_r(qi), vi, up_r(vi))
        tendency = (fl_t[1:] - fl_t[:-1]) + (fl_p[:, 1:] - fl_p[:, :-1]) + (fl_hi - fl_lo)
        densities.append(qi - TIME_STEP * tendency)

    wr = slice(0, ct + 2)
    wc = slice(0, npc + 2)
    b_r = x[5][wr, wc]
    b_t = x[6]
    b_p = x[7]
    c_r = 0.5 * (b_r + up_r(b_r))
    c_t = 0.5 * (b_t[0 : ct + 2, wc] + b_t[1 : ct + 3, wc])
    c_p = 0.5 * (b_p[wr, 0 : npc + 2] + b_p[wr, 1 : npc + 3])
    s_r = x[2][wr, wc]
    s_t = x[3][wr, wc]
    s_p = x[4][wr, wc]
    emf_r = -(s_t * c_p - s_p * c_t)
    emf_t = -(s_p * c_r - s_r * c_p)
    emf_p = -(s_r * c_t - s_t * c_r)
    lane = lax.broadcasted_iota(jnp.int32, emf_t.shape, 2)
    last = emf_t.shape[2] - 1
    edge_t = -(s_p * b_r - s_r * c_p)
    edge_p = -(s_r * c_t - s_t * b_r)
    t_lo = jnp.where(lane == 0, edge_t, down_r(emf_t))
    t_hi = jnp.where(lane == last, edge_t, up_r(emf_t))
    p_lo = jnp.where(lane == 0, edge_p, down_r(emf_p))
    p_hi = jnp.where(lane == last, edge_p, up_r(emf_p))

    rows_a = slice(0, ct + 1)
    rows_b = slice(1, ct + 2)
    cols_in = slice(1, npc + 1)
    ep_lo = corner4(p_lo[rows_a, cols_in], emf_p[rows_a, cols_in], p_lo[rows_b, cols_in], emf_p[rows_b, cols_in])
    ep_hi = corner4(emf_p[rows_a, cols_in], p_hi[rows_a, cols_in], emf_p[rows_b, cols_in], p_hi[rows_b, cols_in])
    rows_in = slice(1, ct + 1)
    cols_a = slice(0, npc + 1)
    cols_b = slice(1, npc + 2)
    et_lo = corner4(t_lo[rows_in, cols_a], emf_t[rows_in, cols_a], t_lo[rows_in, cols_b], emf_t[rows_in, cols_b])
    et_hi = corner4(emf_t[rows_in, cols_a], t_hi[rows_in, cols_a], emf_t[rows_in, cols_b], t_hi[rows_in, cols_b])
    er = corner4(emf_r[rows_a, cols_a], emf_r[rows_a, cols_b], emf_r[rows_b, cols_a], emf_r[rows_b, cols_b])

    inner = (slice(1, ct + 1), slice(1, npc + 1))
    new_radial = x[5][inner] - TIME_STEP * (
        (ep_lo[1:] - ep_lo[:-1]) - (et_lo[:, 1:] - et_lo[:, :-1])
    )
    new_theta = x[6][inner] - TIME_STEP * (
        (er[:-1, 1:] - er[:-1, :-1]) - (ep_hi[:-1] - ep_lo[:-1])
    )
    new_phi = x[7][inner] - TIME_STEP * (
        (et_hi[:, :-1] - et_lo[:, :-1]) - (er[1:, :-1] - er[:-1, :-1])
    )
    return jnp.stack(densities), jnp.stack([new_radial, new_theta, new_phi])


def fourier_rows(cols, cycle_len):
    orders = jnp.arange(KMAX, dtype=jnp.int32)
    phase = (cols[..., None] * orders) % cycle_len
    angle = phase.astype(jnp.float32) * (2.0 * math.pi / cycle_len)
    return jnp.concatenate([jnp.cos(angle), jnp.sin(angle)], axis=-1)


def local(density, velocity, bfield, levels):
    combined = jnp.concatenate([density, velocity, bfield], axis=0)
    channels, ct, npc, nr = combined.shape
    theta_count = lax.axis_size("theta")
    phi_count = lax.axis_size("phi")
    t = lax.axis_index("theta")
    p = lax.axis_index("phi")
    at_north = t == 0
    at_south = t == theta_count - 1
    cycle_len = npc * phi_count
    parity = jnp.array(PARITY, jnp.float32)
    poles = (0, theta_count - 1)
    both = ("theta", "phi")

    def pole_pairs(shift):
        return [
            (a * phi_count + b, a * phi_count + (b + shift) % phi_count)
            for a in poles
            for b in range(phi_count)
        ]

    north_side = t <= 1
    helper = (t == 1) | (t == theta_count - 2)
    half = channels * CAP // 2
    first_half = jnp.concatenate([density, velocity[:2]], axis=0)
    second_half = jnp.concatenate([velocity[2:], bfield], axis=0)

    def cap_of(fields):
        rows = jnp.where(at_north, fields[:, :CAP], fields[:, ct - CAP :])
        return jnp.swapaxes(rows, 0, 1).reshape(half, npc, nr)

    pairs_out = [(0, 1), (theta_count - 1, theta_count - 2)]
    pairs_in = [(1, 0), (theta_count - 2, theta_count - 1)]
    handed = lax.ppermute(cap_of(second_half), "theta", pairs_out)
    work = jnp.where(helper, handed, cap_of(first_half))
    per_device = half // phi_count
    cycle = lax.all_to_all(work, "phi", split_axis=0, concat_axis=1, tiled=True)
    analysis = fourier_rows(jnp.arange(cycle_len, dtype=jnp.int32), cycle_len)
    dst_cols = (
        jnp.arange(phi_count, dtype=jnp.int32)[:, None] * npc
        - 1
        + jnp.arange(npc + 3, dtype=jnp.int32)[None, :]
    ) % cycle_len
    synthesis = fourier_rows(dst_cols, cycle_len)

    pole_pick = jnp.where(north_side, 0, 1).astype(jnp.int32)
    level_row = lax.dynamic_index_in_dim(levels, pole_pick, 0, keepdims=False)
    slot_ids = p * per_device + jnp.arange(per_device, dtype=jnp.int32)
    row_ids = slot_ids // (channels // 2)
    slot_levels = jnp.sum(
        jnp.where(
            row_ids[:, None] == jnp.arange(CAP, dtype=jnp.int32)[None, :], level_row[None, :], 0
        ),
        axis=1,
    )
    limits = jnp.right_shift(jnp.int32(KMAX), slot_levels)
    column_order = jnp.arange(2 * KMAX, dtype=jnp.int32) % KMAX
    column_weight = jnp.where(column_order == 0, 1.0 / cycle_len, 2.0 / cycle_len).astype(
        jnp.float32
    )
    kept_weight = jnp.where(column_order[None, :] < limits[:, None], column_weight[None, :], 0.0)
    coeffs = jnp.einsum("smr,mn->snr", cycle, analysis, precision=lax.Precision.HIGH)
    coeffs = coeffs * kept_weight[:, :, None]
    out = jnp.einsum("snr,kjn->ksjr", coeffs, synthesis, precision=lax.Precision.HIGH)
    out = out.reshape(phi_count * per_device, npc + 3, nr)
    mine = lax.all_to_all(out, "phi", split_axis=0, concat_axis=0, tiled=True)
    mine, halo_src = lax.optimization_barrier((mine, combined))
    low_halo = lax.ppermute(
        halo_src[:, ct - 1], "theta", [(i, i + 1) for i in range(theta_count - 1)]
    )
    up_send = jnp.concatenate([halo_src[:, 0], halo_src[6:7, 1]], axis=0)
    up_halo = lax.ppermute(up_send, "theta", [(i + 1, i) for i in range(theta_count - 1)])
    rows_ext = jnp.concatenate(
        [
            low_halo[:, None],
            combined,
            up_halo[:channels, None],
            jnp.broadcast_to(up_halo[channels:], (channels, npc, nr))[:, None],
        ],
        axis=1,
    )
    left_cols = lax.ppermute(
        rows_ext[:, :, npc - 1 :], "phi", [(i, (i + 1) % phi_count) for i in range(phi_count)]
    )
    right_cols = lax.ppermute(
        rows_ext[:, :, :2], "phi", [((i + 1) % phi_count, i) for i in range(phi_count)]
    )
    early = jnp.concatenate([left_cols, rows_ext, right_cols], axis=2)


    from_helper = lax.ppermute(mine, "theta", pairs_in)
    per_half = channels // 2
    cap_rows = jnp.concatenate([mine, from_helper], axis=0).reshape(2, CAP, per_half, npc + 3, nr)
    cap_rows = jnp.transpose(cap_rows, (0, 2, 1, 3, 4)).reshape(channels, CAP, npc + 3, nr)
    first_rows = mine[:per_half]
    last_rows = mine[(CAP - 1) * per_half :]
    spare_at = (CAP - 2) * per_half + 6 - per_half
    spare = mine[spare_at : spare_at + 1]
    ghost_send = jnp.concatenate([jnp.where(north_side, first_rows, last_rows), spare], axis=0)
    turn = phi_count // 2
    pole_ghost = lax.ppermute(
        ghost_send,
        both,
        [(a * phi_count + b, a * phi_count + (b + turn) % phi_count) for a in poles for b in range(phi_count)],
    )
    helper_ghost = lax.ppermute(
        ghost_send,
        both,
        [
            (h * phi_count + b, a * phi_count + (b + turn) % phi_count)
            for h, a in ((1, 0), (theta_count - 2, theta_count - 1))
            for b in range(phi_count)
        ],
    )
    ghost_main = jnp.concatenate([pole_ghost[:per_half], helper_ghost[:per_half]], axis=0)
    ghost_main = ghost_main * parity[:, None, None]
    ghost_b = helper_ghost[per_half:] * parity[6]
    north_block = jnp.concatenate(
        [ghost_main[:, None], cap_rows, early[:, CAP + 1 : CAP + 2]], axis=1
    )
    south_block = jnp.concatenate(
        [
            cap_rows,
            ghost_main[:, None],
            jnp.broadcast_to(ghost_b, (channels, npc + 3, nr))[:, None],
        ],
        axis=1,
    )
    offset = jnp.where(at_north, 0, ct - CAP + 1)
    kept_block = lax.dynamic_slice_in_dim(early, offset, CAP + 2, axis=1)
    block = jnp.where(
        at_north, north_block, jnp.where(at_south, south_block, kept_block)
    )
    extended = lax.dynamic_update_slice_in_dim(early, block, offset, axis=1)
    return advance(extended)


def solution(mesh):
    return jax.shard_map(
        local,
        mesh=mesh,
        in_specs=(
            P(None, "theta", "phi", None),
            P(None, "theta", "phi", None),
            P(None, "theta", "phi", None),
            P(),
        ),
        out_specs=(P(None, "theta", "phi", None), P(None, "theta", "phi", None)),
        check_vma=False,
    )
```

```python
import math

import jax
import jax.numpy as jnp
from jax import lax
from jax.sharding import PartitionSpec as P

CAP = 4
KMAX = 128


TIME_STEP = 0.2
PARITY = (1.0, 1.0, 1.0, -1.0, -1.0, 1.0, -1.0, -1.0)


def up_r(a):
    return jnp.concatenate([a[..., 1:], a[..., -1:]], axis=-1)


def down_r(a):
    return jnp.concatenate([a[..., :1], a[..., :-1]], axis=-1)


def face_flux(left_amount, right_amount, left_speed, right_speed):
    return 0.5 * (left_amount * left_speed + right_amount * right_speed) - 0.5 * jnp.maximum(
        jnp.abs(left_speed), jnp.abs(right_speed)
    ) * (right_amount - left_amount)


def corner4(e00, e01, e10, e11):
    return 0.25 * (((e00 + e01) + e10) + e11)


def advance(x):
    ct = x.shape[1] - 3
    npc = x.shape[2] - 3
    densities = []
    for channel in range(2):
        q = x[channel]
        v_t = x[3]
        v_p = x[4]
        v_r = x[2]
        fl_t = face_flux(
            q[0 : ct + 1, 1 : npc + 1], q[1 : ct + 2, 1 : npc + 1],
            v_t[0 : ct + 1, 1 : npc + 1], v_t[1 : ct + 2, 1 : npc + 1],
        )
        fl_p = face_flux(
            q[1 : ct + 1, 0 : npc + 1], q[1 : ct + 1, 1 : npc + 2],
            v_p[1 : ct + 1, 0 : npc + 1], v_p[1 : ct + 1, 1 : npc + 2],
        )
        qi = q[1 : ct + 1, 1 : npc + 1]
        vi = v_r[1 : ct + 1, 1 : npc + 1]
        fl_lo = face_flux(down_r(qi), qi, down_r(vi), vi)
        fl_hi = face_flux(qi, up_r(qi), vi, up_r(vi))
        tendency = (fl_t[1:] - fl_t[:-1]) + (fl_p[:, 1:] - fl_p[:, :-1]) + (fl_hi - fl_lo)
        densities.append(qi - TIME_STEP * tendency)

    wr = slice(0, ct + 2)
    wc = slice(0, npc + 2)
    b_r = x[5][wr, wc]
    b_t = x[6]
    b_p = x[7]
    c_r = 0.5 * (b_r + up_r(b_r))
    c_t = 0.5 * (b_t[0 : ct + 2, wc] + b_t[1 : ct + 3, wc])
    c_p = 0.5 * (b_p[wr, 0 : npc + 2] + b_p[wr, 1 : npc + 3])
    s_r = x[2][wr, wc]
    s_t = x[3][wr, wc]
    s_p = x[4][wr, wc]
    emf_r = -(s_t * c_p - s_p * c_t)
    emf_t = -(s_p * c_r - s_r * c_p)
    emf_p = -(s_r * c_t - s_t * c_r)
    lane = lax.broadcasted_iota(jnp.int32, emf_t.shape, 2)
    last = emf_t.shape[2] - 1
    edge_t = -(s_p * b_r - s_r * c_p)
    edge_p = -(s_r * c_t - s_t * b_r)
    t_lo = jnp.where(lane == 0, edge_t, down_r(emf_t))
    t_hi = jnp.where(lane == last, edge_t, up_r(emf_t))
    p_lo = jnp.where(lane == 0, edge_p, down_r(emf_p))
    p_hi = jnp.where(lane == last, edge_p, up_r(emf_p))

    rows_a = slice(0, ct + 1)
    rows_b = slice(1, ct + 2)
    cols_in = slice(1, npc + 1)
    ep_lo = corner4(p_lo[rows_a, cols_in], emf_p[rows_a, cols_in], p_lo[rows_b, cols_in], emf_p[rows_b, cols_in])
    ep_hi = corner4(emf_p[rows_a, cols_in], p_hi[rows_a, cols_in], emf_p[rows_b, cols_in], p_hi[rows_b, cols_in])
    rows_in = slice(1, ct + 1)
    cols_a = slice(0, npc + 1)
    cols_b = slice(1, npc + 2)
    et_lo = corner4(t_lo[rows_in, cols_a], emf_t[rows_in, cols_a], t_lo[rows_in, cols_b], emf_t[rows_in, cols_b])
    et_hi = corner4(emf_t[rows_in, cols_a], t_hi[rows_in, cols_a], emf_t[rows_in, cols_b], t_hi[rows_in, cols_b])
    er = corner4(emf_r[rows_a, cols_a], emf_r[rows_a, cols_b], emf_r[rows_b, cols_a], emf_r[rows_b, cols_b])

    inner = (slice(1, ct + 1), slice(1, npc + 1))
    new_radial = x[5][inner] - TIME_STEP * (
        (ep_lo[1:] - ep_lo[:-1]) - (et_lo[:, 1:] - et_lo[:, :-1])
    )
    new_theta = x[6][inner] - TIME_STEP * (
        (er[:-1, 1:] - er[:-1, :-1]) - (ep_hi[:-1] - ep_lo[:-1])
    )
    new_phi = x[7][inner] - TIME_STEP * (
        (et_hi[:, :-1] - et_lo[:, :-1]) - (er[1:, :-1] - er[:-1, :-1])
    )
    return jnp.stack(densities), jnp.stack([new_radial, new_theta, new_phi])


def fourier_rows(cols, cycle_len):
    orders = jnp.arange(KMAX, dtype=jnp.int32)
    phase = (cols[..., None] * orders) % cycle_len
    angle = phase.astype(jnp.float32) * (2.0 * math.pi / cycle_len)
    return jnp.concatenate([jnp.cos(angle), jnp.sin(angle)], axis=-1)


def local(density, velocity, bfield, levels):
    combined = jnp.concatenate([density, velocity, bfield], axis=0)
    channels, ct, npc, nr = combined.shape
    theta_count = lax.axis_size("theta")
    phi_count = lax.axis_size("phi")
    t = lax.axis_index("theta")
    p = lax.axis_index("phi")
    at_north = t == 0
    at_south = t == theta_count - 1
    cycle_len = npc * phi_count
    parity = jnp.array(PARITY, jnp.float32)
    poles = (0, theta_count - 1)
    both = ("theta", "phi")

    def pole_pairs(shift):
        return [
            (a * phi_count + b, a * phi_count + (b + shift) % phi_count)
            for a in poles
            for b in range(phi_count)
        ]

    low_halo = lax.ppermute(
        combined[:, ct - 1], "theta", [(i, i + 1) for i in range(theta_count - 1)]
    )
    up_send = jnp.concatenate([combined[:, 0], combined[6:7, 1]], axis=0)
    up_halo = lax.ppermute(up_send, "theta", [(i + 1, i) for i in range(theta_count - 1)])
    rows_ext = jnp.concatenate(
        [
            low_halo[:, None],
            combined,
            up_halo[:channels, None],
            jnp.broadcast_to(up_halo[channels:], (channels, npc, nr))[:, None],
        ],
        axis=1,
    )
    left_cols = lax.ppermute(
        rows_ext[:, :, npc - 1 :], "phi", [(i, (i + 1) % phi_count) for i in range(phi_count)]
    )
    right_cols = lax.ppermute(
        rows_ext[:, :, :2], "phi", [((i + 1) % phi_count, i) for i in range(phi_count)]
    )
    early = jnp.concatenate([left_cols, rows_ext, right_cols], axis=2)

    north_side = t <= 1
    helper = (t == 1) | (t == theta_count - 2)
    half = channels * CAP // 2
    pair_rows = CAP // 2

    def rows_at(first):
        parts = [lax.dynamic_slice_in_dim(f, first, pair_rows, axis=1) for f in (density, velocity, bfield)]
        rows = jnp.concatenate(parts, axis=0)
        return jnp.swapaxes(rows, 0, 1).reshape(half, npc, nr)

    keep_first = jnp.where(at_north, 0, ct - pair_rows)
    hand_first = jnp.where(at_north, pair_rows, ct - CAP)
    pairs_out = [(0, 1), (theta_count - 1, theta_count - 2)]
    pairs_in = [(1, 0), (theta_count - 2, theta_count - 1)]
    handed = lax.ppermute(rows_at(hand_first), "theta", pairs_out)
    work = jnp.where(helper, handed, rows_at(keep_first))
    per_device = half // phi_count
    cycle = lax.all_to_all(work, "phi", split_axis=0, concat_axis=1, tiled=True)
    analysis = fourier_rows(jnp.arange(cycle_len, dtype=jnp.int32), cycle_len)
    dst_cols = (
        jnp.arange(phi_count, dtype=jnp.int32)[:, None] * npc
        - 1
        + jnp.arange(npc + 3, dtype=jnp.int32)[None, :]
    ) % cycle_len
    synthesis = fourier_rows(dst_cols, cycle_len)

    pole_pick = jnp.where(north_side, 0, 1).astype(jnp.int32)
    level_row = lax.dynamic_index_in_dim(levels, pole_pick, 0, keepdims=False)
    slot_ids = p * per_device + jnp.arange(per_device, dtype=jnp.int32)
    row_base = jnp.where(north_side == helper, pair_rows, 0)
    row_ids = row_base + slot_ids // channels
    slot_levels = jnp.sum(
        jnp.where(
            row_ids[:, None] == jnp.arange(CAP, dtype=jnp.int32)[None, :], level_row[None, :], 0
        ),
        axis=1,
    )
    limits = jnp.right_shift(jnp.int32(KMAX), slot_levels)
    column_order = jnp.arange(2 * KMAX, dtype=jnp.int32) % KMAX
    column_weight = jnp.where(column_order == 0, 1.0 / cycle_len, 2.0 / cycle_len).astype(
        jnp.float32
    )
    kept_weight = jnp.where(column_order[None, :] < limits[:, None], column_weight[None, :], 0.0)
    coeffs = jnp.einsum("smr,mn->snr", cycle, analysis, precision=lax.Precision.HIGH)
    coeffs = coeffs * kept_weight[:, :, None]
    out = jnp.einsum("snr,kjn->ksjr", coeffs, synthesis, precision=lax.Precision.HIGH)
    out = out.reshape(phi_count * per_device, npc + 3, nr)
    mine = lax.all_to_all(out, "phi", split_axis=0, concat_axis=0, tiled=True)

    from_helper = lax.ppermute(mine, "theta", pairs_in)
    spare = mine[6 : 7]
    ghost_send = jnp.where(
        north_side,
        jnp.concatenate([mine[:channels], spare], axis=0),
        jnp.concatenate([mine[channels:], spare], axis=0),
    )
    turn = phi_count // 2
    ghost = lax.ppermute(
        ghost_send,
        both,
        [(a * phi_count + b, a * phi_count + (b + turn) % phi_count) for a in poles for b in range(phi_count)],
    )
    in_order = jnp.where(
        at_north,
        jnp.concatenate([mine, from_helper], axis=0),
        jnp.concatenate([from_helper, mine], axis=0),
    )
    cap_rows = jnp.swapaxes(in_order.reshape(CAP, channels, npc + 3, nr), 0, 1)
    ghost_main = ghost[:channels]
    ghost_b = ghost[channels:]
    ghost_main = ghost_main * parity[:, None, None]
    ghost_b = ghost_b * parity[6]
    north_block = jnp.concatenate(
        [ghost_main[:, None], cap_rows, early[:, CAP + 1 : CAP + 2]], axis=1
    )
    south_block = jnp.concatenate(
        [
            cap_rows,
            ghost_main[:, None],
            jnp.broadcast_to(ghost_b, (channels, npc + 3, nr))[:, None],
        ],
        axis=1,
    )
    offset = jnp.where(at_north, 0, ct - CAP + 1)
    kept_block = lax.dynamic_slice_in_dim(early, offset, CAP + 2, axis=1)
    block = jnp.where(
        at_north, north_block, jnp.where(at_south, south_block, kept_block)
    )
    extended = lax.dynamic_update_slice_in_dim(early, block, offset, axis=1)
    return advance(extended)


def solution(mesh):
    return jax.shard_map(
        local,
        mesh=mesh,
        in_specs=(
            P(None, "theta", "phi", None),
            P(None, "theta", "phi", None),
            P(None, "theta", "phi", None),
            P(),
        ),
        out_specs=(P(None, "theta", "phi", None), P(None, "theta", "phi", None)),
        check_vma=False,
    )
```

```python
import math

import jax
import jax.numpy as jnp
from jax import lax
from jax.sharding import PartitionSpec as P

CAP = 4
KMAX = 128


TIME_STEP = 0.2
PARITY = (1.0, 1.0, 1.0, -1.0, -1.0, 1.0, -1.0, -1.0)


def up_r(a):
    return jnp.concatenate([a[..., 1:], a[..., -1:]], axis=-1)


def down_r(a):
    return jnp.concatenate([a[..., :1], a[..., :-1]], axis=-1)


def face_flux(left_amount, right_amount, left_speed, right_speed):
    return 0.5 * (left_amount * left_speed + right_amount * right_speed) - 0.5 * jnp.maximum(
        jnp.abs(left_speed), jnp.abs(right_speed)
    ) * (right_amount - left_amount)


def corner4(e00, e01, e10, e11):
    return 0.25 * (((e00 + e01) + e10) + e11)


def advance(x):
    ct = x.shape[1] - 3
    npc = x.shape[2] - 3
    densities = []
    for channel in range(2):
        q = x[channel]
        v_t = x[3]
        v_p = x[4]
        v_r = x[2]
        fl_t = face_flux(
            q[0 : ct + 1, 1 : npc + 1], q[1 : ct + 2, 1 : npc + 1],
            v_t[0 : ct + 1, 1 : npc + 1], v_t[1 : ct + 2, 1 : npc + 1],
        )
        fl_p = face_flux(
            q[1 : ct + 1, 0 : npc + 1], q[1 : ct + 1, 1 : npc + 2],
            v_p[1 : ct + 1, 0 : npc + 1], v_p[1 : ct + 1, 1 : npc + 2],
        )
        qi = q[1 : ct + 1, 1 : npc + 1]
        vi = v_r[1 : ct + 1, 1 : npc + 1]
        fl_lo = face_flux(down_r(qi), qi, down_r(vi), vi)
        fl_hi = face_flux(qi, up_r(qi), vi, up_r(vi))
        tendency = (fl_t[1:] - fl_t[:-1]) + (fl_p[:, 1:] - fl_p[:, :-1]) + (fl_hi - fl_lo)
        densities.append(qi - TIME_STEP * tendency)

    wr = slice(0, ct + 2)
    wc = slice(0, npc + 2)
    b_r = x[5][wr, wc]
    b_t = x[6]
    b_p = x[7]
    c_r = 0.5 * (b_r + up_r(b_r))
    c_t = 0.5 * (b_t[0 : ct + 2, wc] + b_t[1 : ct + 3, wc])
    c_p = 0.5 * (b_p[wr, 0 : npc + 2] + b_p[wr, 1 : npc + 3])
    s_r = x[2][wr, wc]
    s_t = x[3][wr, wc]
    s_p = x[4][wr, wc]
    emf_r = -(s_t * c_p - s_p * c_t)
    emf_t = -(s_p * c_r - s_r * c_p)
    emf_p = -(s_r * c_t - s_t * c_r)
    lane = lax.broadcasted_iota(jnp.int32, emf_t.shape, 2)
    last = emf_t.shape[2] - 1
    edge_t = -(s_p * b_r - s_r * c_p)
    edge_p = -(s_r * c_t - s_t * b_r)
    t_lo = jnp.where(lane == 0, edge_t, down_r(emf_t))
    t_hi = jnp.where(lane == last, edge_t, up_r(emf_t))
    p_lo = jnp.where(lane == 0, edge_p, down_r(emf_p))
    p_hi = jnp.where(lane == last, edge_p, up_r(emf_p))

    rows_a = slice(0, ct + 1)
    rows_b = slice(1, ct + 2)
    cols_in = slice(1, npc + 1)
    ep_lo = corner4(p_lo[rows_a, cols_in], emf_p[rows_a, cols_in], p_lo[rows_b, cols_in], emf_p[rows_b, cols_in])
    ep_hi = corner4(emf_p[rows_a, cols_in], p_hi[rows_a, cols_in], emf_p[rows_b, cols_in], p_hi[rows_b, cols_in])
    rows_in = slice(1, ct + 1)
    cols_a = slice(0, npc + 1)
    cols_b = slice(1, npc + 2)
    et_lo = corner4(t_lo[rows_in, cols_a], emf_t[rows_in, cols_a], t_lo[rows_in, cols_b], emf_t[rows_in, cols_b])
    et_hi = corner4(emf_t[rows_in, cols_a], t_hi[rows_in, cols_a], emf_t[rows_in, cols_b], t_hi[rows_in, cols_b])
    er = corner4(emf_r[rows_a, cols_a], emf_r[rows_a, cols_b], emf_r[rows_b, cols_a], emf_r[rows_b, cols_b])

    inner = (slice(1, ct + 1), slice(1, npc + 1))
    new_radial = x[5][inner] - TIME_STEP * (
        (ep_lo[1:] - ep_lo[:-1]) - (et_lo[:, 1:] - et_lo[:, :-1])
    )
    new_theta = x[6][inner] - TIME_STEP * (
        (er[:-1, 1:] - er[:-1, :-1]) - (ep_hi[:-1] - ep_lo[:-1])
    )
    new_phi = x[7][inner] - TIME_STEP * (
        (et_hi[:, :-1] - et_lo[:, :-1]) - (er[1:, :-1] - er[:-1, :-1])
    )
    return jnp.stack(densities), jnp.stack([new_radial, new_theta, new_phi])


def fourier_rows(cols, cycle_len):
    orders = jnp.arange(KMAX, dtype=jnp.int32)
    phase = (cols[..., None] * orders) % cycle_len
    angle = phase.astype(jnp.float32) * (2.0 * math.pi / cycle_len)
    return jnp.concatenate([jnp.cos(angle), jnp.sin(angle)], axis=-1)


def local(density, velocity, bfield, levels):
    combined = jnp.concatenate([density, velocity, bfield], axis=0)
    channels, ct, npc, nr = combined.shape
    theta_count = lax.axis_size("theta")
    phi_count = lax.axis_size("phi")
    t = lax.axis_index("theta")
    p = lax.axis_index("phi")
    at_north = t == 0
    at_south = t == theta_count - 1
    cycle_len = npc * phi_count
    parity = jnp.array(PARITY, jnp.float32)
    poles = (0, theta_count - 1)
    both = ("theta", "phi")

    def pole_pairs(shift):
        return [
            (a * phi_count + b, a * phi_count + (b + shift) % phi_count)
            for a in poles
            for b in range(phi_count)
        ]

    north_side = t <= 1
    helper = (t == 1) | (t == theta_count - 2)
    half = channels * CAP // 2
    pair_rows = CAP // 2

    def rows_at(first):
        parts = [lax.dynamic_slice_in_dim(f, first, pair_rows, axis=1) for f in (density, velocity, bfield)]
        rows = jnp.concatenate(parts, axis=0)
        return jnp.swapaxes(rows, 0, 1).reshape(half, npc, nr)

    keep_first = jnp.where(at_north, 0, ct - pair_rows)
    hand_first = jnp.where(at_north, pair_rows, ct - CAP)
    pairs_out = [(0, 1), (theta_count - 1, theta_count - 2)]
    pairs_in = [(1, 0), (theta_count - 2, theta_count - 1)]
    handed = lax.ppermute(rows_at(hand_first), "theta", pairs_out)
    work = jnp.where(helper, handed, rows_at(keep_first))
    per_device = half // phi_count
    work, halo_src = lax.optimization_barrier((work, combined))
    cycle = lax.all_to_all(work, "phi", split_axis=0, concat_axis=1, tiled=True)
    low_halo = lax.ppermute(
        halo_src[:, ct - 1], "theta", [(i, i + 1) for i in range(theta_count - 1)]
    )
    up_send = jnp.concatenate([halo_src[:, 0], halo_src[6:7, 1]], axis=0)
    up_halo = lax.ppermute(up_send, "theta", [(i + 1, i) for i in range(theta_count - 1)])
    rows_ext = jnp.concatenate(
        [
            low_halo[:, None],
            combined,
            up_halo[:channels, None],
            jnp.broadcast_to(up_halo[channels:], (channels, npc, nr))[:, None],
        ],
        axis=1,
    )
    left_cols = lax.ppermute(
        rows_ext[:, :, npc - 1 :], "phi", [(i, (i + 1) % phi_count) for i in range(phi_count)]
    )
    right_cols = lax.ppermute(
        rows_ext[:, :, :2], "phi", [((i + 1) % phi_count, i) for i in range(phi_count)]
    )
    early = jnp.concatenate([left_cols, rows_ext, right_cols], axis=2)

    cycle, early = lax.optimization_barrier((cycle, early))
    analysis = fourier_rows(jnp.arange(cycle_len, dtype=jnp.int32), cycle_len)
    dst_cols = (
        jnp.arange(phi_count, dtype=jnp.int32)[:, None] * npc
        - 1
        + jnp.arange(npc + 3, dtype=jnp.int32)[None, :]
    ) % cycle_len
    synthesis = fourier_rows(dst_cols, cycle_len)

    pole_pick = jnp.where(north_side, 0, 1).astype(jnp.int32)
    level_row = lax.dynamic_index_in_dim(levels, pole_pick, 0, keepdims=False)
    slot_ids = p * per_device + jnp.arange(per_device, dtype=jnp.int32)
    row_base = jnp.where(north_side == helper, pair_rows, 0)
    row_ids = row_base + slot_ids // channels
    slot_levels = jnp.sum(
        jnp.where(
            row_ids[:, None] == jnp.arange(CAP, dtype=jnp.int32)[None, :], level_row[None, :], 0
        ),
        axis=1,
    )
    limits = jnp.right_shift(jnp.int32(KMAX), slot_levels)
    column_order = jnp.arange(2 * KMAX, dtype=jnp.int32) % KMAX
    column_weight = jnp.where(column_order == 0, 1.0 / cycle_len, 2.0 / cycle_len).astype(
        jnp.float32
    )
    kept_weight = jnp.where(column_order[None, :] < limits[:, None], column_weight[None, :], 0.0)
    coeffs = jnp.einsum("smr,mn->snr", cycle, analysis, precision=lax.Precision.HIGH)
    coeffs = coeffs * kept_weight[:, :, None]
    out = jnp.einsum("snr,kjn->ksjr", coeffs, synthesis, precision=lax.Precision.HIGH)
    out = out.reshape(phi_count * per_device, npc + 3, nr)
    mine = lax.all_to_all(out, "phi", split_axis=0, concat_axis=0, tiled=True)

    from_helper = lax.ppermute(mine, "theta", pairs_in)
    spare = mine[6 : 7]
    ghost_send = jnp.where(
        north_side,
        jnp.concatenate([mine[:channels], spare], axis=0),
        jnp.concatenate([mine[channels:], spare], axis=0),
    )
    turn = phi_count // 2
    ghost = lax.ppermute(
        ghost_send,
        both,
        [(a * phi_count + b, a * phi_count + (b + turn) % phi_count) for a in poles for b in range(phi_count)],
    )
    in_order = jnp.where(
        at_north,
        jnp.concatenate([mine, from_helper], axis=0),
        jnp.concatenate([from_helper, mine], axis=0),
    )
    cap_rows = jnp.swapaxes(in_order.reshape(CAP, channels, npc + 3, nr), 0, 1)
    ghost_main = ghost[:channels]
    ghost_b = ghost[channels:]
    ghost_main = ghost_main * parity[:, None, None]
    ghost_b = ghost_b * parity[6]
    north_block = jnp.concatenate(
        [ghost_main[:, None], cap_rows, early[:, CAP + 1 : CAP + 2]], axis=1
    )
    south_block = jnp.concatenate(
        [
            cap_rows,
            ghost_main[:, None],
            jnp.broadcast_to(ghost_b, (channels, npc + 3, nr))[:, None],
        ],
        axis=1,
    )
    offset = jnp.where(at_north, 0, ct - CAP + 1)
    kept_block = lax.dynamic_slice_in_dim(early, offset, CAP + 2, axis=1)
    block = jnp.where(
        at_north, north_block, jnp.where(at_south, south_block, kept_block)
    )
    extended = lax.dynamic_update_slice_in_dim(early, block, offset, axis=1)
    return advance(extended)


def solution(mesh):
    return jax.shard_map(
        local,
        mesh=mesh,
        in_specs=(
            P(None, "theta", "phi", None),
            P(None, "theta", "phi", None),
            P(None, "theta", "phi", None),
            P(),
        ),
        out_specs=(P(None, "theta", "phi", None), P(None, "theta", "phi", None)),
        check_vma=False,
    )
```

```python
import math

import jax
import jax.numpy as jnp
from jax import lax
from jax.sharding import PartitionSpec as P

CAP = 4
KMAX = 128


TIME_STEP = 0.2
PARITY = (1.0, 1.0, 1.0, -1.0, -1.0, 1.0, -1.0, -1.0)


def up_r(a):
    return jnp.concatenate([a[..., 1:], a[..., -1:]], axis=-1)


def down_r(a):
    return jnp.concatenate([a[..., :1], a[..., :-1]], axis=-1)


def face_flux(left_amount, right_amount, left_speed, right_speed):
    return 0.5 * (left_amount * left_speed + right_amount * right_speed) - 0.5 * jnp.maximum(
        jnp.abs(left_speed), jnp.abs(right_speed)
    ) * (right_amount - left_amount)


def corner4(e00, e01, e10, e11):
    return 0.25 * (((e00 + e01) + e10) + e11)


def advance(x):
    ct = x.shape[1] - 3
    npc = x.shape[2] - 3
    densities = []
    for channel in range(2):
        q = x[channel]
        v_t = x[3]
        v_p = x[4]
        v_r = x[2]
        fl_t = face_flux(
            q[0 : ct + 1, 1 : npc + 1], q[1 : ct + 2, 1 : npc + 1],
            v_t[0 : ct + 1, 1 : npc + 1], v_t[1 : ct + 2, 1 : npc + 1],
        )
        fl_p = face_flux(
            q[1 : ct + 1, 0 : npc + 1], q[1 : ct + 1, 1 : npc + 2],
            v_p[1 : ct + 1, 0 : npc + 1], v_p[1 : ct + 1, 1 : npc + 2],
        )
        qi = q[1 : ct + 1, 1 : npc + 1]
        vi = v_r[1 : ct + 1, 1 : npc + 1]
        fl_lo = face_flux(down_r(qi), qi, down_r(vi), vi)
        fl_hi = face_flux(qi, up_r(qi), vi, up_r(vi))
        tendency = (fl_t[1:] - fl_t[:-1]) + (fl_p[:, 1:] - fl_p[:, :-1]) + (fl_hi - fl_lo)
        densities.append(qi - TIME_STEP * tendency)

    wr = slice(0, ct + 2)
    wc = slice(0, npc + 2)
    b_r = x[5][wr, wc]
    b_t = x[6]
    b_p = x[7]
    c_r = 0.5 * (b_r + up_r(b_r))
    c_t = 0.5 * (b_t[0 : ct + 2, wc] + b_t[1 : ct + 3, wc])
    c_p = 0.5 * (b_p[wr, 0 : npc + 2] + b_p[wr, 1 : npc + 3])
    s_r = x[2][wr, wc]
    s_t = x[3][wr, wc]
    s_p = x[4][wr, wc]
    emf_r = -(s_t * c_p - s_p * c_t)
    emf_t = -(s_p * c_r - s_r * c_p)
    emf_p = -(s_r * c_t - s_t * c_r)
    lane = lax.broadcasted_iota(jnp.int32, emf_t.shape, 2)
    last = emf_t.shape[2] - 1
    edge_t = -(s_p * b_r - s_r * c_p)
    edge_p = -(s_r * c_t - s_t * b_r)
    t_lo = jnp.where(lane == 0, edge_t, down_r(emf_t))
    t_hi = jnp.where(lane == last, edge_t, up_r(emf_t))
    p_lo = jnp.where(lane == 0, edge_p, down_r(emf_p))
    p_hi = jnp.where(lane == last, edge_p, up_r(emf_p))

    rows_a = slice(0, ct + 1)
    rows_b = slice(1, ct + 2)
    cols_in = slice(1, npc + 1)
    ep_lo = corner4(p_lo[rows_a, cols_in], emf_p[rows_a, cols_in], p_lo[rows_b, cols_in], emf_p[rows_b, cols_in])
    ep_hi = corner4(emf_p[rows_a, cols_in], p_hi[rows_a, cols_in], emf_p[rows_b, cols_in], p_hi[rows_b, cols_in])
    rows_in = slice(1, ct + 1)
    cols_a = slice(0, npc + 1)
    cols_b = slice(1, npc + 2)
    et_lo = corner4(t_lo[rows_in, cols_a], emf_t[rows_in, cols_a], t_lo[rows_in, cols_b], emf_t[rows_in, cols_b])
    et_hi = corner4(emf_t[rows_in, cols_a], t_hi[rows_in, cols_a], emf_t[rows_in, cols_b], t_hi[rows_in, cols_b])
    er = corner4(emf_r[rows_a, cols_a], emf_r[rows_a, cols_b], emf_r[rows_b, cols_a], emf_r[rows_b, cols_b])

    inner = (slice(1, ct + 1), slice(1, npc + 1))
    new_radial = x[5][inner] - TIME_STEP * (
        (ep_lo[1:] - ep_lo[:-1]) - (et_lo[:, 1:] - et_lo[:, :-1])
    )
    new_theta = x[6][inner] - TIME_STEP * (
        (er[:-1, 1:] - er[:-1, :-1]) - (ep_hi[:-1] - ep_lo[:-1])
    )
    new_phi = x[7][inner] - TIME_STEP * (
        (et_hi[:, :-1] - et_lo[:, :-1]) - (er[1:, :-1] - er[:-1, :-1])
    )
    return jnp.stack(densities), jnp.stack([new_radial, new_theta, new_phi])


def fourier_rows(cols, cycle_len):
    orders = jnp.arange(KMAX, dtype=jnp.int32)
    phase = (cols[..., None] * orders) % cycle_len
    angle = phase.astype(jnp.float32) * (2.0 * math.pi / cycle_len)
    return jnp.concatenate([jnp.cos(angle), jnp.sin(angle)], axis=-1)


def local(density, velocity, bfield, levels):
    combined = jnp.concatenate([density, velocity, bfield], axis=0)
    channels, ct, npc, nr = combined.shape
    theta_count = lax.axis_size("theta")
    phi_count = lax.axis_size("phi")
    t = lax.axis_index("theta")
    p = lax.axis_index("phi")
    at_north = t == 0
    at_south = t == theta_count - 1
    cycle_len = npc * phi_count
    parity = jnp.array(PARITY, jnp.float32)
    poles = (0, theta_count - 1)
    both = ("theta", "phi")

    def pole_pairs(shift):
        return [
            (a * phi_count + b, a * phi_count + (b + shift) % phi_count)
            for a in poles
            for b in range(phi_count)
        ]

    north_side = t <= 1
    helper = (t == 1) | (t == theta_count - 2)
    half = channels * CAP // 2
    pair_rows = CAP // 2

    def rows_at(first):
        parts = [lax.dynamic_slice_in_dim(f, first, pair_rows, axis=1) for f in (density, velocity, bfield)]
        rows = jnp.concatenate(parts, axis=0)
        return jnp.swapaxes(rows, 0, 1).reshape(half, npc, nr)

    keep_first = jnp.where(at_north, 0, ct - pair_rows)
    hand_first = jnp.where(at_north, pair_rows, ct - CAP)
    pairs_out = [(0, 1), (theta_count - 1, theta_count - 2)]
    pairs_in = [(1, 0), (theta_count - 2, theta_count - 1)]
    handed = lax.ppermute(rows_at(hand_first), "theta", pairs_out)
    work = jnp.where(helper, handed, rows_at(keep_first))
    per_device = half // phi_count
    work, halo_src = lax.optimization_barrier((work, combined))
    cycle = lax.all_to_all(work, "phi", split_axis=0, concat_axis=1, tiled=True)
    low_halo = lax.ppermute(
        halo_src[:, ct - 1], "theta", [(i, i + 1) for i in range(theta_count - 1)]
    )
    up_send = jnp.concatenate([halo_src[:, 0], halo_src[6:7, 1]], axis=0)
    up_halo = lax.ppermute(up_send, "theta", [(i + 1, i) for i in range(theta_count - 1)])
    rows_ext = jnp.concatenate(
        [
            low_halo[:, None],
            combined,
            up_halo[:channels, None],
            jnp.broadcast_to(up_halo[channels:], (channels, npc, nr))[:, None],
        ],
        axis=1,
    )
    left_cols = lax.ppermute(
        rows_ext[:, :, npc - 1 :], "phi", [(i, (i + 1) % phi_count) for i in range(phi_count)]
    )
    right_cols = lax.ppermute(
        rows_ext[:, :, :2], "phi", [((i + 1) % phi_count, i) for i in range(phi_count)]
    )
    early = jnp.concatenate([left_cols, rows_ext, right_cols], axis=2)

    cycle, early = lax.optimization_barrier((cycle, early))
    analysis = fourier_rows(jnp.arange(cycle_len, dtype=jnp.int32), cycle_len)
    dst_cols = (
        jnp.arange(phi_count, dtype=jnp.int32)[:, None] * npc
        - 1
        + jnp.arange(npc + 3, dtype=jnp.int32)[None, :]
    ) % cycle_len
    synthesis = fourier_rows(dst_cols, cycle_len)

    pole_pick = jnp.where(north_side, 0, 1).astype(jnp.int32)
    level_row = lax.dynamic_index_in_dim(levels, pole_pick, 0, keepdims=False)
    slot_ids = p * per_device + jnp.arange(per_device, dtype=jnp.int32)
    row_base = jnp.where(north_side == helper, pair_rows, 0)
    row_ids = row_base + slot_ids // channels
    slot_levels = jnp.sum(
        jnp.where(
            row_ids[:, None] == jnp.arange(CAP, dtype=jnp.int32)[None, :], level_row[None, :], 0
        ),
        axis=1,
    )
    limits = jnp.right_shift(jnp.int32(KMAX), slot_levels)
    column_order = jnp.arange(2 * KMAX, dtype=jnp.int32) % KMAX
    column_weight = jnp.where(column_order == 0, 1.0 / cycle_len, 2.0 / cycle_len).astype(
        jnp.float32
    )
    kept_weight = jnp.where(column_order[None, :] < limits[:, None], column_weight[None, :], 0.0)
    coeffs = jnp.einsum("smr,mn->snr", cycle, analysis, precision=lax.Precision.HIGH)
    coeffs = coeffs * kept_weight[:, :, None]
    out = jnp.einsum("snr,kjn->ksjr", coeffs, synthesis, precision=lax.Precision.HIGH)
    out = out.reshape(phi_count * per_device, npc + 3, nr)
    mine = lax.all_to_all(out, "phi", split_axis=0, concat_axis=0, tiled=True)

    from_helper = lax.ppermute(mine, "theta", pairs_in)
    spare = mine[6 : 7]
    ghost_send = jnp.where(
        north_side,
        jnp.concatenate([mine[:channels], spare], axis=0),
        jnp.concatenate([mine[channels:], spare], axis=0),
    )
    turn = phi_count // 2
    ghost = lax.ppermute(
        ghost_send,
        both,
        [(a * phi_count + b, a * phi_count + (b + turn) % phi_count) for a in poles for b in range(phi_count)],
    )
    in_order = jnp.where(
        at_north,
        jnp.concatenate([mine, from_helper], axis=0),
        jnp.concatenate([from_helper, mine], axis=0),
    )
    cap_rows = jnp.swapaxes(in_order.reshape(CAP, channels, npc + 3, nr), 0, 1)
    cap_start = jnp.where(at_north, 1, ct - CAP + 1)
    kept_cap = lax.dynamic_slice_in_dim(early, cap_start, CAP, axis=1)
    cap_block = jnp.where(at_north | at_south, cap_rows, kept_cap)
    with_caps = lax.dynamic_update_slice_in_dim(early, cap_block, cap_start, axis=1)

    near_rows = 2
    rest_rows = ct - near_rows

    def rows_from(x, first, count):
        return advance(lax.dynamic_slice_in_dim(x, first, count + 3, axis=1))

    rest = rows_from(with_caps, jnp.where(at_north, near_rows, 0), rest_rows)
    ghost, rest = lax.optimization_barrier((ghost, rest))
    ghost_main = ghost[:channels]
    ghost_b = ghost[channels:]
    ghost_main = ghost_main * parity[:, None, None]
    ghost_b = ghost_b * parity[6]
    north_block = jnp.concatenate(
        [ghost_main[:, None], cap_rows, early[:, CAP + 1 : CAP + 2]], axis=1
    )
    south_block = jnp.concatenate(
        [
            cap_rows,
            ghost_main[:, None],
            jnp.broadcast_to(ghost_b, (channels, npc + 3, nr))[:, None],
        ],
        axis=1,
    )
    offset = jnp.where(at_north, 0, ct - CAP + 1)
    kept_block = lax.dynamic_slice_in_dim(early, offset, CAP + 2, axis=1)
    block = jnp.where(
        at_north, north_block, jnp.where(at_south, south_block, kept_block)
    )
    extended = lax.dynamic_update_slice_in_dim(early, block, offset, axis=1)
    near = rows_from(extended, jnp.where(at_north, 0, rest_rows), near_rows)
    outs = []
    for a, c in zip(rest, near):
        north_order = jnp.concatenate([c, a], axis=1)
        other_order = jnp.concatenate([a, c], axis=1)
        outs.append(jnp.where(at_north, north_order, other_order))
    return tuple(outs)


def solution(mesh):
    return jax.shard_map(
        local,
        mesh=mesh,
        in_specs=(
            P(None, "theta", "phi", None),
            P(None, "theta", "phi", None),
            P(None, "theta", "phi", None),
            P(),
        ),
        out_specs=(P(None, "theta", "phi", None), P(None, "theta", "phi", None)),
        check_vma=False,
    )
```

```python
import math

import jax
import jax.numpy as jnp
from jax import lax
from jax.sharding import PartitionSpec as P

CAP = 4
KMAX = 128


TIME_STEP = 0.2
PARITY = (1.0, 1.0, 1.0, -1.0, -1.0, 1.0, -1.0, -1.0)


def up_r(a):
    return jnp.concatenate([a[..., 1:], a[..., -1:]], axis=-1)


def down_r(a):
    return jnp.concatenate([a[..., :1], a[..., :-1]], axis=-1)


def face_flux(left_amount, right_amount, left_speed, right_speed):
    return 0.5 * (left_amount * left_speed + right_amount * right_speed) - 0.5 * jnp.maximum(
        jnp.abs(left_speed), jnp.abs(right_speed)
    ) * (right_amount - left_amount)


def corner4(e00, e01, e10, e11):
    return 0.25 * (((e00 + e01) + e10) + e11)


def advance(x):
    ct = x.shape[1] - 3
    npc = x.shape[2] - 3
    densities = []
    for channel in range(2):
        q = x[channel]
        v_t = x[3]
        v_p = x[4]
        v_r = x[2]
        fl_t = face_flux(
            q[0 : ct + 1, 1 : npc + 1], q[1 : ct + 2, 1 : npc + 1],
            v_t[0 : ct + 1, 1 : npc + 1], v_t[1 : ct + 2, 1 : npc + 1],
        )
        fl_p = face_flux(
            q[1 : ct + 1, 0 : npc + 1], q[1 : ct + 1, 1 : npc + 2],
            v_p[1 : ct + 1, 0 : npc + 1], v_p[1 : ct + 1, 1 : npc + 2],
        )
        qi = q[1 : ct + 1, 1 : npc + 1]
        vi = v_r[1 : ct + 1, 1 : npc + 1]
        fl_lo = face_flux(down_r(qi), qi, down_r(vi), vi)
        fl_hi = face_flux(qi, up_r(qi), vi, up_r(vi))
        tendency = (fl_t[1:] - fl_t[:-1]) + (fl_p[:, 1:] - fl_p[:, :-1]) + (fl_hi - fl_lo)
        densities.append(qi - TIME_STEP * tendency)

    wr = slice(0, ct + 2)
    wc = slice(0, npc + 2)
    b_r = x[5][wr, wc]
    b_t = x[6]
    b_p = x[7]
    c_r = 0.5 * (b_r + up_r(b_r))
    c_t = 0.5 * (b_t[0 : ct + 2, wc] + b_t[1 : ct + 3, wc])
    c_p = 0.5 * (b_p[wr, 0 : npc + 2] + b_p[wr, 1 : npc + 3])
    s_r = x[2][wr, wc]
    s_t = x[3][wr, wc]
    s_p = x[4][wr, wc]
    emf_r = -(s_t * c_p - s_p * c_t)
    emf_t = -(s_p * c_r - s_r * c_p)
    emf_p = -(s_r * c_t - s_t * c_r)
    lane = lax.broadcasted_iota(jnp.int32, emf_t.shape, 2)
    last = emf_t.shape[2] - 1
    edge_t = -(s_p * b_r - s_r * c_p)
    edge_p = -(s_r * c_t - s_t * b_r)
    t_lo = jnp.where(lane == 0, edge_t, down_r(emf_t))
    t_hi = jnp.where(lane == last, edge_t, up_r(emf_t))
    p_lo = jnp.where(lane == 0, edge_p, down_r(emf_p))
    p_hi = jnp.where(lane == last, edge_p, up_r(emf_p))

    rows_a = slice(0, ct + 1)
    rows_b = slice(1, ct + 2)
    cols_in = slice(1, npc + 1)
    ep_lo = corner4(p_lo[rows_a, cols_in], emf_p[rows_a, cols_in], p_lo[rows_b, cols_in], emf_p[rows_b, cols_in])
    ep_hi = corner4(emf_p[rows_a, cols_in], p_hi[rows_a, cols_in], emf_p[rows_b, cols_in], p_hi[rows_b, cols_in])
    rows_in = slice(1, ct + 1)
    cols_a = slice(0, npc + 1)
    cols_b = slice(1, npc + 2)
    et_lo = corner4(t_lo[rows_in, cols_a], emf_t[rows_in, cols_a], t_lo[rows_in, cols_b], emf_t[rows_in, cols_b])
    et_hi = corner4(emf_t[rows_in, cols_a], t_hi[rows_in, cols_a], emf_t[rows_in, cols_b], t_hi[rows_in, cols_b])
    er = corner4(emf_r[rows_a, cols_a], emf_r[rows_a, cols_b], emf_r[rows_b, cols_a], emf_r[rows_b, cols_b])

    inner = (slice(1, ct + 1), slice(1, npc + 1))
    new_radial = x[5][inner] - TIME_STEP * (
        (ep_lo[1:] - ep_lo[:-1]) - (et_lo[:, 1:] - et_lo[:, :-1])
    )
    new_theta = x[6][inner] - TIME_STEP * (
        (er[:-1, 1:] - er[:-1, :-1]) - (ep_hi[:-1] - ep_lo[:-1])
    )
    new_phi = x[7][inner] - TIME_STEP * (
        (et_hi[:, :-1] - et_lo[:, :-1]) - (er[1:, :-1] - er[:-1, :-1])
    )
    return jnp.stack(densities), jnp.stack([new_radial, new_theta, new_phi])


def fourier_rows(cols, cycle_len):
    orders = jnp.arange(KMAX, dtype=jnp.int32)
    phase = (cols[..., None] * orders) % cycle_len
    angle = phase.astype(jnp.float32) * (2.0 * math.pi / cycle_len)
    return jnp.concatenate([jnp.cos(angle), jnp.sin(angle)], axis=-1)


def local(density, velocity, bfield, levels):
    combined = jnp.concatenate([density, velocity, bfield], axis=0)
    channels, ct, npc, nr = combined.shape
    theta_count = lax.axis_size("theta")
    phi_count = lax.axis_size("phi")
    t = lax.axis_index("theta")
    p = lax.axis_index("phi")
    at_north = t == 0
    at_south = t == theta_count - 1
    cycle_len = npc * phi_count
    parity = jnp.array(PARITY, jnp.float32)
    poles = (0, theta_count - 1)
    both = ("theta", "phi")

    def pole_pairs(shift):
        return [
            (a * phi_count + b, a * phi_count + (b + shift) % phi_count)
            for a in poles
            for b in range(phi_count)
        ]

    north_side = t <= 1
    helper = (t == 1) | (t == theta_count - 2)
    half = channels * CAP // 2
    pair_rows = CAP // 2

    def rows_at(first):
        parts = [lax.dynamic_slice_in_dim(f, first, pair_rows, axis=1) for f in (density, velocity, bfield)]
        rows = jnp.concatenate(parts, axis=0)
        return jnp.swapaxes(rows, 0, 1).reshape(half, npc, nr)

    keep_first = jnp.where(at_north, 0, ct - pair_rows)
    hand_first = jnp.where(at_north, pair_rows, ct - CAP)
    pairs_out = [(0, 1), (theta_count - 1, theta_count - 2)]
    pairs_in = [(1, 0), (theta_count - 2, theta_count - 1)]
    handed = lax.ppermute(rows_at(hand_first), "theta", pairs_out)
    work = jnp.where(helper, handed, rows_at(keep_first))
    per_device = half // phi_count
    low_send = jnp.concatenate([f[:, ct - 1] for f in (density, velocity, bfield)], axis=0)
    up_send = jnp.concatenate([f[:, 0] for f in (density, velocity, bfield)] + [bfield[1:2, 1]], axis=0)
    work, low_send, up_send = lax.optimization_barrier((work, low_send, up_send))
    cycle = lax.all_to_all(work, "phi", split_axis=0, concat_axis=1, tiled=True)
    low_halo = lax.ppermute(low_send, "theta", [(i, i + 1) for i in range(theta_count - 1)])
    up_halo = lax.ppermute(up_send, "theta", [(i + 1, i) for i in range(theta_count - 1)])
    rows_ext = jnp.concatenate(
        [
            low_halo[:, None],
            combined,
            up_halo[:channels, None],
            jnp.broadcast_to(up_halo[channels:], (channels, npc, nr))[:, None],
        ],
        axis=1,
    )
    left_cols = lax.ppermute(
        rows_ext[:, :, npc - 1 :], "phi", [(i, (i + 1) % phi_count) for i in range(phi_count)]
    )
    right_cols = lax.ppermute(
        rows_ext[:, :, :2], "phi", [((i + 1) % phi_count, i) for i in range(phi_count)]
    )
    early = jnp.concatenate([left_cols, rows_ext, right_cols], axis=2)

    cycle, early = lax.optimization_barrier((cycle, early))
    analysis = fourier_rows(jnp.arange(cycle_len, dtype=jnp.int32), cycle_len)
    dst_cols = (
        jnp.arange(phi_count, dtype=jnp.int32)[:, None] * npc
        - 1
        + jnp.arange(npc + 3, dtype=jnp.int32)[None, :]
    ) % cycle_len
    synthesis = fourier_rows(dst_cols, cycle_len)

    pole_pick = jnp.where(north_side, 0, 1).astype(jnp.int32)
    level_row = lax.dynamic_index_in_dim(levels, pole_pick, 0, keepdims=False)
    slot_ids = p * per_device + jnp.arange(per_device, dtype=jnp.int32)
    row_base = jnp.where(north_side == helper, pair_rows, 0)
    row_ids = row_base + slot_ids // channels
    slot_levels = jnp.sum(
        jnp.where(
            row_ids[:, None] == jnp.arange(CAP, dtype=jnp.int32)[None, :], level_row[None, :], 0
        ),
        axis=1,
    )
    limits = jnp.right_shift(jnp.int32(KMAX), slot_levels)
    column_order = jnp.arange(2 * KMAX, dtype=jnp.int32) % KMAX
    column_weight = jnp.where(column_order == 0, 1.0 / cycle_len, 2.0 / cycle_len).astype(
        jnp.float32
    )
    kept_weight = jnp.where(column_order[None, :] < limits[:, None], column_weight[None, :], 0.0)
    coeffs = jnp.einsum("smr,mn->snr", cycle, analysis, precision=lax.Precision.HIGH)
    coeffs = coeffs * kept_weight[:, :, None]
    out = jnp.einsum("snr,kjn->ksjr", coeffs, synthesis, precision=lax.Precision.HIGH)
    out = out.reshape(phi_count * per_device, npc + 3, nr)
    mine = lax.all_to_all(out, "phi", split_axis=0, concat_axis=0, tiled=True)

    from_helper = lax.ppermute(mine, "theta", pairs_in)
    spare = mine[6 : 7]
    ghost_send = jnp.where(
        north_side,
        jnp.concatenate([mine[:channels], spare], axis=0),
        jnp.concatenate([mine[channels:], spare], axis=0),
    )
    turn = phi_count // 2
    ghost = lax.ppermute(
        ghost_send,
        both,
        [(a * phi_count + b, a * phi_count + (b + turn) % phi_count) for a in poles for b in range(phi_count)],
    )
    in_order = jnp.where(
        at_north,
        jnp.concatenate([mine, from_helper], axis=0),
        jnp.concatenate([from_helper, mine], axis=0),
    )
    cap_rows = jnp.swapaxes(in_order.reshape(CAP, channels, npc + 3, nr), 0, 1)
    ghost_main = ghost[:channels]
    ghost_b = ghost[channels:]
    ghost_main = ghost_main * parity[:, None, None]
    ghost_b = ghost_b * parity[6]
    north_block = jnp.concatenate(
        [ghost_main[:, None], cap_rows, early[:, CAP + 1 : CAP + 2]], axis=1
    )
    south_block = jnp.concatenate(
        [
            cap_rows,
            ghost_main[:, None],
            jnp.broadcast_to(ghost_b, (channels, npc + 3, nr))[:, None],
        ],
        axis=1,
    )
    offset = jnp.where(at_north, 0, ct - CAP + 1)
    kept_block = lax.dynamic_slice_in_dim(early, offset, CAP + 2, axis=1)
    block = jnp.where(
        at_north, north_block, jnp.where(at_south, south_block, kept_block)
    )
    extended = lax.dynamic_update_slice_in_dim(early, block, offset, axis=1)
    return advance(extended)


def solution(mesh):
    return jax.shard_map(
        local,
        mesh=mesh,
        in_specs=(
            P(None, "theta", "phi", None),
            P(None, "theta", "phi", None),
            P(None, "theta", "phi", None),
            P(),
        ),
        out_specs=(P(None, "theta", "phi", None), P(None, "theta", "phi", None)),
        check_vma=False,
    )
```

```python
import math

import jax
import jax.numpy as jnp
from jax import lax
from jax.sharding import PartitionSpec as P

CAP = 4
KMAX = 128


TIME_STEP = 0.2
PARITY = (1.0, 1.0, 1.0, -1.0, -1.0, 1.0, -1.0, -1.0)


def up_r(a):
    return jnp.concatenate([a[..., 1:], a[..., -1:]], axis=-1)


def down_r(a):
    return jnp.concatenate([a[..., :1], a[..., :-1]], axis=-1)


def face_flux(left_amount, right_amount, left_speed, right_speed):
    return 0.5 * (left_amount * left_speed + right_amount * right_speed) - 0.5 * jnp.maximum(
        jnp.abs(left_speed), jnp.abs(right_speed)
    ) * (right_amount - left_amount)


def corner4(e00, e01, e10, e11):
    return 0.25 * (((e00 + e01) + e10) + e11)


def advance(x):
    ct = x.shape[1] - 3
    npc = x.shape[2] - 3
    densities = []
    for channel in range(2):
        q = x[channel]
        v_t = x[3]
        v_p = x[4]
        v_r = x[2]
        fl_t = face_flux(
            q[0 : ct + 1, 1 : npc + 1], q[1 : ct + 2, 1 : npc + 1],
            v_t[0 : ct + 1, 1 : npc + 1], v_t[1 : ct + 2, 1 : npc + 1],
        )
        fl_p = face_flux(
            q[1 : ct + 1, 0 : npc + 1], q[1 : ct + 1, 1 : npc + 2],
            v_p[1 : ct + 1, 0 : npc + 1], v_p[1 : ct + 1, 1 : npc + 2],
        )
        qi = q[1 : ct + 1, 1 : npc + 1]
        vi = v_r[1 : ct + 1, 1 : npc + 1]
        fl_lo = face_flux(down_r(qi), qi, down_r(vi), vi)
        fl_hi = face_flux(qi, up_r(qi), vi, up_r(vi))
        tendency = (fl_t[1:] - fl_t[:-1]) + (fl_p[:, 1:] - fl_p[:, :-1]) + (fl_hi - fl_lo)
        densities.append(qi - TIME_STEP * tendency)

    wr = slice(0, ct + 2)
    wc = slice(0, npc + 2)
    b_r = x[5][wr, wc]
    b_t = x[6]
    b_p = x[7]
    c_r = 0.5 * (b_r + up_r(b_r))
    c_t = 0.5 * (b_t[0 : ct + 2, wc] + b_t[1 : ct + 3, wc])
    c_p = 0.5 * (b_p[wr, 0 : npc + 2] + b_p[wr, 1 : npc + 3])
    s_r = x[2][wr, wc]
    s_t = x[3][wr, wc]
    s_p = x[4][wr, wc]
    emf_r = -(s_t * c_p - s_p * c_t)
    emf_t = -(s_p * c_r - s_r * c_p)
    emf_p = -(s_r * c_t - s_t * c_r)
    lane = lax.broadcasted_iota(jnp.int32, emf_t.shape, 2)
    last = emf_t.shape[2] - 1
    edge_t = -(s_p * b_r - s_r * c_p)
    edge_p = -(s_r * c_t - s_t * b_r)
    t_lo = jnp.where(lane == 0, edge_t, down_r(emf_t))
    t_hi = jnp.where(lane == last, edge_t, up_r(emf_t))
    p_lo = jnp.where(lane == 0, edge_p, down_r(emf_p))
    p_hi = jnp.where(lane == last, edge_p, up_r(emf_p))

    rows_a = slice(0, ct + 1)
    rows_b = slice(1, ct + 2)
    cols_in = slice(1, npc + 1)
    ep_lo = corner4(p_lo[rows_a, cols_in], emf_p[rows_a, cols_in], p_lo[rows_b, cols_in], emf_p[rows_b, cols_in])
    ep_hi = corner4(emf_p[rows_a, cols_in], p_hi[rows_a, cols_in], emf_p[rows_b, cols_in], p_hi[rows_b, cols_in])
    rows_in = slice(1, ct + 1)
    cols_a = slice(0, npc + 1)
    cols_b = slice(1, npc + 2)
    et_lo = corner4(t_lo[rows_in, cols_a], emf_t[rows_in, cols_a], t_lo[rows_in, cols_b], emf_t[rows_in, cols_b])
    et_hi = corner4(emf_t[rows_in, cols_a], t_hi[rows_in, cols_a], emf_t[rows_in, cols_b], t_hi[rows_in, cols_b])
    er = corner4(emf_r[rows_a, cols_a], emf_r[rows_a, cols_b], emf_r[rows_b, cols_a], emf_r[rows_b, cols_b])

    inner = (slice(1, ct + 1), slice(1, npc + 1))
    new_radial = x[5][inner] - TIME_STEP * (
        (ep_lo[1:] - ep_lo[:-1]) - (et_lo[:, 1:] - et_lo[:, :-1])
    )
    new_theta = x[6][inner] - TIME_STEP * (
        (er[:-1, 1:] - er[:-1, :-1]) - (ep_hi[:-1] - ep_lo[:-1])
    )
    new_phi = x[7][inner] - TIME_STEP * (
        (et_hi[:, :-1] - et_lo[:, :-1]) - (er[1:, :-1] - er[:-1, :-1])
    )
    return jnp.stack(densities), jnp.stack([new_radial, new_theta, new_phi])


def fourier_rows(cols, cycle_len):
    orders = jnp.arange(KMAX, dtype=jnp.int32)
    phase = (cols[..., None] * orders) % cycle_len
    angle = phase.astype(jnp.float32) * (2.0 * math.pi / cycle_len)
    return jnp.concatenate([jnp.cos(angle), jnp.sin(angle)], axis=-1)


def local(density, velocity, bfield, levels):
    combined = jnp.concatenate([density, velocity, bfield], axis=0)
    channels, ct, npc, nr = combined.shape
    theta_count = lax.axis_size("theta")
    phi_count = lax.axis_size("phi")
    t = lax.axis_index("theta")
    p = lax.axis_index("phi")
    at_north = t == 0
    at_south = t == theta_count - 1
    cycle_len = npc * phi_count
    parity = jnp.array(PARITY, jnp.float32)
    poles = (0, theta_count - 1)
    both = ("theta", "phi")

    def pole_pairs(shift):
        return [
            (a * phi_count + b, a * phi_count + (b + shift) % phi_count)
            for a in poles
            for b in range(phi_count)
        ]

    north_side = t <= 1
    helper = (t == 1) | (t == theta_count - 2)
    half = channels * CAP // 2
    pair_rows = CAP // 2

    def rows_at(first):
        parts = [lax.dynamic_slice_in_dim(f, first, pair_rows, axis=1) for f in (density, velocity, bfield)]
        rows = jnp.concatenate(parts, axis=0)
        return jnp.swapaxes(rows, 0, 1).reshape(half, npc, nr)

    keep_first = jnp.where(at_north, 0, ct - pair_rows)
    hand_first = jnp.where(at_north, pair_rows, ct - CAP)
    pairs_out = [(0, 1), (theta_count - 1, theta_count - 2)]
    pairs_in = [(1, 0), (theta_count - 2, theta_count - 1)]
    handed = lax.ppermute(rows_at(hand_first), "theta", pairs_out)
    work = jnp.where(helper, handed, rows_at(keep_first))
    per_device = half // phi_count
    work, halo_src = lax.optimization_barrier((work, combined))
    cycle = lax.all_to_all(work, "phi", split_axis=0, concat_axis=1, tiled=True)
    low_halo = lax.ppermute(
        halo_src[:, ct - 1], "theta", [(i, i + 1) for i in range(theta_count - 1)]
    )
    up_send = jnp.concatenate([halo_src[:, 0], halo_src[6:7, 1]], axis=0)
    up_halo = lax.ppermute(up_send, "theta", [(i + 1, i) for i in range(theta_count - 1)])
    rows_ext = jnp.concatenate(
        [
            low_halo[:, None],
            combined,
            up_halo[:channels, None],
            jnp.broadcast_to(up_halo[channels:], (channels, npc, nr))[:, None],
        ],
        axis=1,
    )
    left_cols = lax.ppermute(
        rows_ext[:, :, npc - 1 :], "phi", [(i, (i + 1) % phi_count) for i in range(phi_count)]
    )
    right_cols = lax.ppermute(
        rows_ext[:, :, :2], "phi", [((i + 1) % phi_count, i) for i in range(phi_count)]
    )
    early = jnp.concatenate([left_cols, rows_ext, right_cols], axis=2)

    cycle, early = lax.optimization_barrier((cycle, early))
    analysis = fourier_rows(jnp.arange(cycle_len, dtype=jnp.int32), cycle_len)
    dst_cols = (
        jnp.arange(phi_count, dtype=jnp.int32)[:, None] * npc
        - 1
        + jnp.arange(npc + 3, dtype=jnp.int32)[None, :]
    ) % cycle_len
    synthesis = jnp.take(analysis, dst_cols.reshape(-1), axis=0).reshape(phi_count, npc + 3, 2 * KMAX)

    pole_pick = jnp.where(north_side, 0, 1).astype(jnp.int32)
    level_row = lax.dynamic_index_in_dim(levels, pole_pick, 0, keepdims=False)
    slot_ids = p * per_device + jnp.arange(per_device, dtype=jnp.int32)
    row_base = jnp.where(north_side == helper, pair_rows, 0)
    row_ids = row_base + slot_ids // channels
    slot_levels = jnp.sum(
        jnp.where(
            row_ids[:, None] == jnp.arange(CAP, dtype=jnp.int32)[None, :], level_row[None, :], 0
        ),
        axis=1,
    )
    limits = jnp.right_shift(jnp.int32(KMAX), slot_levels)
    column_order = jnp.arange(2 * KMAX, dtype=jnp.int32) % KMAX
    column_weight = jnp.where(column_order == 0, 1.0 / cycle_len, 2.0 / cycle_len).astype(
        jnp.float32
    )
    kept_weight = jnp.where(column_order[None, :] < limits[:, None], column_weight[None, :], 0.0)
    coeffs = jnp.einsum("smr,mn->snr", cycle, analysis, precision=lax.Precision.HIGH)
    coeffs = coeffs * kept_weight[:, :, None]
    out = jnp.einsum("snr,kjn->ksjr", coeffs, synthesis, precision=lax.Precision.HIGH)
    out = out.reshape(phi_count * per_device, npc + 3, nr)
    mine = lax.all_to_all(out, "phi", split_axis=0, concat_axis=0, tiled=True)

    from_helper = lax.ppermute(mine, "theta", pairs_in)
    spare = mine[6 : 7]
    ghost_send = jnp.where(
        north_side,
        jnp.concatenate([mine[:channels], spare], axis=0),
        jnp.concatenate([mine[channels:], spare], axis=0),
    )
    turn = phi_count // 2
    ghost = lax.ppermute(
        ghost_send,
        both,
        [(a * phi_count + b, a * phi_count + (b + turn) % phi_count) for a in poles for b in range(phi_count)],
    )
    in_order = jnp.where(
        at_north,
        jnp.concatenate([mine, from_helper], axis=0),
        jnp.concatenate([from_helper, mine], axis=0),
    )
    cap_rows = jnp.swapaxes(in_order.reshape(CAP, channels, npc + 3, nr), 0, 1)
    ghost_main = ghost[:channels]
    ghost_b = ghost[channels:]
    ghost_main = ghost_main * parity[:, None, None]
    ghost_b = ghost_b * parity[6]
    north_block = jnp.concatenate(
        [ghost_main[:, None], cap_rows, early[:, CAP + 1 : CAP + 2]], axis=1
    )
    south_block = jnp.concatenate(
        [
            cap_rows,
            ghost_main[:, None],
            jnp.broadcast_to(ghost_b, (channels, npc + 3, nr))[:, None],
        ],
        axis=1,
    )
    offset = jnp.where(at_north, 0, ct - CAP + 1)
    kept_block = lax.dynamic_slice_in_dim(early, offset, CAP + 2, axis=1)
    block = jnp.where(
        at_north, north_block, jnp.where(at_south, south_block, kept_block)
    )
    extended = lax.dynamic_update_slice_in_dim(early, block, offset, axis=1)
    return advance(extended)


def solution(mesh):
    return jax.shard_map(
        local,
        mesh=mesh,
        in_specs=(
            P(None, "theta", "phi", None),
            P(None, "theta", "phi", None),
            P(None, "theta", "phi", None),
            P(),
        ),
        out_specs=(P(None, "theta", "phi", None), P(None, "theta", "phi", None)),
        check_vma=False,
    )
```

```python
import math

import jax
import jax.numpy as jnp
from jax import lax
from jax.sharding import PartitionSpec as P

CAP = 4
KMAX = 128


TIME_STEP = 0.2
PARITY = (1.0, 1.0, 1.0, -1.0, -1.0, 1.0, -1.0, -1.0)


def up_r(a):
    return jnp.concatenate([a[..., 1:], a[..., -1:]], axis=-1)


def down_r(a):
    return jnp.concatenate([a[..., :1], a[..., :-1]], axis=-1)


def face_flux(left_amount, right_amount, left_speed, right_speed):
    return 0.5 * (left_amount * left_speed + right_amount * right_speed) - 0.5 * jnp.maximum(
        jnp.abs(left_speed), jnp.abs(right_speed)
    ) * (right_amount - left_amount)


def corner4(e00, e01, e10, e11):
    return 0.25 * (((e00 + e01) + e10) + e11)


def advance(x):
    ct = x.shape[1] - 3
    npc = x.shape[2] - 3
    densities = []
    for channel in range(2):
        q = x[channel]
        v_t = x[3]
        v_p = x[4]
        v_r = x[2]
        fl_t = face_flux(
            q[0 : ct + 1, 1 : npc + 1], q[1 : ct + 2, 1 : npc + 1],
            v_t[0 : ct + 1, 1 : npc + 1], v_t[1 : ct + 2, 1 : npc + 1],
        )
        fl_p = face_flux(
            q[1 : ct + 1, 0 : npc + 1], q[1 : ct + 1, 1 : npc + 2],
            v_p[1 : ct + 1, 0 : npc + 1], v_p[1 : ct + 1, 1 : npc + 2],
        )
        qi = q[1 : ct + 1, 1 : npc + 1]
        vi = v_r[1 : ct + 1, 1 : npc + 1]
        fl_lo = face_flux(down_r(qi), qi, down_r(vi), vi)
        fl_hi = face_flux(qi, up_r(qi), vi, up_r(vi))
        tendency = (fl_t[1:] - fl_t[:-1]) + (fl_p[:, 1:] - fl_p[:, :-1]) + (fl_hi - fl_lo)
        densities.append(qi - TIME_STEP * tendency)

    wr = slice(0, ct + 2)
    wc = slice(0, npc + 2)
    b_r = x[5][wr, wc]
    b_t = x[6]
    b_p = x[7]
    c_r = 0.5 * (b_r + up_r(b_r))
    c_t = 0.5 * (b_t[0 : ct + 2, wc] + b_t[1 : ct + 3, wc])
    c_p = 0.5 * (b_p[wr, 0 : npc + 2] + b_p[wr, 1 : npc + 3])
    s_r = x[2][wr, wc]
    s_t = x[3][wr, wc]
    s_p = x[4][wr, wc]
    emf_r = -(s_t * c_p - s_p * c_t)
    emf_t = -(s_p * c_r - s_r * c_p)
    emf_p = -(s_r * c_t - s_t * c_r)
    lane = lax.broadcasted_iota(jnp.int32, emf_t.shape, 2)
    last = emf_t.shape[2] - 1
    edge_t = -(s_p * b_r - s_r * c_p)
    edge_p = -(s_r * c_t - s_t * b_r)
    t_lo = jnp.where(lane == 0, edge_t, down_r(emf_t))
    t_hi = jnp.where(lane == last, edge_t, up_r(emf_t))
    p_lo = jnp.where(lane == 0, edge_p, down_r(emf_p))
    p_hi = jnp.where(lane == last, edge_p, up_r(emf_p))

    rows_a = slice(0, ct + 1)
    rows_b = slice(1, ct + 2)
    cols_in = slice(1, npc + 1)
    ep_lo = corner4(p_lo[rows_a, cols_in], emf_p[rows_a, cols_in], p_lo[rows_b, cols_in], emf_p[rows_b, cols_in])
    ep_hi = corner4(emf_p[rows_a, cols_in], p_hi[rows_a, cols_in], emf_p[rows_b, cols_in], p_hi[rows_b, cols_in])
    rows_in = slice(1, ct + 1)
    cols_a = slice(0, npc + 1)
    cols_b = slice(1, npc + 2)
    et_lo = corner4(t_lo[rows_in, cols_a], emf_t[rows_in, cols_a], t_lo[rows_in, cols_b], emf_t[rows_in, cols_b])
    et_hi = corner4(emf_t[rows_in, cols_a], t_hi[rows_in, cols_a], emf_t[rows_in, cols_b], t_hi[rows_in, cols_b])
    er = corner4(emf_r[rows_a, cols_a], emf_r[rows_a, cols_b], emf_r[rows_b, cols_a], emf_r[rows_b, cols_b])

    inner = (slice(1, ct + 1), slice(1, npc + 1))
    new_radial = x[5][inner] - TIME_STEP * (
        (ep_lo[1:] - ep_lo[:-1]) - (et_lo[:, 1:] - et_lo[:, :-1])
    )
    new_theta = x[6][inner] - TIME_STEP * (
        (er[:-1, 1:] - er[:-1, :-1]) - (ep_hi[:-1] - ep_lo[:-1])
    )
    new_phi = x[7][inner] - TIME_STEP * (
        (et_hi[:, :-1] - et_lo[:, :-1]) - (er[1:, :-1] - er[:-1, :-1])
    )
    return jnp.stack(densities), jnp.stack([new_radial, new_theta, new_phi])


def fourier_rows(cols, cycle_len):
    orders = jnp.arange(KMAX, dtype=jnp.int32)
    phase = (cols[..., None] * orders) % cycle_len
    angle = phase.astype(jnp.float32) * (2.0 * math.pi / cycle_len)
    return jnp.concatenate([jnp.cos(angle), jnp.sin(angle)], axis=-1)


def local(density, velocity, bfield, levels):
    combined = jnp.concatenate([density, velocity, bfield], axis=0)
    channels, ct, npc, nr = combined.shape
    theta_count = lax.axis_size("theta")
    phi_count = lax.axis_size("phi")
    t = lax.axis_index("theta")
    p = lax.axis_index("phi")
    at_north = t == 0
    at_south = t == theta_count - 1
    cycle_len = npc * phi_count
    parity = jnp.array(PARITY, jnp.float32)
    poles = (0, theta_count - 1)
    both = ("theta", "phi")

    def pole_pairs(shift):
        return [
            (a * phi_count + b, a * phi_count + (b + shift) % phi_count)
            for a in poles
            for b in range(phi_count)
        ]

    north_side = t <= 1
    helper = (t == 1) | (t == theta_count - 2)
    half = channels * CAP // 2
    pair_rows = CAP // 2

    def rows_at(first):
        parts = [lax.dynamic_slice_in_dim(f, first, pair_rows, axis=1) for f in (density, velocity, bfield)]
        rows = jnp.concatenate(parts, axis=0)
        return jnp.swapaxes(rows, 0, 1).reshape(half, npc, nr)

    keep_first = jnp.where(at_north, 0, ct - pair_rows)
    hand_first = jnp.where(at_north, pair_rows, ct - CAP)
    pairs_out = [(0, 1), (theta_count - 1, theta_count - 2)]
    pairs_in = [(1, 0), (theta_count - 2, theta_count - 1)]
    handed = lax.ppermute(rows_at(hand_first), "theta", pairs_out)
    work = jnp.where(helper, handed, rows_at(keep_first))
    per_device = half // phi_count
    work, halo_src = lax.optimization_barrier((work, combined))
    cycle = lax.all_to_all(work, "phi", split_axis=0, concat_axis=1, tiled=True)
    low_halo = lax.ppermute(
        halo_src[:, ct - 1], "theta", [(i, i + 1) for i in range(theta_count - 1)]
    )
    up_send = jnp.concatenate([halo_src[:, 0], halo_src[6:7, 1]], axis=0)
    up_halo = lax.ppermute(up_send, "theta", [(i + 1, i) for i in range(theta_count - 1)])
    rows_ext = jnp.concatenate(
        [
            low_halo[:, None],
            combined,
            up_halo[:channels, None],
            jnp.broadcast_to(up_halo[channels:], (channels, npc, nr))[:, None],
        ],
        axis=1,
    )
    left_cols = lax.ppermute(
        rows_ext[:, :, npc - 1 :], "phi", [(i, (i + 1) % phi_count) for i in range(phi_count)]
    )
    right_cols = lax.ppermute(
        rows_ext[:, :, :2], "phi", [((i + 1) % phi_count, i) for i in range(phi_count)]
    )
    early = jnp.concatenate([left_cols, rows_ext, right_cols], axis=2)

    cycle, early = lax.optimization_barrier((cycle, early))
    orders = jnp.arange(KMAX, dtype=jnp.int32)
    scale = 2.0 * math.pi / cycle_len
    block_phase = ((jnp.arange(phi_count, dtype=jnp.int32) * npc)[:, None] * orders) % cycle_len
    ca = jnp.cos(block_phase.astype(jnp.float32) * scale)[:, None]
    sa = jnp.sin(block_phase.astype(jnp.float32) * scale)[:, None]

    def fourier_blocks(first, count):
        inner = ((jnp.arange(count, dtype=jnp.int32) + first)[:, None] * orders) % cycle_len
        cb = jnp.cos(inner.astype(jnp.float32) * scale)[None]
        sb = jnp.sin(inner.astype(jnp.float32) * scale)[None]
        return jnp.concatenate([ca * cb - sa * sb, sa * cb + ca * sb], axis=-1)

    analysis = fourier_blocks(0, npc).reshape(cycle_len, 2 * KMAX)
    synthesis = fourier_blocks(-1, npc + 3)

    pole_pick = jnp.where(north_side, 0, 1).astype(jnp.int32)
    level_row = lax.dynamic_index_in_dim(levels, pole_pick, 0, keepdims=False)
    slot_ids = p * per_device + jnp.arange(per_device, dtype=jnp.int32)
    row_base = jnp.where(north_side == helper, pair_rows, 0)
    row_ids = row_base + slot_ids // channels
    slot_levels = jnp.sum(
        jnp.where(
            row_ids[:, None] == jnp.arange(CAP, dtype=jnp.int32)[None, :], level_row[None, :], 0
        ),
        axis=1,
    )
    limits = jnp.right_shift(jnp.int32(KMAX), slot_levels)
    column_order = jnp.arange(2 * KMAX, dtype=jnp.int32) % KMAX
    column_weight = jnp.where(column_order == 0, 1.0 / cycle_len, 2.0 / cycle_len).astype(
        jnp.float32
    )
    kept_weight = jnp.where(column_order[None, :] < limits[:, None], column_weight[None, :], 0.0)
    coeffs = jnp.einsum("smr,mn->snr", cycle, analysis, precision=lax.Precision.HIGH)
    coeffs = coeffs * kept_weight[:, :, None]
    out = jnp.einsum("snr,kjn->ksjr", coeffs, synthesis, precision=lax.Precision.HIGH)
    out = out.reshape(phi_count * per_device, npc + 3, nr)
    mine = lax.all_to_all(out, "phi", split_axis=0, concat_axis=0, tiled=True)

    from_helper = lax.ppermute(mine, "theta", pairs_in)
    spare = mine[6 : 7]
    ghost_send = jnp.where(
        north_side,
        jnp.concatenate([mine[:channels], spare], axis=0),
        jnp.concatenate([mine[channels:], spare], axis=0),
    )
    turn = phi_count // 2
    ghost = lax.ppermute(
        ghost_send,
        both,
        [(a * phi_count + b, a * phi_count + (b + turn) % phi_count) for a in poles for b in range(phi_count)],
    )
    in_order = jnp.where(
        at_north,
        jnp.concatenate([mine, from_helper], axis=0),
        jnp.concatenate([from_helper, mine], axis=0),
    )
    cap_rows = jnp.swapaxes(in_order.reshape(CAP, channels, npc + 3, nr), 0, 1)
    ghost_main = ghost[:channels]
    ghost_b = ghost[channels:]
    ghost_main = ghost_main * parity[:, None, None]
    ghost_b = ghost_b * parity[6]
    north_block = jnp.concatenate(
        [ghost_main[:, None], cap_rows, early[:, CAP + 1 : CAP + 2]], axis=1
    )
    south_block = jnp.concatenate(
        [
            cap_rows,
            ghost_main[:, None],
            jnp.broadcast_to(ghost_b, (channels, npc + 3, nr))[:, None],
        ],
        axis=1,
    )
    offset = jnp.where(at_north, 0, ct - CAP + 1)
    kept_block = lax.dynamic_slice_in_dim(early, offset, CAP + 2, axis=1)
    block = jnp.where(
        at_north, north_block, jnp.where(at_south, south_block, kept_block)
    )
    extended = lax.dynamic_update_slice_in_dim(early, block, offset, axis=1)
    return advance(extended)


def solution(mesh):
    return jax.shard_map(
        local,
        mesh=mesh,
        in_specs=(
            P(None, "theta", "phi", None),
            P(None, "theta", "phi", None),
            P(None, "theta", "phi", None),
            P(),
        ),
        out_specs=(P(None, "theta", "phi", None), P(None, "theta", "phi", None)),
        check_vma=False,
    )
```
